32 devices in a mesh: blk: 2 (over x), gy: 4 (over y, core), gz: 4 (over z).
Axes of the slice: x: 2, y: 2, z: 4, core: 2. Of those that a mesh axis runs over, the one named last changes fastest.
Arguments:
- vacancy: float32 [64, 64, 1024], P('blk', 'gy', 'gz'), may hold values from -6 to 6
- grain_label: int32 [64, 64, 1024], P('blk', 'gy', 'gz'), may hold values from 0 to 7
- pore_mask: int32 [64, 64, 1024], P('blk', 'gy', 'gz'), may hold values 0 or 1
- cotangent: float32 [64, 64, 1024], P('blk', 'gy', 'gz'), may hold values from -6 to 6
Outputs:
- final_field: float32 [64, 64, 1024], P('blk', 'gy', 'gz')
- gradient: float32 [64, 64, 1024], P('blk', 'gy', 'gz')
The draws below stay inside these ranges and needn't reach their ends.
All inputs are finite; a program needn't handle non-finite values. No bound on the sum of `pore_mask` on one device may be relied on, other than what follows from the above.
Results may differ from the reference program's by a relative error of at most 0.00017.
Values sent between devices are 32-bit elements; how exact they have to be, the bound alone decides.
No kernel may reach another device: no remote copies, remote signals or barrier semaphores. Data moves between devices by JAX's collectives and lax.ppermute only.
A program may use at most 128 MiB of HBM per device.

```python
import jax
import jax.numpy as jnp
from jax import lax

NX = 64
NY = 64
NZ = 1024
DT_X = 64


def plant(values, own_key, least, high):
    longest = values.shape.index(max(values.shape))
    spots = []
    for shift in (0, 1):
        where = [jax.random.randint(jax.random.fold_in(own_key, axis), (), 0, length) for axis, length in enumerate(values.shape)]
        where[longest] = (where[longest] + shift) % values.shape[longest]
        spots.append(tuple(where))
    return values.at[spots[0]].set(least).at[spots[1]].set(high)


def shard_levels(own_key, dims, cuts, least, high):
    level = 1.0
    for position, shards_of in cuts:
        steps = jax.random.uniform(jax.random.fold_in(jax.random.fold_in(own_key, 6), position), (shards_of,), jnp.float32, least / len(cuts), high / len(cuts))
        level = level * jnp.repeat(jnp.exp(steps), dims[position] // shards_of).reshape((-1,) + (1,) * (len(dims) - 1 - position))
    return level


def centred(stream_key, extent, deviation, reach, shards=(), kind=jnp.bfloat16):
    factor_of = shard_levels(stream_key, extent, shards, -0.22, 0.18) if shards else 1.0
    values = jax.random.normal(stream_key, extent, jnp.float32) * deviation * factor_of
    return jnp.minimum(jnp.maximum(values, -reach), reach).astype(kind)


def setup_inputs(seed: int = 0) -> dict:
    seeds = jax.random.split(jax.random.key(seed), 5)
    vacancy = centred(seeds[0], (NX, NY, NZ), 1.0, 6.0, ((0, 2), (1, 4), (2, 4)), jnp.float32)
    grain_label = plant(jax.random.randint(seeds[1], (NX, NY, NZ), 0, 8), jax.random.fold_in(seeds[1], 1), 0, 7).astype(jnp.int32)
    pore_mask = plant((jax.random.randint(seeds[2], (NX, NY, NZ), 0, 3) < 1).astype(jnp.int32), jax.random.fold_in(seeds[2], 1), 0, 1)
    cotangent = centred(seeds[3], (NX, NY, NZ), 1.0, 6.0, ((0, 2), (1, 4), (2, 4)), jnp.float32)
    return {"vacancy": vacancy, "grain_label": grain_label, "pore_mask": pore_mask, "cotangent": cotangent}


cross_rate = 0.0125
boundary_gain = 3.0


def face_value(mobility_here, mobility_there, label_here, label_there):
    harmonic = 2.0 * mobility_here * mobility_there / (mobility_here + mobility_there)
    return harmonic * jnp.where(label_here != label_there, boundary_gain, 1.0)


def factor_rows(lower_band, main_band, upper_band):
    def advance(previous, entries):
        below_value, centre_value, above_value = entries
        pivot_value = centre_value - below_value * previous
        ratio_value = above_value / pivot_value
        return ratio_value, (ratio_value, pivot_value)
    anchor = jnp.zeros(main_band.shape[1:], main_band.dtype)
    _, (ratios, pivots) = lax.scan(advance, anchor, (lower_band, main_band, upper_band))
    return ratios, pivots


def apply_rows(lower_band, ratios, pivots, source):
    def descend(previous, entries):
        below_value, pivot_value, source_value = entries
        solved_value = (source_value - below_value * previous) / pivot_value
        return solved_value, solved_value
    anchor = jnp.zeros(source.shape[1:], source.dtype)
    _, forward_sweep = lax.scan(descend, anchor, (lower_band, pivots, source))

    def ascend(previous, entries):
        ratio_value, sweep_value = entries
        solved_value = sweep_value - ratio_value * previous
        return solved_value, solved_value
    _, result = lax.scan(ascend, anchor, (ratios, forward_sweep), reverse=True)
    return result


def cyclic_prepare(lower_band, main_band, upper_band):
    interior = main_band.shape[0] - 1
    ratios, pivots = factor_rows(lower_band[:interior], main_band[:interior], upper_band[:interior])
    filler = jnp.zeros((interior - 1,) + main_band.shape[1:], main_band.dtype)
    coupling = jnp.concatenate([lower_band[:1], filler]) + jnp.concatenate([filler, upper_band[interior - 1:interior]])
    linked = apply_rows(lower_band[:interior], ratios, pivots, coupling)
    closing = main_band[interior] - lower_band[interior] * linked[interior - 1] - upper_band[interior] * linked[0]
    return (lower_band[:interior], ratios, pivots, linked, lower_band[interior], upper_band[interior], closing)


def cyclic_apply(prepared, source):
    lower_inner, ratios, pivots, linked, last_lower, last_upper, closing = prepared
    interior = ratios.shape[0]
    inner_values = apply_rows(lower_inner, ratios, pivots, source[:interior])
    separator = (source[interior] - last_lower * inner_values[interior - 1] - last_upper * inner_values[0]) / closing
    return jnp.concatenate([inner_values - linked * separator[None], separator[None]])


def reference(vacancy, grain_label, pore_mask, cotangent):
    mobility = 1.0 + 2.0 * pore_mask.astype(jnp.float32)
    weight = 0.5 * (1.0 + mobility)
    cycle_step = float(DT_X)
    forward_face = face_value(mobility, jnp.roll(mobility, -1, 0), grain_label, jnp.roll(grain_label, -1, 0))
    backward_face = jnp.roll(forward_face, 1, 0)
    lower_band = -cycle_step * backward_face * jnp.roll(weight, 1, 0)
    main_band = 1.0 + cycle_step * weight * (backward_face + forward_face)
    upper_band = -cycle_step * forward_face * jnp.roll(weight, -1, 0)
    lower_dual = -cycle_step * backward_face * weight
    upper_dual = -cycle_step * forward_face * weight
    padded_mobility = jnp.pad(mobility, ((0, 0), (1, 1), (1, 1)))
    padded_labels = jnp.pad(grain_label, ((0, 0), (1, 1), (1, 1)))
    faces_rows = face_value(padded_mobility[:, :-1, 1:-1], padded_mobility[:, 1:, 1:-1],
                            padded_labels[:, :-1, 1:-1], padded_labels[:, 1:, 1:-1])
    faces_depth = face_value(padded_mobility[:, 1:-1, :-1], padded_mobility[:, 1:-1, 1:],
                             padded_labels[:, 1:-1, :-1], padded_labels[:, 1:-1, 1:])

    def cross_flux(field):
        padded = jnp.pad(field, ((0, 0), (1, 1), (1, 1)))
        fluxes = faces_rows[:, 1:] * (padded[:, 2:, 1:-1] - field)
        fluxes = fluxes + faces_rows[:, :-1] * (padded[:, :-2, 1:-1] - field)
        fluxes = fluxes + faces_depth[:, :, 1:] * (padded[:, 1:-1, 2:] - field)
        fluxes = fluxes + faces_depth[:, :, :-1] * (padded[:, 1:-1, :-2] - field)
        return fluxes

    forward_prep = cyclic_prepare(lower_band, main_band, upper_band)
    adjoint_prep = cyclic_prepare(lower_dual, main_band, upper_dual)
    field_one = cyclic_apply(forward_prep, vacancy + cross_rate * cross_flux(weight * vacancy))
    final_field = cyclic_apply(forward_prep, field_one + cross_rate * cross_flux(weight * field_one))
    adjoint_one = cyclic_apply(adjoint_prep, cotangent)
    adjoint_two = cyclic_apply(adjoint_prep, adjoint_one + cross_rate * (weight * cross_flux(adjoint_one)))
    gradient = adjoint_two + cross_rate * (weight * cross_flux(adjoint_two))
    return final_field, gradient
```

```python
import jax
import jax.numpy as jnp
from jax import lax
from jax.experimental import pallas as pl
from jax.experimental.pallas import tpu as pltpu
from jax.sharding import PartitionSpec as P

cross_rate = 0.0125
boundary_gain = 3.0
F32 = jnp.float32


def face_value(mobility_here, mobility_there, label_here, label_there):
    harmonic = 2.0 * mobility_here * mobility_there / (mobility_here + mobility_there)
    return harmonic * jnp.where(label_here != label_there, boundary_gain, 1.0)


def _vmem():
    return pl.BlockSpec(memory_space=pltpu.VMEM)


def _smem():
    return pl.BlockSpec(memory_space=pltpu.SMEM)


def _shift(x, edge, axis, up):
    n = x.shape[axis]
    idx = lax.broadcasted_iota(jnp.int32, x.shape, axis)
    edge = jnp.broadcast_to(edge, x.shape)
    if up:
        return jnp.where(idx == n - 1, edge, pltpu.roll(x, n - 1, axis))
    return jnp.where(idx == 0, edge, pltpu.roll(x, 1, axis))


def _neighbours(x, ylo, yhi, zlo, zhi):
    return (
        _shift(x, yhi, 0, True),
        _shift(x, ylo, 0, False),
        _shift(x, zhi, 1, True),
        _shift(x, zlo, 1, False),
    )


def _faces(mob, lab, mob_n, lab_n):
    ups = (True, False, True, False)
    out = []
    for up, mn, ln in zip(ups, mob_n, lab_n):
        if up:
            out.append(face_value(mob, mn, lab, ln))
        else:
            out.append(face_value(mn, mob, ln, lab))
    return out


def _flux(u, u_n, faces):
    total = faces[0] * (u_n[0] - u)
    total = total + faces[1] * (u_n[1] - u)
    total = total + faces[2] * (u_n[2] - u)
    total = total + faces[3] * (u_n[3] - u)
    return total


def _geo_row(i, pore_ref, lab_ref, gy_lo, gy_hi, gz_lo, gz_hi):
    mob = 1.0 + 2.0 * pore_ref[i].astype(F32)
    lab = lab_ref[i].astype(F32)
    mob_n = _neighbours(mob, gy_lo[0, i], gy_hi[0, i], gz_lo[0, i], gz_hi[0, i])
    lab_n = _neighbours(lab, gy_lo[1, i], gy_hi[1, i], gz_lo[1, i], gz_hi[1, i])
    return mob, lab, mob_n, _faces(mob, lab, mob_n, lab_n)


def _sweep(m, lower, pivots, ratios, source):
    ys = [None] * m
    prev = None
    for r in range(m - 1):
        num = source[r]
        if num is None:
            if prev is None:
                continue
            num = -(lower[r] * prev)
        elif prev is not None:
            num = num - lower[r] * prev
        ys[r] = num / pivots[r]
        prev = ys[r]
    xs = [None] * m
    prev = None
    for r in range(m - 2, -1, -1):
        if prev is None:
            xs[r] = ys[r]
        elif ys[r] is None:
            xs[r] = -(ratios[r] * prev)
        else:
            xs[r] = ys[r] - ratios[r] * prev
        prev = xs[r]
    return xs


def _prep_kernel(cs, vac_ref, pore_ref, lab_ref, cot_ref, bx_lo, bx_hi, gy_lo, gy_hi, gz_lo, gz_hi,
                 fac_ref, loc_ref, rows_ref):
    m = vac_ref.shape[0]
    zero = jnp.zeros(vac_ref.shape[1:], F32)
    mobs = [1.0 + 2.0 * pore_ref[r].astype(F32) for r in range(m)]
    labs = [lab_ref[r].astype(F32) for r in range(m)]
    m_ext = [bx_lo[0]] + mobs + [bx_hi[0]]
    l_ext = [bx_lo[1]] + labs + [bx_hi[1]]
    w_ext = [0.5 * (1.0 + x) for x in m_ext]
    faces = [face_value(m_ext[k], m_ext[k + 1], l_ext[k], l_ext[k + 1]) for k in range(m + 1)]
    bands = {"f": ([], [], []), "a": ([], [], [])}
    for r in range(m):
        bf, ff = faces[r], faces[r + 1]
        w = w_ext[r + 1]
        main = 1.0 + cs * w * (bf + ff)
        bands["f"][0].append(-cs * bf * w_ext[r])
        bands["f"][1].append(main)
        bands["f"][2].append(-cs * ff * w_ext[r + 2])
        bands["a"][0].append(-cs * bf * w)
        bands["a"][1].append(main)
        bands["a"][2].append(-cs * ff * w)

    src_f = []
    for i in range(m):
        mob, lab, mob_n, fc = _geo_row(i, pore_ref, lab_ref, gy_lo, gy_hi, gz_lo, gz_hi)
        v = vac_ref[i]
        u = w_ext[i + 1] * v
        v_n = _neighbours(v, gy_lo[2, i], gy_hi[2, i], gz_lo[2, i], gz_hi[2, i])
        u_n = [0.5 * (1.0 + mn) * vn for mn, vn in zip(mob_n, v_n)]
        src_f.append(v + cross_rate * (1.0 * _flux(u, u_n, fc)))
    src_a = [cot_ref[r] for r in range(m)]

    for c, key, src in ((0, "f", src_f), (1, "a", src_a)):
        lower, main, upper = bands[key]
        pivots, ratios = [], []
        prev = None
        for r in range(m - 1):
            piv = main[r] if prev is None else main[r] - lower[r] * prev
            rat = upper[r] / piv
            pivots.append(piv)
            ratios.append(rat)
            prev = rat
        left_src = [lower[0]] + [None] * (m - 1)
        right_src = [None] * (m - 2) + [upper[m - 2], None]
        left = _sweep(m, lower, pivots, ratios, left_src)
        right = _sweep(m, lower, pivots, ratios, right_src)
        local = _sweep(m, lower, pivots, ratios, src[: m - 1] + [None])
        for r in range(m):
            fac_ref[c, 0, r] = lower[r]
            fac_ref[c, 1, r] = ratios[r] if r < m - 1 else zero
            fac_ref[c, 2, r] = pivots[r] if r < m - 1 else zero + 1.0
            fac_ref[c, 3, r] = left[r] if r < m - 1 else zero
            fac_ref[c, 4, r] = right[r] if r < m - 1 else zero - 1.0
            loc_ref[c, r] = local[r] if r < m - 1 else zero
        last_lower = lower[m - 1]
        rows_ref[c, 0] = last_lower * left[m - 2]
        rows_ref[c, 1] = main[m - 1] - last_lower * right[m - 2]
        rows_ref[c, 2] = upper[m - 1]
        rows_ref[c, 3] = left[0]
        rows_ref[c, 4] = right[0]
        rows_ref[c, 5] = src[m - 1] - last_lower * local[m - 2]
        rows_ref[c, 6] = local[0]


def _reduced_solve(gs, gv, voff, c, n):
    g = [[gs[p, c, k] for k in range(5)] for p in range(n)]
    lower = [-g[p][0] for p in range(n)]
    main = [g[p][1] - g[p][2] * g[(p + 1) % n][3] for p in range(n)]
    upper = [-g[p][2] * g[(p + 1) % n][4] for p in range(n)]
    src = [gv[p, c, voff] - g[p][2] * gv[(p + 1) % n, c, voff + 1] for p in range(n)]
    k_in = n - 1
    pivots, ratios = [], []
    prev = None
    for r in range(k_in):
        piv = main[r] if prev is None else main[r] - lower[r] * prev
        rat = upper[r] / piv
        pivots.append(piv)
        ratios.append(rat)
        prev = rat

    def apply(source):
        ys = []
        prev = None
        for r in range(k_in):
            num = source[r] if prev is None else source[r] - lower[r] * prev
            ys.append(num / pivots[r])
            prev = ys[-1]
        xs = [None] * k_in
        prev = None
        for r in range(k_in - 1, -1, -1):
            xs[r] = ys[r] if prev is None else ys[r] - ratios[r] * prev
            prev = xs[r]
        return xs

    coupling = []
    for r in range(k_in):
        term = None
        if r == 0:
            term = lower[0]
        if r == k_in - 1:
            term = upper[k_in - 1] if term is None else term + upper[k_in - 1]
        coupling.append(term if term is not None else jnp.zeros_like(lower[0]))
    linked = apply(coupling)
    closing = main[k_in] - lower[k_in] * linked[k_in - 1] - upper[k_in] * linked[0]
    inner = apply(src[:k_in])
    sep = (src[k_in] - lower[k_in] * inner[k_in - 1] - upper[k_in] * inner[0]) / closing
    return [inner[r] - linked[r] * sep for r in range(k_in)] + [sep]


def _combine_kernel(voff, stacked, pos_ref, gs_ref, gv_ref, fac_ref, loc_ref, *refs):
    if stacked:
        out_ref, sep_ref = refs
        outs = (out_ref.at[0], out_ref.at[1])
    else:
        out0, out1, sep_ref = refs
        outs = (out0, out1)
    n = gs_ref.shape[0]
    m = loc_ref.shape[1]
    p = pos_ref[0]
    for c in range(2):
        seps = _reduced_solve(gs_ref, gv_ref, voff, c, n)
        for q in range(n):
            sep_ref[q] = seps[q]
        own = sep_ref[p]
        prior = sep_ref[(p + n - 1) % n]
        for r in range(m):
            outs[c][r] = loc_ref[c, r] - fac_ref[c, 3, r] * prior - fac_ref[c, 4, r] * own


def _second_kernel(pore_ref, lab_ref, fa_ref, fac_ref, gy_lo, gy_hi, gz_lo, gz_hi,
                   hy_lo, hy_hi, hz_lo, hz_hi, loc_ref, vals_ref):
    m = pore_ref.shape[0]
    srcs = ([], [])
    for i in range(m):
        mob, lab, mob_n, fc = _geo_row(i, pore_ref, lab_ref, gy_lo, gy_hi, gz_lo, gz_hi)
        w = 0.5 * (1.0 + mob)
        f1 = fa_ref[0, i]
        f_n = _neighbours(f1, hy_lo[0, i], hy_hi[0, i], hz_lo[0, i], hz_hi[0, i])
        u_n = [0.5 * (1.0 + mn) * fn for mn, fn in zip(mob_n, f_n)]
        srcs[0].append(f1 + cross_rate * (1.0 * _flux(w * f1, u_n, fc)))
        a1 = fa_ref[1, i]
        a_n = _neighbours(a1, hy_lo[1, i], hy_hi[1, i], hz_lo[1, i], hz_hi[1, i])
        srcs[1].append(a1 + cross_rate * (w * _flux(a1, a_n, fc)))
    zero = jnp.zeros(pore_ref.shape[1:], F32)
    for c in range(2):
        lower = [fac_ref[c, 0, r] for r in range(m)]
        ratios = [fac_ref[c, 1, r] for r in range(m - 1)]
        pivots = [fac_ref[c, 2, r] for r in range(m - 1)]
        src = srcs[c]
        local = _sweep(m, lower, pivots, ratios, src[: m - 1] + [None])
        for r in range(m):
            loc_ref[c, r] = local[r] if r < m - 1 else zero
        vals_ref[c, 0] = src[m - 1] - lower[m - 1] * local[m - 2]
        vals_ref[c, 1] = local[0]


def _gradient_kernel(pore_ref, lab_ref, a2_ref, gy_lo, gy_hi, gz_lo, gz_hi,
                     hy_lo, hy_hi, hz_lo, hz_hi, out_ref):
    m = pore_ref.shape[0]
    for i in range(m):
        mob, lab, mob_n, fc = _geo_row(i, pore_ref, lab_ref, gy_lo, gy_hi, gz_lo, gz_hi)
        w = 0.5 * (1.0 + mob)
        a2 = a2_ref[i]
        a_n = _neighbours(a2, hy_lo[0, i], hy_hi[0, i], hz_lo[0, i], hz_hi[0, i])
        out_ref[i] = a2 + cross_rate * (w * _flux(a2, a_n, fc))


def _halo_pairs(axis, periodic):
    count = lax.axis_size(axis)
    forward = [(i, i + 1) for i in range(count - 1)]
    if periodic:
        forward.append((count - 1, 0))
    backward = [(t, s) for s, t in forward]
    return forward, backward


def _exchange(first, last, axis, periodic):
    forward, backward = _halo_pairs(axis, periodic)
    lo = lax.ppermute(last, axis, forward)
    hi = lax.ppermute(first, axis, backward)
    return lo, hi


def _yz_halos(stack):
    y = stack.shape[2]
    z = stack.shape[3]
    gy_lo, gy_hi = _exchange(stack[:, :, 0:1, :], stack[:, :, y - 1 : y, :], "gy", False)
    gz_lo, gz_hi = _exchange(stack[:, :, :, 0:1], stack[:, :, :, z - 1 : z], "gz", False)
    return gy_lo, gy_hi, gz_lo, gz_hi


def shards(vacancy, grain_label, pore_mask, cotangent):
    m, ny, nz = vacancy.shape
    n_blk = lax.axis_size("blk")
    cycle_step = float((m * n_blk) ** 2 // 64)
    shape = jax.ShapeDtypeStruct((m, ny, nz), F32)

    mobility = 1.0 + 2.0 * pore_mask.astype(F32)
    labels = grain_label.astype(F32)
    geo0 = jnp.stack([mobility[0], labels[0]])
    geo1 = jnp.stack([mobility[m - 1], labels[m - 1]])
    bx_lo, bx_hi = _exchange(geo0, geo1, "blk", True)
    gy_lo, gy_hi, gz_lo, gz_hi = _yz_halos(jnp.stack([mobility, labels, vacancy]))

    fac, loc, rows = pl.pallas_call(
        lambda *r: _prep_kernel(cycle_step, *r),
        out_shape=(
            jax.ShapeDtypeStruct((2, 5, m, ny, nz), F32),
            jax.ShapeDtypeStruct((2, m, ny, nz), F32),
            jax.ShapeDtypeStruct((2, 7, ny, nz), F32),
        ),
        in_specs=[_vmem()] * 10,
        out_specs=(_vmem(), _vmem(), _vmem()),
    )(vacancy, pore_mask, grain_label, cotangent, bx_lo, bx_hi, gy_lo, gy_hi, gz_lo, gz_hi)

    gathered = lax.all_gather(rows, "blk", axis=0, tiled=False)
    pos = jnp.reshape(lax.axis_index("blk"), (1,)).astype(jnp.int32)

    fa = pl.pallas_call(
        lambda *r: _combine_kernel(5, True, *r),
        out_shape=jax.ShapeDtypeStruct((2, m, ny, nz), F32),
        in_specs=[_smem()] + [_vmem()] * 4,
        out_specs=_vmem(),
        scratch_shapes=[pltpu.VMEM((n_blk, ny, nz), F32)],
    )(pos, gathered, gathered, fac, loc)

    hy_lo, hy_hi, hz_lo, hz_hi = _yz_halos(fa)
    loc2, vals2 = pl.pallas_call(
        _second_kernel,
        out_shape=(
            jax.ShapeDtypeStruct((2, m, ny, nz), F32),
            jax.ShapeDtypeStruct((2, 2, ny, nz), F32),
        ),
        in_specs=[_vmem()] * 12,
        out_specs=(_vmem(), _vmem()),
    )(pore_mask, grain_label, fa, fac, gy_lo, gy_hi, gz_lo, gz_hi, hy_lo, hy_hi, hz_lo, hz_hi)

    gathered2 = lax.all_gather(vals2, "blk", axis=0, tiled=False)
    final_field, adjoint_two = pl.pallas_call(
        lambda *r: _combine_kernel(0, False, *r),
        out_shape=(shape, shape),
        in_specs=[_smem()] + [_vmem()] * 4,
        out_specs=(_vmem(), _vmem()),
        scratch_shapes=[pltpu.VMEM((n_blk, ny, nz), F32)],
    )(pos, gathered, gathered2, fac, loc2)

    a2_lo, a2_hi, a2z_lo, a2z_hi = _yz_halos(adjoint_two[None])
    gradient = pl.pallas_call(
        _gradient_kernel,
        out_shape=shape,
        in_specs=[_vmem()] * 11,
        out_specs=_vmem(),
    )(pore_mask, grain_label, adjoint_two, gy_lo, gy_hi, gz_lo, gz_hi, a2_lo, a2_hi, a2z_lo, a2z_hi)
    return (final_field, gradient)


def solution(mesh):
    in_specs = (
        P("blk", "gy", "gz"),
        P("blk", "gy", "gz"),
        P("blk", "gy", "gz"),
        P("blk", "gy", "gz"),
    )
    out_specs = (P("blk", "gy", "gz"), P("blk", "gy", "gz"))
    return jax.shard_map(shards, mesh=mesh, in_specs=in_specs, out_specs=out_specs, check_vma=False)
```

```python
import jax
import jax.numpy as jnp
from jax import lax
from jax.experimental import pallas as pl
from jax.experimental.pallas import tpu as pltpu
from jax.sharding import PartitionSpec as P

cross_rate = 0.0125
boundary_gain = 3.0
F32 = jnp.float32


def face_value(mobility_here, mobility_there, label_here, label_there):
    harmonic = 2.0 * mobility_here * mobility_there / (mobility_here + mobility_there)
    return harmonic * jnp.where(label_here != label_there, boundary_gain, 1.0)


def _vmem():
    return pl.BlockSpec(memory_space=pltpu.VMEM)


def _smem():
    return pl.BlockSpec(memory_space=pltpu.SMEM)


def _shift(x, edge, axis, up):
    n = x.shape[axis]
    idx = lax.broadcasted_iota(jnp.int32, x.shape, axis)
    edge = jnp.broadcast_to(edge, x.shape)
    if up:
        return jnp.where(idx == n - 1, edge, pltpu.roll(x, n - 1, axis))
    return jnp.where(idx == 0, edge, pltpu.roll(x, 1, axis))


def _neighbours(x, ylo, yhi, zlo, zhi):
    return (
        _shift(x, yhi, 0, True),
        _shift(x, ylo, 0, False),
        _shift(x, zhi, 1, True),
        _shift(x, zlo, 1, False),
    )


def _faces(mob, lab, mob_n, lab_n):
    ups = (True, False, True, False)
    out = []
    for up, mn, ln in zip(ups, mob_n, lab_n):
        if up:
            out.append(face_value(mob, mn, lab, ln))
        else:
            out.append(face_value(mn, mob, ln, lab))
    return out


def _flux(u, u_n, faces):
    total = faces[0] * (u_n[0] - u)
    total = total + faces[1] * (u_n[1] - u)
    total = total + faces[2] * (u_n[2] - u)
    total = total + faces[3] * (u_n[3] - u)
    return total


def _yrow(ref, c, i):
    return ref[c, pl.ds(i, 1), :]


def _geo_row(i, pore_ref, lab_ref, gy_lo, gy_hi, gz_lo, gz_hi):
    mob = 1.0 + 2.0 * pore_ref[i].astype(F32)
    lab = lab_ref[i].astype(F32)
    mob_n = _neighbours(mob, _yrow(gy_lo, 0, i), _yrow(gy_hi, 0, i), gz_lo[0, i], gz_hi[0, i])
    lab_n = _neighbours(lab, _yrow(gy_lo, 1, i), _yrow(gy_hi, 1, i), gz_lo[1, i], gz_hi[1, i])
    return mob, lab, mob_n, _faces(mob, lab, mob_n, lab_n)


def _sweep(m, lower, pivots, ratios, source):
    ys = [None] * m
    prev = None
    for r in range(m - 1):
        num = source[r]
        if num is None:
            if prev is None:
                continue
            num = -(lower[r] * prev)
        elif prev is not None:
            num = num - lower[r] * prev
        ys[r] = num / pivots[r]
        prev = ys[r]
    xs = [None] * m
    prev = None
    for r in range(m - 2, -1, -1):
        if prev is None:
            xs[r] = ys[r]
        elif ys[r] is None:
            xs[r] = -(ratios[r] * prev)
        else:
            xs[r] = ys[r] - ratios[r] * prev
        prev = xs[r]
    return xs


def _prep_kernel(cs, vac_ref, pore_ref, lab_ref, cot_ref, bx_lo, bx_hi, gy_lo, gy_hi, gz_lo, gz_hi,
                 fac_ref, loc_ref, rows_ref):
    m = vac_ref.shape[0]
    zero = jnp.zeros(vac_ref.shape[1:], F32)
    mobs = [1.0 + 2.0 * pore_ref[r].astype(F32) for r in range(m)]
    labs = [lab_ref[r].astype(F32) for r in range(m)]
    m_ext = [bx_lo[0]] + mobs + [bx_hi[0]]
    l_ext = [bx_lo[1]] + labs + [bx_hi[1]]
    w_ext = [0.5 * (1.0 + x) for x in m_ext]
    faces = [face_value(m_ext[k], m_ext[k + 1], l_ext[k], l_ext[k + 1]) for k in range(m + 1)]
    bands = {"f": ([], [], []), "a": ([], [], [])}
    for r in range(m):
        bf, ff = faces[r], faces[r + 1]
        w = w_ext[r + 1]
        main = 1.0 + cs * w * (bf + ff)
        bands["f"][0].append(-cs * bf * w_ext[r])
        bands["f"][1].append(main)
        bands["f"][2].append(-cs * ff * w_ext[r + 2])
        bands["a"][0].append(-cs * bf * w)
        bands["a"][1].append(main)
        bands["a"][2].append(-cs * ff * w)

    src_f = []
    for i in range(m):
        mob, lab, mob_n, fc = _geo_row(i, pore_ref, lab_ref, gy_lo, gy_hi, gz_lo, gz_hi)
        v = vac_ref[i]
        u = w_ext[i + 1] * v
        v_n = _neighbours(v, _yrow(gy_lo, 2, i), _yrow(gy_hi, 2, i), gz_lo[2, i], gz_hi[2, i])
        u_n = [0.5 * (1.0 + mn) * vn for mn, vn in zip(mob_n, v_n)]
        src_f.append(v + cross_rate * (1.0 * _flux(u, u_n, fc)))
    src_a = [cot_ref[r] for r in range(m)]

    for c, key, src in ((0, "f", src_f), (1, "a", src_a)):
        lower, main, upper = bands[key]
        pivots, ratios = [], []
        prev = None
        for r in range(m - 1):
            piv = main[r] if prev is None else main[r] - lower[r] * prev
            rat = upper[r] / piv
            pivots.append(piv)
            ratios.append(rat)
            prev = rat
        left_src = [lower[0]] + [None] * (m - 1)
        right_src = [None] * (m - 2) + [upper[m - 2], None]
        left = _sweep(m, lower, pivots, ratios, left_src)
        right = _sweep(m, lower, pivots, ratios, right_src)
        local = _sweep(m, lower, pivots, ratios, src[: m - 1] + [None])
        for r in range(m):
            fac_ref[c, 0, r] = lower[r]
            fac_ref[c, 1, r] = ratios[r] if r < m - 1 else zero
            fac_ref[c, 2, r] = pivots[r] if r < m - 1 else zero + 1.0
            fac_ref[c, 3, r] = left[r] if r < m - 1 else zero
            fac_ref[c, 4, r] = right[r] if r < m - 1 else zero - 1.0
            loc_ref[c, r] = local[r] if r < m - 1 else zero
        last_lower = lower[m - 1]
        rows_ref[c, 0] = last_lower * left[m - 2]
        rows_ref[c, 1] = main[m - 1] - last_lower * right[m - 2]
        rows_ref[c, 2] = upper[m - 1]
        rows_ref[c, 3] = left[0]
        rows_ref[c, 4] = right[0]
        rows_ref[c, 5] = src[m - 1] - last_lower * local[m - 2]
        rows_ref[c, 6] = local[0]


def _reduced_solve(gs, gv, voff, c, n):
    g = [[gs[p, c, k] for k in range(5)] for p in range(n)]
    lower = [-g[p][0] for p in range(n)]
    main = [g[p][1] - g[p][2] * g[(p + 1) % n][3] for p in range(n)]
    upper = [-g[p][2] * g[(p + 1) % n][4] for p in range(n)]
    src = [gv[p, c, voff] - g[p][2] * gv[(p + 1) % n, c, voff + 1] for p in range(n)]
    k_in = n - 1
    pivots, ratios = [], []
    prev = None
    for r in range(k_in):
        piv = main[r] if prev is None else main[r] - lower[r] * prev
        rat = upper[r] / piv
        pivots.append(piv)
        ratios.append(rat)
        prev = rat

    def apply(source):
        ys = []
        prev = None
        for r in range(k_in):
            num = source[r] if prev is None else source[r] - lower[r] * prev
            ys.append(num / pivots[r])
            prev = ys[-1]
        xs = [None] * k_in
        prev = None
        for r in range(k_in - 1, -1, -1):
            xs[r] = ys[r] if prev is None else ys[r] - ratios[r] * prev
            prev = xs[r]
        return xs

    coupling = []
    for r in range(k_in):
        term = None
        if r == 0:
            term = lower[0]
        if r == k_in - 1:
            term = upper[k_in - 1] if term is None else term + upper[k_in - 1]
        coupling.append(term if term is not None else jnp.zeros_like(lower[0]))
    linked = apply(coupling)
    closing = main[k_in] - lower[k_in] * linked[k_in - 1] - upper[k_in] * linked[0]
    inner = apply(src[:k_in])
    sep = (src[k_in] - lower[k_in] * inner[k_in - 1] - upper[k_in] * inner[0]) / closing
    return [inner[r] - linked[r] * sep for r in range(k_in)] + [sep]


def _combine_kernel(voff, stacked, pos_ref, gs_ref, gv_ref, fac_ref, loc_ref, *refs):
    if stacked:
        out_ref, sep_ref = refs
        outs = (out_ref.at[0], out_ref.at[1])
    else:
        out0, out1, sep_ref = refs
        outs = (out0, out1)
    n = gs_ref.shape[0]
    m = loc_ref.shape[1]
    p = pos_ref[0]
    for c in range(2):
        seps = _reduced_solve(gs_ref, gv_ref, voff, c, n)
        for q in range(n):
            sep_ref[q] = seps[q]
        own = sep_ref[p]
        prior = sep_ref[(p + n - 1) % n]
        for r in range(m):
            outs[c][r] = loc_ref[c, r] - fac_ref[c, 3, r] * prior - fac_ref[c, 4, r] * own


def _second_kernel(pore_ref, lab_ref, fa_ref, fac_ref, gy_lo, gy_hi, gz_lo, gz_hi,
                   hy_lo, hy_hi, hz_lo, hz_hi, loc_ref, vals_ref):
    m = pore_ref.shape[0]
    srcs = ([], [])
    for i in range(m):
        mob, lab, mob_n, fc = _geo_row(i, pore_ref, lab_ref, gy_lo, gy_hi, gz_lo, gz_hi)
        w = 0.5 * (1.0 + mob)
        f1 = fa_ref[0, i]
        f_n = _neighbours(f1, _yrow(hy_lo, 0, i), _yrow(hy_hi, 0, i), hz_lo[0, i], hz_hi[0, i])
        u_n = [0.5 * (1.0 + mn) * fn for mn, fn in zip(mob_n, f_n)]
        srcs[0].append(f1 + cross_rate * (1.0 * _flux(w * f1, u_n, fc)))
        a1 = fa_ref[1, i]
        a_n = _neighbours(a1, _yrow(hy_lo, 1, i), _yrow(hy_hi, 1, i), hz_lo[1, i], hz_hi[1, i])
        srcs[1].append(a1 + cross_rate * (w * _flux(a1, a_n, fc)))
    zero = jnp.zeros(pore_ref.shape[1:], F32)
    for c in range(2):
        lower = [fac_ref[c, 0, r] for r in range(m)]
        ratios = [fac_ref[c, 1, r] for r in range(m - 1)]
        pivots = [fac_ref[c, 2, r] for r in range(m - 1)]
        src = srcs[c]
        local = _sweep(m, lower, pivots, ratios, src[: m - 1] + [None])
        for r in range(m):
            loc_ref[c, r] = local[r] if r < m - 1 else zero
        vals_ref[c, 0] = src[m - 1] - lower[m - 1] * local[m - 2]
        vals_ref[c, 1] = local[0]


def _gradient_kernel(pore_ref, lab_ref, a2_ref, gy_lo, gy_hi, gz_lo, gz_hi,
                     hy_lo, hy_hi, hz_lo, hz_hi, out_ref):
    m = pore_ref.shape[0]
    for i in range(m):
        mob, lab, mob_n, fc = _geo_row(i, pore_ref, lab_ref, gy_lo, gy_hi, gz_lo, gz_hi)
        w = 0.5 * (1.0 + mob)
        a2 = a2_ref[i]
        a_n = _neighbours(a2, _yrow(hy_lo, 0, i), _yrow(hy_hi, 0, i), hz_lo[0, i], hz_hi[0, i])
        out_ref[i] = a2 + cross_rate * (w * _flux(a2, a_n, fc))


def _halo_pairs(axis, periodic):
    count = lax.axis_size(axis)
    forward = [(i, i + 1) for i in range(count - 1)]
    if periodic:
        forward.append((count - 1, 0))
    backward = [(t, s) for s, t in forward]
    return forward, backward


def _exchange(first, last, axis, periodic):
    forward, backward = _halo_pairs(axis, periodic)
    lo = lax.ppermute(last, axis, forward)
    hi = lax.ppermute(first, axis, backward)
    return lo, hi


def _yz_halos(fields):
    y = fields[0].shape[1]
    z = fields[0].shape[2]
    gy_lo, gy_hi = _exchange(
        jnp.stack([f[:, 0, :] for f in fields]), jnp.stack([f[:, y - 1, :] for f in fields]), "gy", False
    )
    gz_lo, gz_hi = _exchange(
        jnp.stack([f[:, :, 0] for f in fields]), jnp.stack([f[:, :, z - 1] for f in fields]), "gz", False
    )
    return gy_lo, gy_hi, gz_lo[..., None], gz_hi[..., None]


def shards(vacancy, grain_label, pore_mask, cotangent):
    m, ny, nz = vacancy.shape
    n_blk = lax.axis_size("blk")
    cycle_step = float((m * n_blk) ** 2 // 64)
    shape = jax.ShapeDtypeStruct((m, ny, nz), F32)

    mobility = 1.0 + 2.0 * pore_mask.astype(F32)
    labels = grain_label.astype(F32)
    geo0 = jnp.stack([mobility[0], labels[0]])
    geo1 = jnp.stack([mobility[m - 1], labels[m - 1]])
    bx_lo, bx_hi = _exchange(geo0, geo1, "blk", True)
    gy_lo, gy_hi, gz_lo, gz_hi = _yz_halos([mobility, labels, vacancy])

    fac, loc, rows = pl.pallas_call(
        lambda *r: _prep_kernel(cycle_step, *r),
        out_shape=(
            jax.ShapeDtypeStruct((2, 5, m, ny, nz), F32),
            jax.ShapeDtypeStruct((2, m, ny, nz), F32),
            jax.ShapeDtypeStruct((2, 7, ny, nz), F32),
        ),
        in_specs=[_vmem()] * 10,
        out_specs=(_vmem(), _vmem(), _vmem()),
    )(vacancy, pore_mask, grain_label, cotangent, bx_lo, bx_hi, gy_lo, gy_hi, gz_lo, gz_hi)

    gathered = lax.all_gather(rows, "blk", axis=0, tiled=False)
    pos = jnp.reshape(lax.axis_index("blk"), (1,)).astype(jnp.int32)

    fa = pl.pallas_call(
        lambda *r: _combine_kernel(5, True, *r),
        out_shape=jax.ShapeDtypeStruct((2, m, ny, nz), F32),
        in_specs=[_smem()] + [_vmem()] * 4,
        out_specs=_vmem(),
        scratch_shapes=[pltpu.VMEM((n_blk, ny, nz), F32)],
    )(pos, gathered, gathered, fac, loc)

    hy_lo, hy_hi, hz_lo, hz_hi = _yz_halos([fa[0], fa[1]])
    loc2, vals2 = pl.pallas_call(
        _second_kernel,
        out_shape=(
            jax.ShapeDtypeStruct((2, m, ny, nz), F32),
            jax.ShapeDtypeStruct((2, 2, ny, nz), F32),
        ),
        in_specs=[_vmem()] * 12,
        out_specs=(_vmem(), _vmem()),
    )(pore_mask, grain_label, fa, fac, gy_lo, gy_hi, gz_lo, gz_hi, hy_lo, hy_hi, hz_lo, hz_hi)

    gathered2 = lax.all_gather(vals2, "blk", axis=0, tiled=False)
    final_field, adjoint_two = pl.pallas_call(
        lambda *r: _combine_kernel(0, False, *r),
        out_shape=(shape, shape),
        in_specs=[_smem()] + [_vmem()] * 4,
        out_specs=(_vmem(), _vmem()),
        scratch_shapes=[pltpu.VMEM((n_blk, ny, nz), F32)],
    )(pos, gathered, gathered2, fac, loc2)

    a2_lo, a2_hi, a2z_lo, a2z_hi = _yz_halos([adjoint_two])
    gradient = pl.pallas_call(
        _gradient_kernel,
        out_shape=shape,
        in_specs=[_vmem()] * 11,
        out_specs=_vmem(),
    )(pore_mask, grain_label, adjoint_two, gy_lo, gy_hi, gz_lo, gz_hi, a2_lo, a2_hi, a2z_lo, a2z_hi)
    return (final_field, gradient)


def solution(mesh):
    in_specs = (
        P("blk", "gy", "gz"),
        P("blk", "gy", "gz"),
        P("blk", "gy", "gz"),
        P("blk", "gy", "gz"),
    )
    out_specs = (P("blk", "gy", "gz"), P("blk", "gy", "gz"))
    return jax.shard_map(shards, mesh=mesh, in_specs=in_specs, out_specs=out_specs, check_vma=False)
```

```python
import jax
import jax.numpy as jnp
from jax import lax
from jax.experimental import pallas as pl
from jax.experimental.pallas import tpu as pltpu
from jax.sharding import PartitionSpec as P

cross_rate = 0.0125
boundary_gain = 3.0
F32 = jnp.float32


def face_value(mobility_here, mobility_there, label_here, label_there):
    harmonic = 2.0 * mobility_here * mobility_there / (mobility_here + mobility_there)
    return harmonic * jnp.where(label_here != label_there, boundary_gain, 1.0)


def _vmem():
    return pl.BlockSpec(memory_space=pltpu.VMEM)


def _smem():
    return pl.BlockSpec(memory_space=pltpu.SMEM)


def _shift(x, edge, axis, up):
    n = x.shape[axis]
    idx = lax.broadcasted_iota(jnp.int32, x.shape, axis)
    edge = jnp.broadcast_to(edge, x.shape)
    if up:
        return jnp.where(idx == n - 1, edge, pltpu.roll(x, n - 1, axis))
    return jnp.where(idx == 0, edge, pltpu.roll(x, 1, axis))


def _neighbours(x, ylo, yhi, zlo, zhi):
    return (
        _shift(x, yhi, 0, True),
        _shift(x, ylo, 0, False),
        _shift(x, zhi, 1, True),
        _shift(x, zlo, 1, False),
    )


def _faces(mob, lab, mob_n, lab_n):
    ups = (True, False, True, False)
    out = []
    for up, mn, ln in zip(ups, mob_n, lab_n):
        if up:
            out.append(face_value(mob, mn, lab, ln))
        else:
            out.append(face_value(mn, mob, ln, lab))
    return out


def _flux(u, u_n, faces):
    total = faces[0] * (u_n[0] - u)
    total = total + faces[1] * (u_n[1] - u)
    total = total + faces[2] * (u_n[2] - u)
    total = total + faces[3] * (u_n[3] - u)
    return total


def _yrow(ref, c, i):
    return ref[c, pl.ds(i, 1), :]


def _zcol(ref, c, i):
    return ref[c, :, pl.ds(i, 1)]


def _write_edges(edges, c, r, val):
    y_first, y_last, z_first, z_last = edges
    ny, nz = val.shape
    y_first[c, pl.ds(r, 1), :] = val[0:1, :]
    y_last[c, pl.ds(r, 1), :] = val[ny - 1 : ny, :]
    z_first[c, :, pl.ds(r, 1)] = val[:, 0:1]
    z_last[c, :, pl.ds(r, 1)] = val[:, nz - 1 : nz]


def _geo_row(i, pore_ref, lab_ref, gy_lo, gy_hi, gz_lo, gz_hi):
    mob = 1.0 + 2.0 * pore_ref[i].astype(F32)
    lab = lab_ref[i].astype(F32)
    mob_n = _neighbours(mob, _yrow(gy_lo, 0, i), _yrow(gy_hi, 0, i), _zcol(gz_lo, 0, i), _zcol(gz_hi, 0, i))
    lab_n = _neighbours(lab, _yrow(gy_lo, 1, i), _yrow(gy_hi, 1, i), _zcol(gz_lo, 1, i), _zcol(gz_hi, 1, i))
    return mob, lab, mob_n, _faces(mob, lab, mob_n, lab_n)


def _sweep(m, lower, pivots, ratios, source):
    ys = [None] * m
    prev = None
    for r in range(m - 1):
        num = source[r]
        if num is None:
            if prev is None:
                continue
            num = -(lower[r] * prev)
        elif prev is not None:
            num = num - lower[r] * prev
        ys[r] = num / pivots[r]
        prev = ys[r]
    xs = [None] * m
    prev = None
    for r in range(m - 2, -1, -1):
        if prev is None:
            xs[r] = ys[r]
        elif ys[r] is None:
            xs[r] = -(ratios[r] * prev)
        else:
            xs[r] = ys[r] - ratios[r] * prev
        prev = xs[r]
    return xs


def _prep_kernel(cs, vac_ref, pore_ref, lab_ref, cot_ref, bx_lo, bx_hi, gy_lo, gy_hi, gz_lo, gz_hi,
                 fac_ref, loc_ref, rows_ref):
    m = vac_ref.shape[0]
    zero = jnp.zeros(vac_ref.shape[1:], F32)
    mobs = [1.0 + 2.0 * pore_ref[r].astype(F32) for r in range(m)]
    labs = [lab_ref[r].astype(F32) for r in range(m)]
    m_ext = [bx_lo[0]] + mobs + [bx_hi[0]]
    l_ext = [bx_lo[1]] + labs + [bx_hi[1]]
    w_ext = [0.5 * (1.0 + x) for x in m_ext]
    faces = [face_value(m_ext[k], m_ext[k + 1], l_ext[k], l_ext[k + 1]) for k in range(m + 1)]
    bands = {"f": ([], [], []), "a": ([], [], [])}
    for r in range(m):
        bf, ff = faces[r], faces[r + 1]
        w = w_ext[r + 1]
        main = 1.0 + cs * w * (bf + ff)
        bands["f"][0].append(-cs * bf * w_ext[r])
        bands["f"][1].append(main)
        bands["f"][2].append(-cs * ff * w_ext[r + 2])
        bands["a"][0].append(-cs * bf * w)
        bands["a"][1].append(main)
        bands["a"][2].append(-cs * ff * w)

    src_f = []
    for i in range(m):
        mob, lab, mob_n, fc = _geo_row(i, pore_ref, lab_ref, gy_lo, gy_hi, gz_lo, gz_hi)
        v = vac_ref[i]
        u = w_ext[i + 1] * v
        v_n = _neighbours(v, _yrow(gy_lo, 2, i), _yrow(gy_hi, 2, i), _zcol(gz_lo, 2, i), _zcol(gz_hi, 2, i))
        u_n = [0.5 * (1.0 + mn) * vn for mn, vn in zip(mob_n, v_n)]
        src_f.append(v + cross_rate * (1.0 * _flux(u, u_n, fc)))
    src_a = [cot_ref[r] for r in range(m)]

    for c, key, src in ((0, "f", src_f), (1, "a", src_a)):
        lower, main, upper = bands[key]
        pivots, ratios = [], []
        prev = None
        for r in range(m - 1):
            piv = main[r] if prev is None else main[r] - lower[r] * prev
            rat = upper[r] / piv
            pivots.append(piv)
            ratios.append(rat)
            prev = rat
        left_src = [lower[0]] + [None] * (m - 1)
        right_src = [None] * (m - 2) + [upper[m - 2], None]
        left = _sweep(m, lower, pivots, ratios, left_src)
        right = _sweep(m, lower, pivots, ratios, right_src)
        local = _sweep(m, lower, pivots, ratios, src[: m - 1] + [None])
        for r in range(m):
            fac_ref[c, 0, r] = lower[r]
            fac_ref[c, 1, r] = ratios[r] if r < m - 1 else zero
            fac_ref[c, 2, r] = pivots[r] if r < m - 1 else zero + 1.0
            fac_ref[c, 3, r] = left[r] if r < m - 1 else zero
            fac_ref[c, 4, r] = right[r] if r < m - 1 else zero - 1.0
            loc_ref[c, r] = local[r] if r < m - 1 else zero
        last_lower = lower[m - 1]
        rows_ref[c, 0] = last_lower * left[m - 2]
        rows_ref[c, 1] = main[m - 1] - last_lower * right[m - 2]
        rows_ref[c, 2] = upper[m - 1]
        rows_ref[c, 3] = left[0]
        rows_ref[c, 4] = right[0]
        rows_ref[c, 5] = src[m - 1] - last_lower * local[m - 2]
        rows_ref[c, 6] = local[0]


def _reduced_solve(gs, gv, voff, c, n):
    g = [[gs[p, c, k] for k in range(5)] for p in range(n)]
    lower = [-g[p][0] for p in range(n)]
    main = [g[p][1] - g[p][2] * g[(p + 1) % n][3] for p in range(n)]
    upper = [-g[p][2] * g[(p + 1) % n][4] for p in range(n)]
    src = [gv[p, c, voff] - g[p][2] * gv[(p + 1) % n, c, voff + 1] for p in range(n)]
    k_in = n - 1
    pivots, ratios = [], []
    prev = None
    for r in range(k_in):
        piv = main[r] if prev is None else main[r] - lower[r] * prev
        rat = upper[r] / piv
        pivots.append(piv)
        ratios.append(rat)
        prev = rat

    def apply(source):
        ys = []
        prev = None
        for r in range(k_in):
            num = source[r] if prev is None else source[r] - lower[r] * prev
            ys.append(num / pivots[r])
            prev = ys[-1]
        xs = [None] * k_in
        prev = None
        for r in range(k_in - 1, -1, -1):
            xs[r] = ys[r] if prev is None else ys[r] - ratios[r] * prev
            prev = xs[r]
        return xs

    coupling = []
    for r in range(k_in):
        term = None
        if r == 0:
            term = lower[0]
        if r == k_in - 1:
            term = upper[k_in - 1] if term is None else term + upper[k_in - 1]
        coupling.append(term if term is not None else jnp.zeros_like(lower[0]))
    linked = apply(coupling)
    closing = main[k_in] - lower[k_in] * linked[k_in - 1] - upper[k_in] * linked[0]
    inner = apply(src[:k_in])
    sep = (src[k_in] - lower[k_in] * inner[k_in - 1] - upper[k_in] * inner[0]) / closing
    return [inner[r] - linked[r] * sep for r in range(k_in)] + [sep]


def _combine_kernel(voff, stacked, edge_of, pos_ref, gs_ref, gv_ref, fac_ref, loc_ref, *refs):
    if stacked:
        out_ref = refs[0]
        outs = (out_ref.at[0], out_ref.at[1])
        rest = refs[1:]
    else:
        outs = refs[:2]
        rest = refs[2:]
    edges, sep_ref = rest[:4], rest[4]
    n = gs_ref.shape[0]
    m = loc_ref.shape[1]
    p = pos_ref[0]
    for c in range(2):
        seps = _reduced_solve(gs_ref, gv_ref, voff, c, n)
        for q in range(n):
            sep_ref[q] = seps[q]
        own = sep_ref[p]
        prior = sep_ref[(p + n - 1) % n]
        for r in range(m):
            val = loc_ref[c, r] - fac_ref[c, 3, r] * prior - fac_ref[c, 4, r] * own
            outs[c][r] = val
            if c in edge_of:
                _write_edges(edges, edge_of[c], r, val)


def _edge_kernel(vac_ref, pore_ref, lab_ref, y_first, y_last, z_first, z_last, bx_first, bx_last):
    m = vac_ref.shape[0]
    edges = (y_first, y_last, z_first, z_last)
    for r in range(m):
        mob = 1.0 + 2.0 * pore_ref[r].astype(F32)
        lab = lab_ref[r].astype(F32)
        for c, val in enumerate((mob, lab, vac_ref[r])):
            _write_edges(edges, c, r, val)
        if r == 0:
            bx_first[0] = mob
            bx_first[1] = lab
        if r == m - 1:
            bx_last[0] = mob
            bx_last[1] = lab


def _second_kernel(pore_ref, lab_ref, fa_ref, fac_ref, gy_lo, gy_hi, gz_lo, gz_hi,
                   hy_lo, hy_hi, hz_lo, hz_hi, loc_ref, vals_ref):
    m = pore_ref.shape[0]
    srcs = ([], [])
    for i in range(m):
        mob, lab, mob_n, fc = _geo_row(i, pore_ref, lab_ref, gy_lo, gy_hi, gz_lo, gz_hi)
        w = 0.5 * (1.0 + mob)
        f1 = fa_ref[0, i]
        f_n = _neighbours(f1, _yrow(hy_lo, 0, i), _yrow(hy_hi, 0, i), _zcol(hz_lo, 0, i), _zcol(hz_hi, 0, i))
        u_n = [0.5 * (1.0 + mn) * fn for mn, fn in zip(mob_n, f_n)]
        srcs[0].append(f1 + cross_rate * (1.0 * _flux(w * f1, u_n, fc)))
        a1 = fa_ref[1, i]
        a_n = _neighbours(a1, _yrow(hy_lo, 1, i), _yrow(hy_hi, 1, i), _zcol(hz_lo, 1, i), _zcol(hz_hi, 1, i))
        srcs[1].append(a1 + cross_rate * (w * _flux(a1, a_n, fc)))
    zero = jnp.zeros(pore_ref.shape[1:], F32)
    for c in range(2):
        lower = [fac_ref[c, 0, r] for r in range(m)]
        ratios = [fac_ref[c, 1, r] for r in range(m - 1)]
        pivots = [fac_ref[c, 2, r] for r in range(m - 1)]
        src = srcs[c]
        local = _sweep(m, lower, pivots, ratios, src[: m - 1] + [None])
        for r in range(m):
            loc_ref[c, r] = local[r] if r < m - 1 else zero
        vals_ref[c, 0] = src[m - 1] - lower[m - 1] * local[m - 2]
        vals_ref[c, 1] = local[0]


def _gradient_kernel(pore_ref, lab_ref, a2_ref, gy_lo, gy_hi, gz_lo, gz_hi,
                     hy_lo, hy_hi, hz_lo, hz_hi, out_ref):
    m = pore_ref.shape[0]
    for i in range(m):
        mob, lab, mob_n, fc = _geo_row(i, pore_ref, lab_ref, gy_lo, gy_hi, gz_lo, gz_hi)
        w = 0.5 * (1.0 + mob)
        a2 = a2_ref[i]
        a_n = _neighbours(a2, _yrow(hy_lo, 0, i), _yrow(hy_hi, 0, i), _zcol(hz_lo, 0, i), _zcol(hz_hi, 0, i))
        out_ref[i] = a2 + cross_rate * (w * _flux(a2, a_n, fc))


def _halo_pairs(axis, periodic):
    count = lax.axis_size(axis)
    forward = [(i, i + 1) for i in range(count - 1)]
    if periodic:
        forward.append((count - 1, 0))
    backward = [(t, s) for s, t in forward]
    return forward, backward


def _exchange(first, last, axis, periodic):
    forward, backward = _halo_pairs(axis, periodic)
    lo = lax.ppermute(last, axis, forward)
    hi = lax.ppermute(first, axis, backward)
    return lo, hi


def _edge_shapes(chans, m, ny, nz):
    return (
        jax.ShapeDtypeStruct((chans, m, nz), F32),
        jax.ShapeDtypeStruct((chans, m, nz), F32),
        jax.ShapeDtypeStruct((chans, ny, m), F32),
        jax.ShapeDtypeStruct((chans, ny, m), F32),
    )


def _yz_halos(y_first, y_last, z_first, z_last):
    gy_lo, gy_hi = _exchange(y_first, y_last, "gy", False)
    gz_lo, gz_hi = _exchange(z_first, z_last, "gz", False)
    return gy_lo, gy_hi, gz_lo, gz_hi


def shards(vacancy, grain_label, pore_mask, cotangent):
    m, ny, nz = vacancy.shape
    n_blk = lax.axis_size("blk")
    cycle_step = float((m * n_blk) ** 2 // 64)
    shape = jax.ShapeDtypeStruct((m, ny, nz), F32)

    outs = pl.pallas_call(
        _edge_kernel,
        out_shape=_edge_shapes(3, m, ny, nz) + (jax.ShapeDtypeStruct((2, ny, nz), F32),) * 2,
        in_specs=[_vmem()] * 3,
        out_specs=tuple(_vmem() for _ in range(6)),
    )(vacancy, pore_mask, grain_label)
    bx_lo, bx_hi = _exchange(outs[4], outs[5], "blk", True)
    gy_lo, gy_hi, gz_lo, gz_hi = _yz_halos(*outs[:4])

    fac, loc, rows = pl.pallas_call(
        lambda *r: _prep_kernel(cycle_step, *r),
        out_shape=(
            jax.ShapeDtypeStruct((2, 5, m, ny, nz), F32),
            jax.ShapeDtypeStruct((2, m, ny, nz), F32),
            jax.ShapeDtypeStruct((2, 7, ny, nz), F32),
        ),
        in_specs=[_vmem()] * 10,
        out_specs=(_vmem(), _vmem(), _vmem()),
    )(vacancy, pore_mask, grain_label, cotangent, bx_lo, bx_hi, gy_lo, gy_hi, gz_lo, gz_hi)

    gathered = lax.all_gather(rows, "blk", axis=0, tiled=False)
    pos = jnp.reshape(lax.axis_index("blk"), (1,)).astype(jnp.int32)

    outs = pl.pallas_call(
        lambda *r: _combine_kernel(5, True, {0: 0, 1: 1}, *r),
        out_shape=(jax.ShapeDtypeStruct((2, m, ny, nz), F32),) + _edge_shapes(2, m, ny, nz),
        in_specs=[_smem()] + [_vmem()] * 4,
        out_specs=tuple(_vmem() for _ in range(5)),
        scratch_shapes=[pltpu.VMEM((n_blk, ny, nz), F32)],
    )(pos, gathered, gathered, fac, loc)
    fa = outs[0]

    hy_lo, hy_hi, hz_lo, hz_hi = _yz_halos(*outs[1:])
    loc2, vals2 = pl.pallas_call(
        _second_kernel,
        out_shape=(
            jax.ShapeDtypeStruct((2, m, ny, nz), F32),
            jax.ShapeDtypeStruct((2, 2, ny, nz), F32),
        ),
        in_specs=[_vmem()] * 12,
        out_specs=(_vmem(), _vmem()),
    )(pore_mask, grain_label, fa, fac, gy_lo, gy_hi, gz_lo, gz_hi, hy_lo, hy_hi, hz_lo, hz_hi)

    gathered2 = lax.all_gather(vals2, "blk", axis=0, tiled=False)
    outs = pl.pallas_call(
        lambda *r: _combine_kernel(0, False, {1: 0}, *r),
        out_shape=(shape, shape) + _edge_shapes(1, m, ny, nz),
        in_specs=[_smem()] + [_vmem()] * 4,
        out_specs=tuple(_vmem() for _ in range(6)),
        scratch_shapes=[pltpu.VMEM((n_blk, ny, nz), F32)],
    )(pos, gathered, gathered2, fac, loc2)
    final_field, adjoint_two = outs[:2]

    a2_lo, a2_hi, a2z_lo, a2z_hi = _yz_halos(*outs[2:])
    gradient = pl.pallas_call(
        _gradient_kernel,
        out_shape=shape,
        in_specs=[_vmem()] * 11,
        out_specs=_vmem(),
    )(pore_mask, grain_label, adjoint_two, gy_lo, gy_hi, gz_lo, gz_hi, a2_lo, a2_hi, a2z_lo, a2z_hi)
    return (final_field, gradient)


def solution(mesh):
    in_specs = (
        P("blk", "gy", "gz"),
        P("blk", "gy", "gz"),
        P("blk", "gy", "gz"),
        P("blk", "gy", "gz"),
    )
    out_specs = (P("blk", "gy", "gz"), P("blk", "gy", "gz"))
    return jax.shard_map(shards, mesh=mesh, in_specs=in_specs, out_specs=out_specs, check_vma=False)
```

```python
import jax
import jax.numpy as jnp
from jax import lax
from jax.experimental import pallas as pl
from jax.experimental.pallas import tpu as pltpu
from jax.sharding import PartitionSpec as P


cross_rate = 0.0125
boundary_gain = 3.0
F32 = jnp.float32


def face_value(mobility_here, mobility_there, label_here, label_there):
    harmonic = 2.0 * mobility_here * mobility_there / (mobility_here + mobility_there)
    return harmonic * jnp.where(label_here != label_there, boundary_gain, 1.0)


def _vmem():
    return pl.BlockSpec(memory_space=pltpu.VMEM)


def _smem():
    return pl.BlockSpec(memory_space=pltpu.SMEM)


def _shift(x, edge, axis, up):
    n = x.shape[axis]
    idx = lax.broadcasted_iota(jnp.int32, x.shape, axis)
    edge = jnp.broadcast_to(edge, x.shape)
    if up:
        return jnp.where(idx == n - 1, edge, pltpu.roll(x, n - 1, axis))
    return jnp.where(idx == 0, edge, pltpu.roll(x, 1, axis))


def _neighbours(x, ylo, yhi, zlo, zhi):
    return (
        _shift(x, yhi, 0, True),
        _shift(x, ylo, 0, False),
        _shift(x, zhi, 1, True),
        _shift(x, zlo, 1, False),
    )


def _faces(mob, lab, mob_n, lab_n):
    ups = (True, False, True, False)
    out = []
    for up, mn, ln in zip(ups, mob_n, lab_n):
        if up:
            out.append(face_value(mob, mn, lab, ln))
        else:
            out.append(face_value(mn, mob, ln, lab))
    return out


def _flux(u, u_n, faces):
    total = faces[0] * (u_n[0] - u)
    total = total + faces[1] * (u_n[1] - u)
    total = total + faces[2] * (u_n[2] - u)
    total = total + faces[3] * (u_n[3] - u)
    return total


def _yrow(ref, c, i):
    return ref[c, pl.ds(i, 1), :]


def _zcol(ref, c, i):
    return ref[c, :, pl.ds(i, 1)]


def _write_edges(edges, c, r, val):
    y_first, y_last, z_first, z_last = edges
    ny, nz = val.shape
    y_first[c, pl.ds(r, 1), :] = val[0:1, :]
    y_last[c, pl.ds(r, 1), :] = val[ny - 1 : ny, :]
    z_first[c, :, pl.ds(r, 1)] = val[:, 0:1]
    z_last[c, :, pl.ds(r, 1)] = val[:, nz - 1 : nz]


def _geo_row(i, pore_ref, lab_ref, gy_lo, gy_hi, gz_lo, gz_hi):
    mob = 1.0 + 2.0 * pore_ref[i].astype(F32)
    lab = lab_ref[i].astype(F32)
    mob_n = _neighbours(mob, _yrow(gy_lo, 0, i), _yrow(gy_hi, 0, i), _zcol(gz_lo, 0, i), _zcol(gz_hi, 0, i))
    lab_n = _neighbours(lab, _yrow(gy_lo, 1, i), _yrow(gy_hi, 1, i), _zcol(gz_lo, 1, i), _zcol(gz_hi, 1, i))
    return mob, lab, mob_n, _faces(mob, lab, mob_n, lab_n)


def _sweep(m, lower, pivots, ratios, source):
    ys = [None] * m
    prev = None
    for r in range(m - 1):
        num = source[r]
        if num is None:
            if prev is None:
                continue
            num = -(lower[r] * prev)
        elif prev is not None:
            num = num - lower[r] * prev
        ys[r] = num / pivots[r]
        prev = ys[r]
    xs = [None] * m
    prev = None
    for r in range(m - 2, -1, -1):
        if prev is None:
            xs[r] = ys[r]
        elif ys[r] is None:
            xs[r] = -(ratios[r] * prev)
        else:
            xs[r] = ys[r] - ratios[r] * prev
        prev = xs[r]
    return xs


def _factor_kernel(cs, pore_ref, lab_ref, bx_lo, bx_hi, fac_ref, lr_ref, rows_ref):
    m = pore_ref.shape[0]
    zero = jnp.zeros(pore_ref.shape[1:], F32)
    mobs = [1.0 + 2.0 * pore_ref[r].astype(F32) for r in range(m)]
    labs = [lab_ref[r].astype(F32) for r in range(m)]
    m_ext = [bx_lo[0]] + mobs + [bx_hi[0]]
    l_ext = [bx_lo[1]] + labs + [bx_hi[1]]
    w_ext = [0.5 * (1.0 + x) for x in m_ext]
    faces = [face_value(m_ext[k], m_ext[k + 1], l_ext[k], l_ext[k + 1]) for k in range(m + 1)]
    bands = {"f": ([], [], []), "a": ([], [], [])}
    for r in range(m):
        bf, ff = faces[r], faces[r + 1]
        w = w_ext[r + 1]
        main = 1.0 + cs * w * (bf + ff)
        bands["f"][0].append(-cs * bf * w_ext[r])
        bands["f"][1].append(main)
        bands["f"][2].append(-cs * ff * w_ext[r + 2])
        bands["a"][0].append(-cs * bf * w)
        bands["a"][1].append(main)
        bands["a"][2].append(-cs * ff * w)

    for c, key in ((0, "f"), (1, "a")):
        lower, main, upper = bands[key]
        pivots, ratios = [], []
        prev = None
        for r in range(m - 1):
            piv = main[r] if prev is None else main[r] - lower[r] * prev
            rat = upper[r] / piv
            pivots.append(piv)
            ratios.append(rat)
            prev = rat
        left_src = [lower[0]] + [None] * (m - 1)
        right_src = [None] * (m - 2) + [upper[m - 2], None]
        left = _sweep(m, lower, pivots, ratios, left_src)
        right = _sweep(m, lower, pivots, ratios, right_src)
        for r in range(m):
            fac_ref[c, 0, r] = lower[r]
            fac_ref[c, 1, r] = ratios[r] if r < m - 1 else zero
            fac_ref[c, 2, r] = pivots[r] if r < m - 1 else zero + 1.0
            lr_ref[c, 0, r] = left[r] if r < m - 1 else zero
            lr_ref[c, 1, r] = right[r] if r < m - 1 else zero - 1.0
        last_lower = lower[m - 1]
        rows_ref[c, 0] = last_lower * left[m - 2]
        rows_ref[c, 1] = main[m - 1] - last_lower * right[m - 2]
        rows_ref[c, 2] = upper[m - 1]
        rows_ref[c, 3] = left[0]
        rows_ref[c, 4] = right[0]


def _reduced_solve(gs, gv, voff, c, n, pos):
    slot = [(pos - p + n) % n for p in range(n)]
    g = [[gs[slot[p], c, k] for k in range(5)] for p in range(n)]
    v = [[gv[slot[p], c, voff + k] for k in range(2)] for p in range(n)]
    lower = [-g[p][0] for p in range(n)]
    main = [g[p][1] - g[p][2] * g[(p + 1) % n][3] for p in range(n)]
    upper = [-g[p][2] * g[(p + 1) % n][4] for p in range(n)]
    src = [v[p][0] - g[p][2] * v[(p + 1) % n][1] for p in range(n)]
    k_in = n - 1
    pivots, ratios = [], []
    prev = None
    for r in range(k_in):
        piv = main[r] if prev is None else main[r] - lower[r] * prev
        rat = upper[r] / piv
        pivots.append(piv)
        ratios.append(rat)
        prev = rat

    def apply(source):
        ys = []
        prev = None
        for r in range(k_in):
            num = source[r] if prev is None else source[r] - lower[r] * prev
            ys.append(num / pivots[r])
            prev = ys[-1]
        xs = [None] * k_in
        prev = None
        for r in range(k_in - 1, -1, -1):
            xs[r] = ys[r] if prev is None else ys[r] - ratios[r] * prev
            prev = xs[r]
        return xs

    coupling = []
    for r in range(k_in):
        term = None
        if r == 0:
            term = lower[0]
        if r == k_in - 1:
            term = upper[k_in - 1] if term is None else term + upper[k_in - 1]
        coupling.append(term if term is not None else jnp.zeros_like(lower[0]))
    linked = apply(coupling)
    closing = main[k_in] - lower[k_in] * linked[k_in - 1] - upper[k_in] * linked[0]
    inner = apply(src[:k_in])
    sep = (src[k_in] - lower[k_in] * inner[k_in - 1] - upper[k_in] * inner[0]) / closing
    return [inner[r] - linked[r] * sep for r in range(k_in)] + [sep]


def _combine_kernel(voff, stacked, edge_of, pos_ref, gs_ref, gv_ref, lr_ref, loc_ref, *refs):
    if stacked:
        out_ref = refs[0]
        outs = (out_ref.at[0], out_ref.at[1])
        rest = refs[1:]
    else:
        outs = refs[:2]
        rest = refs[2:]
    edges, sep_ref = rest[:4], rest[4]
    n = gs_ref.shape[0]
    m = loc_ref.shape[1]
    p = pos_ref[0]
    for c in range(2):
        seps = _reduced_solve(gs_ref, gv_ref, voff, c, n, p)
        for q in range(n):
            sep_ref[q] = seps[q]
        own = sep_ref[p]
        prior = sep_ref[(p + n - 1) % n]
        for r in range(m):
            val = loc_ref[c, r] - lr_ref[c, 0, r] * prior - lr_ref[c, 1, r] * own
            outs[c][r] = val
            if c in edge_of:
                _write_edges(edges, edge_of[c], r, val)


def _edge_kernel(vac_ref, pore_ref, lab_ref, y_first, y_last, z_first, z_last, bx_first, bx_last):
    m = vac_ref.shape[0]
    edges = (y_first, y_last, z_first, z_last)
    for r in range(m):
        mob = 1.0 + 2.0 * pore_ref[r].astype(F32)
        lab = lab_ref[r].astype(F32)
        for c, val in enumerate((mob, lab, vac_ref[r])):
            _write_edges(edges, c, r, val)
        if r == 0:
            bx_first[0] = mob
            bx_first[1] = lab
        if r == m - 1:
            bx_last[0] = mob
            bx_last[1] = lab


def _local_solves(fac_ref, srcs, loc_ref, vals_ref):
    m = loc_ref.shape[1]
    zero = jnp.zeros(loc_ref.shape[2:], F32)
    for c in range(2):
        lower = [fac_ref[c, 0, r] for r in range(m)]
        ratios = [fac_ref[c, 1, r] for r in range(m - 1)]
        pivots = [fac_ref[c, 2, r] for r in range(m - 1)]
        src = srcs[c]
        local = _sweep(m, lower, pivots, ratios, src[: m - 1] + [None])
        for r in range(m):
            loc_ref[c, r] = local[r] if r < m - 1 else zero
        vals_ref[c, 0] = src[m - 1] - lower[m - 1] * local[m - 2]
        vals_ref[c, 1] = local[0]


def _first_kernel(vac_ref, cot_ref, pore_ref, lab_ref, fac_ref, gy_lo, gy_hi, gz_lo, gz_hi, loc_ref, vals_ref):
    m = pore_ref.shape[0]
    srcs = ([], [cot_ref[r] for r in range(m)])
    for i in range(m):
        mob, _, mob_n, fc = _geo_row(i, pore_ref, lab_ref, gy_lo, gy_hi, gz_lo, gz_hi)
        w = 0.5 * (1.0 + mob)
        v = vac_ref[i]
        v_n = _neighbours(v, _yrow(gy_lo, 2, i), _yrow(gy_hi, 2, i), _zcol(gz_lo, 2, i), _zcol(gz_hi, 2, i))
        u_n = [0.5 * (1.0 + mn) * vn for mn, vn in zip(mob_n, v_n)]
        srcs[0].append(v + cross_rate * (1.0 * _flux(w * v, u_n, fc)))
    _local_solves(fac_ref, srcs, loc_ref, vals_ref)


def _second_kernel(pore_ref, lab_ref, fa_ref, fac_ref, gy_lo, gy_hi, gz_lo, gz_hi,
                   hy_lo, hy_hi, hz_lo, hz_hi, loc_ref, vals_ref):
    m = pore_ref.shape[0]
    srcs = ([], [])
    for i in range(m):
        mob, _, mob_n, fc = _geo_row(i, pore_ref, lab_ref, gy_lo, gy_hi, gz_lo, gz_hi)
        w = 0.5 * (1.0 + mob)
        f1 = fa_ref[0, i]
        f_n = _neighbours(f1, _yrow(hy_lo, 0, i), _yrow(hy_hi, 0, i), _zcol(hz_lo, 0, i), _zcol(hz_hi, 0, i))
        u_n = [0.5 * (1.0 + mn) * fn for mn, fn in zip(mob_n, f_n)]
        srcs[0].append(f1 + cross_rate * (1.0 * _flux(w * f1, u_n, fc)))
        a1 = fa_ref[1, i]
        a_n = _neighbours(a1, _yrow(hy_lo, 1, i), _yrow(hy_hi, 1, i), _zcol(hz_lo, 1, i), _zcol(hz_hi, 1, i))
        srcs[1].append(a1 + cross_rate * (w * _flux(a1, a_n, fc)))
    _local_solves(fac_ref, srcs, loc_ref, vals_ref)


def _gradient_kernel(pore_ref, lab_ref, a2_ref, gy_lo, gy_hi, gz_lo, gz_hi,
                     hy_lo, hy_hi, hz_lo, hz_hi, out_ref):
    m = pore_ref.shape[0]
    for i in range(m):
        mob, _, _, fc = _geo_row(i, pore_ref, lab_ref, gy_lo, gy_hi, gz_lo, gz_hi)
        w = 0.5 * (1.0 + mob)
        a2 = a2_ref[i]
        a_n = _neighbours(a2, _yrow(hy_lo, 0, i), _yrow(hy_hi, 0, i), _zcol(hz_lo, 0, i), _zcol(hz_hi, 0, i))
        out_ref[i] = a2 + cross_rate * (w * _flux(a2, a_n, fc))


def _halo_pairs(axis, periodic):
    count = lax.axis_size(axis)
    forward = [(i, i + 1) for i in range(count - 1)]
    if periodic:
        forward.append((count - 1, 0))
    backward = [(t, s) for s, t in forward]
    return forward, backward


def _exchange(first, last, axis, periodic):
    forward, backward = _halo_pairs(axis, periodic)
    lo = lax.ppermute(last, axis, forward)
    hi = lax.ppermute(first, axis, backward)
    return lo, hi


def _first_call(m, ny, nz):
    return pl.pallas_call(
        _first_kernel,
        out_shape=(
            jax.ShapeDtypeStruct((2, m, ny, nz), F32),
            jax.ShapeDtypeStruct((2, 2, ny, nz), F32),
        ),
        in_specs=[_vmem()] * 9,
        out_specs=(_vmem(), _vmem()),
    )


def _gather_blk(x):
    n = lax.axis_size("blk")
    parts = [x]
    for k in range(1, n):
        parts.append(lax.ppermute(x, "blk", [(j, (j + k) % n) for j in range(n)]))
    return jnp.stack(parts)


def _edge_shapes(chans, m, ny, nz):
    return (
        jax.ShapeDtypeStruct((chans, m, nz), F32),
        jax.ShapeDtypeStruct((chans, m, nz), F32),
        jax.ShapeDtypeStruct((chans, ny, m), F32),
        jax.ShapeDtypeStruct((chans, ny, m), F32),
    )


def _yz_halos(y_first, y_last, z_first, z_last):
    gy_lo, gy_hi = _exchange(y_first, y_last, "gy", False)
    gz_lo, gz_hi = _exchange(z_first, z_last, "gz", False)
    return gy_lo, gy_hi, gz_lo, gz_hi


def _shards(vacancy, grain_label, pore_mask, cotangent):
    m, ny, nz = vacancy.shape
    n_blk = lax.axis_size("blk")
    cycle_step = float((m * n_blk) ** 2 // 64)
    shape = jax.ShapeDtypeStruct((m, ny, nz), F32)

    outs = pl.pallas_call(
        _edge_kernel,
        out_shape=_edge_shapes(3, m, ny, nz) + (jax.ShapeDtypeStruct((2, ny, nz), F32),) * 2,
        in_specs=[_vmem()] * 3,
        out_specs=tuple(_vmem() for _ in range(6)),
    )(vacancy, pore_mask, grain_label)
    bx_lo, bx_hi = _exchange(outs[4], outs[5], "blk", True)
    gy_lo, gy_hi, gz_lo, gz_hi = _yz_halos(*outs[:4])

    fac, lr, rows = pl.pallas_call(
        lambda *r: _factor_kernel(cycle_step, *r),
        out_shape=(
            jax.ShapeDtypeStruct((2, 3, m, ny, nz), F32),
            jax.ShapeDtypeStruct((2, 2, m, ny, nz), F32),
            jax.ShapeDtypeStruct((2, 5, ny, nz), F32),
        ),
        in_specs=[_vmem()] * 4,
        out_specs=(_vmem(), _vmem(), _vmem()),
    )(pore_mask, grain_label, bx_lo, bx_hi)
    gathered = _gather_blk(rows)

    loc, vals = _first_call(m, ny, nz)(
        vacancy, cotangent, pore_mask, grain_label, fac, gy_lo, gy_hi, gz_lo, gz_hi
    )
    gathered1 = _gather_blk(vals)
    pos = jnp.reshape(lax.axis_index("blk"), (1,)).astype(jnp.int32)

    outs = pl.pallas_call(
        lambda *r: _combine_kernel(0, True, {0: 0, 1: 1}, *r),
        out_shape=(jax.ShapeDtypeStruct((2, m, ny, nz), F32),) + _edge_shapes(2, m, ny, nz),
        in_specs=[_smem()] + [_vmem()] * 4,
        out_specs=tuple(_vmem() for _ in range(5)),
        scratch_shapes=[pltpu.VMEM((n_blk, ny, nz), F32)],
    )(pos, gathered, gathered1, lr, loc)
    fa = outs[0]

    hy_lo, hy_hi, hz_lo, hz_hi = _yz_halos(*outs[1:])
    loc2, vals2 = pl.pallas_call(
        _second_kernel,
        out_shape=(
            jax.ShapeDtypeStruct((2, m, ny, nz), F32),
            jax.ShapeDtypeStruct((2, 2, ny, nz), F32),
        ),
        in_specs=[_vmem()] * 12,
        out_specs=(_vmem(), _vmem()),
    )(pore_mask, grain_label, fa, fac, gy_lo, gy_hi, gz_lo, gz_hi, hy_lo, hy_hi, hz_lo, hz_hi)

    gathered2 = _gather_blk(vals2)
    outs = pl.pallas_call(
        lambda *r: _combine_kernel(0, False, {1: 0}, *r),
        out_shape=(shape, shape) + _edge_shapes(1, m, ny, nz),
        in_specs=[_smem()] + [_vmem()] * 4,
        out_specs=tuple(_vmem() for _ in range(6)),
        scratch_shapes=[pltpu.VMEM((n_blk, ny, nz), F32)],
    )(pos, gathered, gathered2, lr, loc2)
    final_field, adjoint_two = outs[:2]

    a2_lo, a2_hi, a2z_lo, a2z_hi = _yz_halos(*outs[2:])
    gradient = pl.pallas_call(
        _gradient_kernel,
        out_shape=shape,
        in_specs=[_vmem()] * 11,
        out_specs=_vmem(),
    )(pore_mask, grain_label, adjoint_two, gy_lo, gy_hi, gz_lo, gz_hi, a2_lo, a2_hi, a2z_lo, a2z_hi)
    return (final_field, gradient)


def solution(mesh):
    in_specs = (
        P("blk", "gy", "gz"),
        P("blk", "gy", "gz"),
        P("blk", "gy", "gz"),
        P("blk", "gy", "gz"),
    )
    out_specs = (P("blk", "gy", "gz"), P("blk", "gy", "gz"))
    return jax.shard_map(_shards, mesh=mesh, in_specs=in_specs, out_specs=out_specs, check_vma=False)
```

```python
import jax
import jax.numpy as jnp
from jax import lax
from jax.experimental import pallas as pl
from jax.experimental.pallas import tpu as pltpu
from jax.sharding import PartitionSpec as P


cross_rate = 0.0125
boundary_gain = 3.0
F32 = jnp.float32


def face_value(mobility_here, mobility_there, label_here, label_there):
    harmonic = 2.0 * mobility_here * mobility_there / (mobility_here + mobility_there)
    return harmonic * jnp.where(label_here != label_there, boundary_gain, 1.0)


def _vmem():
    return pl.BlockSpec(memory_space=pltpu.VMEM)


def _smem():
    return pl.BlockSpec(memory_space=pltpu.SMEM)


def _shift(x, edge, axis, up):
    n = x.shape[axis]
    idx = lax.broadcasted_iota(jnp.int32, x.shape, axis)
    edge = jnp.broadcast_to(edge, x.shape)
    if up:
        return jnp.where(idx == n - 1, edge, pltpu.roll(x, n - 1, axis))
    return jnp.where(idx == 0, edge, pltpu.roll(x, 1, axis))


def _neighbours(x, ylo, yhi, zlo, zhi):
    return (
        _shift(x, yhi, 0, True),
        _shift(x, ylo, 0, False),
        _shift(x, zhi, 1, True),
        _shift(x, zlo, 1, False),
    )


def _faces(mob, lab, mob_n, lab_n):
    ups = (True, False, True, False)
    out = []
    for up, mn, ln in zip(ups, mob_n, lab_n):
        if up:
            out.append(face_value(mob, mn, lab, ln))
        else:
            out.append(face_value(mn, mob, ln, lab))
    return out


def _flux(u, u_n, faces):
    total = faces[0] * (u_n[0] - u)
    total = total + faces[1] * (u_n[1] - u)
    total = total + faces[2] * (u_n[2] - u)
    total = total + faces[3] * (u_n[3] - u)
    return total


def _yrow(ref, c, i):
    return ref[c, pl.ds(i, 1), :]


def _zcol(ref, c, i):
    return ref[c, :, pl.ds(i, 1)]


def _write_edges(edges, c, r, val):
    y_first, y_last, z_first, z_last = edges
    ny, nz = val.shape
    y_first[c, pl.ds(r, 1), :] = val[0:1, :]
    y_last[c, pl.ds(r, 1), :] = val[ny - 1 : ny, :]
    z_first[c, :, pl.ds(r, 1)] = val[:, 0:1]
    z_last[c, :, pl.ds(r, 1)] = val[:, nz - 1 : nz]


def _geo_row(i, pore_ref, lab_ref, gy_lo, gy_hi, gz_lo, gz_hi):
    mob = 1.0 + 2.0 * pore_ref[i].astype(F32)
    lab = lab_ref[i].astype(F32)
    mob_n = _neighbours(mob, _yrow(gy_lo, 0, i), _yrow(gy_hi, 0, i), _zcol(gz_lo, 0, i), _zcol(gz_hi, 0, i))
    lab_n = _neighbours(lab, _yrow(gy_lo, 1, i), _yrow(gy_hi, 1, i), _zcol(gz_lo, 1, i), _zcol(gz_hi, 1, i))
    return mob, lab, mob_n, _faces(mob, lab, mob_n, lab_n)


def _sweep(m, lower, pivots, ratios, source):
    ys = [None] * m
    prev = None
    for r in range(m - 1):
        num = source[r]
        if num is None:
            if prev is None:
                continue
            num = -(lower[r] * prev)
        elif prev is not None:
            num = num - lower[r] * prev
        ys[r] = num / pivots[r]
        prev = ys[r]
    xs = [None] * m
    prev = None
    for r in range(m - 2, -1, -1):
        if prev is None:
            xs[r] = ys[r]
        elif ys[r] is None:
            xs[r] = -(ratios[r] * prev)
        else:
            xs[r] = ys[r] - ratios[r] * prev
        prev = xs[r]
    return xs


def _factor_kernel(cs, pore_ref, lab_ref, bx_lo, bx_hi, fac_ref, lr_ref, rows_ref):
    m = pore_ref.shape[0]
    zero = jnp.zeros(pore_ref.shape[1:], F32)
    mobs = [1.0 + 2.0 * pore_ref[r].astype(F32) for r in range(m)]
    labs = [lab_ref[r].astype(F32) for r in range(m)]
    m_ext = [bx_lo[0]] + mobs + [bx_hi[0]]
    l_ext = [bx_lo[1]] + labs + [bx_hi[1]]
    w_ext = [0.5 * (1.0 + x) for x in m_ext]
    faces = [face_value(m_ext[k], m_ext[k + 1], l_ext[k], l_ext[k + 1]) for k in range(m + 1)]
    bands = {"f": ([], [], []), "a": ([], [], [])}
    for r in range(m):
        bf, ff = faces[r], faces[r + 1]
        w = w_ext[r + 1]
        main = 1.0 + cs * w * (bf + ff)
        bands["f"][0].append(-cs * bf * w_ext[r])
        bands["f"][1].append(main)
        bands["f"][2].append(-cs * ff * w_ext[r + 2])
        bands["a"][0].append(-cs * bf * w)
        bands["a"][1].append(main)
        bands["a"][2].append(-cs * ff * w)

    for c, key in ((0, "f"), (1, "a")):
        lower, main, upper = bands[key]
        pivots, ratios = [], []
        prev = None
        for r in range(m - 1):
            piv = main[r] if prev is None else main[r] - lower[r] * prev
            rat = upper[r] / piv
            pivots.append(piv)
            ratios.append(rat)
            prev = rat
        left_src = [lower[0]] + [None] * (m - 1)
        right_src = [None] * (m - 2) + [upper[m - 2], None]
        left = _sweep(m, lower, pivots, ratios, left_src)
        right = _sweep(m, lower, pivots, ratios, right_src)
        for r in range(m):
            fac_ref[c, 0, r] = lower[r]
            fac_ref[c, 1, r] = ratios[r] if r < m - 1 else zero
            fac_ref[c, 2, r] = pivots[r] if r < m - 1 else zero + 1.0
            lr_ref[c, 0, r] = left[r] if r < m - 1 else zero
            lr_ref[c, 1, r] = right[r] if r < m - 1 else zero - 1.0
        last_lower = lower[m - 1]
        rows_ref[c, 0] = last_lower * left[m - 2]
        rows_ref[c, 1] = main[m - 1] - last_lower * right[m - 2]
        rows_ref[c, 2] = upper[m - 1]
        rows_ref[c, 3] = left[0]
        rows_ref[c, 4] = right[0]


def _reduced_solve(gs, gv, voff, c, n, pos):
    slot = [(pos - p + n) % n for p in range(n)]
    g = [[gs[slot[p], c, k] for k in range(5)] for p in range(n)]
    v = [[gv[slot[p], c, voff + k] for k in range(2)] for p in range(n)]
    lower = [-g[p][0] for p in range(n)]
    main = [g[p][1] - g[p][2] * g[(p + 1) % n][3] for p in range(n)]
    upper = [-g[p][2] * g[(p + 1) % n][4] for p in range(n)]
    src = [v[p][0] - g[p][2] * v[(p + 1) % n][1] for p in range(n)]
    k_in = n - 1
    pivots, ratios = [], []
    prev = None
    for r in range(k_in):
        piv = main[r] if prev is None else main[r] - lower[r] * prev
        rat = upper[r] / piv
        pivots.append(piv)
        ratios.append(rat)
        prev = rat

    def apply(source):
        ys = []
        prev = None
        for r in range(k_in):
            num = source[r] if prev is None else source[r] - lower[r] * prev
            ys.append(num / pivots[r])
            prev = ys[-1]
        xs = [None] * k_in
        prev = None
        for r in range(k_in - 1, -1, -1):
            xs[r] = ys[r] if prev is None else ys[r] - ratios[r] * prev
            prev = xs[r]
        return xs

    coupling = []
    for r in range(k_in):
        term = None
        if r == 0:
            term = lower[0]
        if r == k_in - 1:
            term = upper[k_in - 1] if term is None else term + upper[k_in - 1]
        coupling.append(term if term is not None else jnp.zeros_like(lower[0]))
    linked = apply(coupling)
    closing = main[k_in] - lower[k_in] * linked[k_in - 1] - upper[k_in] * linked[0]
    inner = apply(src[:k_in])
    sep = (src[k_in] - lower[k_in] * inner[k_in - 1] - upper[k_in] * inner[0]) / closing
    return [inner[r] - linked[r] * sep for r in range(k_in)] + [sep]


def _combine_kernel(n, stacked, edge_of, pos_ref, *refs):
    gs_parts, gv_parts = refs[:n], refs[n : 2 * n]
    lr_ref, loc_ref = refs[2 * n], refs[2 * n + 1]
    refs = refs[2 * n + 2 :]
    if stacked:
        out_ref = refs[0]
        outs = (out_ref.at[0], out_ref.at[1])
        rest = refs[1:]
    else:
        outs = refs[:2]
        rest = refs[2:]
    edges, sep_ref, gs_ref, gv_ref = rest[:4], rest[4], rest[5], rest[6]
    for k in range(n):
        gs_ref[k] = gs_parts[k][...]
        gv_ref[k] = gv_parts[k][...]
    m = loc_ref.shape[1]
    p = pos_ref[0]
    for c in range(2):
        seps = _reduced_solve(gs_ref, gv_ref, 0, c, n, p)
        for q in range(n):
            sep_ref[q] = seps[q]
        own = sep_ref[p]
        prior = sep_ref[(p + n - 1) % n]
        for r in range(m):
            val = loc_ref[c, r] - lr_ref[c, 0, r] * prior - lr_ref[c, 1, r] * own
            outs[c][r] = val
            if c in edge_of:
                _write_edges(edges, edge_of[c], r, val)


def _edge_kernel(vac_ref, pore_ref, lab_ref, y_first, y_last, z_first, z_last, bx_first, bx_last):
    m = vac_ref.shape[0]
    edges = (y_first, y_last, z_first, z_last)
    for r in range(m):
        mob = 1.0 + 2.0 * pore_ref[r].astype(F32)
        lab = lab_ref[r].astype(F32)
        for c, val in enumerate((mob, lab, vac_ref[r])):
            _write_edges(edges, c, r, val)
        if r == 0:
            bx_first[0] = mob
            bx_first[1] = lab
        if r == m - 1:
            bx_last[0] = mob
            bx_last[1] = lab


def _local_solves(fac_ref, srcs, loc_ref, vals_ref):
    m = loc_ref.shape[1]
    zero = jnp.zeros(loc_ref.shape[2:], F32)
    for c in range(2):
        lower = [fac_ref[c, 0, r] for r in range(m)]
        ratios = [fac_ref[c, 1, r] for r in range(m - 1)]
        pivots = [fac_ref[c, 2, r] for r in range(m - 1)]
        src = srcs[c]
        local = _sweep(m, lower, pivots, ratios, src[: m - 1] + [None])
        for r in range(m):
            loc_ref[c, r] = local[r] if r < m - 1 else zero
        vals_ref[c, 0] = src[m - 1] - lower[m - 1] * local[m - 2]
        vals_ref[c, 1] = local[0]


def _first_kernel(vac_ref, cot_ref, pore_ref, lab_ref, fac_ref, gy_lo, gy_hi, gz_lo, gz_hi, loc_ref, vals_ref):
    m = pore_ref.shape[0]
    srcs = ([], [cot_ref[r] for r in range(m)])
    for i in range(m):
        mob, _, mob_n, fc = _geo_row(i, pore_ref, lab_ref, gy_lo, gy_hi, gz_lo, gz_hi)
        w = 0.5 * (1.0 + mob)
        v = vac_ref[i]
        v_n = _neighbours(v, _yrow(gy_lo, 2, i), _yrow(gy_hi, 2, i), _zcol(gz_lo, 2, i), _zcol(gz_hi, 2, i))
        u_n = [0.5 * (1.0 + mn) * vn for mn, vn in zip(mob_n, v_n)]
        srcs[0].append(v + cross_rate * (1.0 * _flux(w * v, u_n, fc)))
    _local_solves(fac_ref, srcs, loc_ref, vals_ref)


def _second_kernel(pore_ref, lab_ref, fa_ref, fac_ref, gy_lo, gy_hi, gz_lo, gz_hi,
                   hy_lo, hy_hi, hz_lo, hz_hi, loc_ref, vals_ref):
    m = pore_ref.shape[0]
    srcs = ([], [])
    for i in range(m):
        mob, _, mob_n, fc = _geo_row(i, pore_ref, lab_ref, gy_lo, gy_hi, gz_lo, gz_hi)
        w = 0.5 * (1.0 + mob)
        f1 = fa_ref[0, i]
        f_n = _neighbours(f1, _yrow(hy_lo, 0, i), _yrow(hy_hi, 0, i), _zcol(hz_lo, 0, i), _zcol(hz_hi, 0, i))
        u_n = [0.5 * (1.0 + mn) * fn for mn, fn in zip(mob_n, f_n)]
        srcs[0].append(f1 + cross_rate * (1.0 * _flux(w * f1, u_n, fc)))
        a1 = fa_ref[1, i]
        a_n = _neighbours(a1, _yrow(hy_lo, 1, i), _yrow(hy_hi, 1, i), _zcol(hz_lo, 1, i), _zcol(hz_hi, 1, i))
        srcs[1].append(a1 + cross_rate * (w * _flux(a1, a_n, fc)))
    _local_solves(fac_ref, srcs, loc_ref, vals_ref)


def _gradient_kernel(pore_ref, lab_ref, a2_ref, gy_lo, gy_hi, gz_lo, gz_hi,
                     hy_lo, hy_hi, hz_lo, hz_hi, out_ref):
    m = pore_ref.shape[0]
    for i in range(m):
        mob, _, _, fc = _geo_row(i, pore_ref, lab_ref, gy_lo, gy_hi, gz_lo, gz_hi)
        w = 0.5 * (1.0 + mob)
        a2 = a2_ref[i]
        a_n = _neighbours(a2, _yrow(hy_lo, 0, i), _yrow(hy_hi, 0, i), _zcol(hz_lo, 0, i), _zcol(hz_hi, 0, i))
        out_ref[i] = a2 + cross_rate * (w * _flux(a2, a_n, fc))


def _halo_pairs(axis, periodic):
    count = lax.axis_size(axis)
    forward = [(i, i + 1) for i in range(count - 1)]
    if periodic:
        forward.append((count - 1, 0))
    backward = [(t, s) for s, t in forward]
    return forward, backward


def _exchange(first, last, axis, periodic):
    forward, backward = _halo_pairs(axis, periodic)
    lo = lax.ppermute(last, axis, forward)
    hi = lax.ppermute(first, axis, backward)
    return lo, hi


def _first_call(m, ny, nz):
    return pl.pallas_call(
        _first_kernel,
        out_shape=(
            jax.ShapeDtypeStruct((2, m, ny, nz), F32),
            jax.ShapeDtypeStruct((2, 2, ny, nz), F32),
        ),
        in_specs=[_vmem()] * 9,
        out_specs=(_vmem(), _vmem()),
    )


def _combine_scratch(n, ny, nz):
    return [
        pltpu.VMEM((n, ny, nz), F32),
        pltpu.VMEM((n, 2, 5, ny, nz), F32),
        pltpu.VMEM((n, 2, 2, ny, nz), F32),
    ]


def _gather_blk(x):
    n = lax.axis_size("blk")
    parts = [x]
    for k in range(1, n):
        parts.append(lax.ppermute(x, "blk", [(j, (j + k) % n) for j in range(n)]))
    return parts


def _edge_shapes(chans, m, ny, nz):
    return (
        jax.ShapeDtypeStruct((chans, m, nz), F32),
        jax.ShapeDtypeStruct((chans, m, nz), F32),
        jax.ShapeDtypeStruct((chans, ny, m), F32),
        jax.ShapeDtypeStruct((chans, ny, m), F32),
    )


def _yz_halos(y_first, y_last, z_first, z_last):
    gy_lo, gy_hi = _exchange(y_first, y_last, "gy", False)
    gz_lo, gz_hi = _exchange(z_first, z_last, "gz", False)
    return gy_lo, gy_hi, gz_lo, gz_hi


def _shards(vacancy, grain_label, pore_mask, cotangent):
    m, ny, nz = vacancy.shape
    n_blk = lax.axis_size("blk")
    cycle_step = float((m * n_blk) ** 2 // 64)
    shape = jax.ShapeDtypeStruct((m, ny, nz), F32)

    outs = pl.pallas_call(
        _edge_kernel,
        out_shape=_edge_shapes(3, m, ny, nz) + (jax.ShapeDtypeStruct((2, ny, nz), F32),) * 2,
        in_specs=[_vmem()] * 3,
        out_specs=tuple(_vmem() for _ in range(6)),
    )(vacancy, pore_mask, grain_label)
    bx_lo, bx_hi = _exchange(outs[4], outs[5], "blk", True)
    gy_lo, gy_hi, gz_lo, gz_hi = _yz_halos(*outs[:4])

    fac, lr, rows = pl.pallas_call(
        lambda *r: _factor_kernel(cycle_step, *r),
        out_shape=(
            jax.ShapeDtypeStruct((2, 3, m, ny, nz), F32),
            jax.ShapeDtypeStruct((2, 2, m, ny, nz), F32),
            jax.ShapeDtypeStruct((2, 5, ny, nz), F32),
        ),
        in_specs=[_vmem()] * 4,
        out_specs=(_vmem(), _vmem(), _vmem()),
    )(pore_mask, grain_label, bx_lo, bx_hi)
    gathered = _gather_blk(rows)

    loc, vals = _first_call(m, ny, nz)(
        vacancy, cotangent, pore_mask, grain_label, fac, gy_lo, gy_hi, gz_lo, gz_hi
    )
    gathered1 = _gather_blk(vals)
    pos = jnp.reshape(lax.axis_index("blk"), (1,)).astype(jnp.int32)

    outs = pl.pallas_call(
        lambda *r: _combine_kernel(n_blk, True, {0: 0, 1: 1}, *r),
        out_shape=(jax.ShapeDtypeStruct((2, m, ny, nz), F32),) + _edge_shapes(2, m, ny, nz),
        in_specs=[_smem()] + [_vmem()] * (2 * n_blk + 2),
        out_specs=tuple(_vmem() for _ in range(5)),
        scratch_shapes=_combine_scratch(n_blk, ny, nz),
    )(pos, *gathered, *gathered1, lr, loc)
    fa = outs[0]

    hy_lo, hy_hi, hz_lo, hz_hi = _yz_halos(*outs[1:])
    loc2, vals2 = pl.pallas_call(
        _second_kernel,
        out_shape=(
            jax.ShapeDtypeStruct((2, m, ny, nz), F32),
            jax.ShapeDtypeStruct((2, 2, ny, nz), F32),
        ),
        in_specs=[_vmem()] * 12,
        out_specs=(_vmem(), _vmem()),
    )(pore_mask, grain_label, fa, fac, gy_lo, gy_hi, gz_lo, gz_hi, hy_lo, hy_hi, hz_lo, hz_hi)

    gathered2 = _gather_blk(vals2)
    outs = pl.pallas_call(
        lambda *r: _combine_kernel(n_blk, False, {1: 0}, *r),
        out_shape=(shape, shape) + _edge_shapes(1, m, ny, nz),
        in_specs=[_smem()] + [_vmem()] * (2 * n_blk + 2),
        out_specs=tuple(_vmem() for _ in range(6)),
        scratch_shapes=_combine_scratch(n_blk, ny, nz),
    )(pos, *gathered, *gathered2, lr, loc2)
    final_field, adjoint_two = outs[:2]

    a2_lo, a2_hi, a2z_lo, a2z_hi = _yz_halos(*outs[2:])
    gradient = pl.pallas_call(
        _gradient_kernel,
        out_shape=shape,
        in_specs=[_vmem()] * 11,
        out_specs=_vmem(),
    )(pore_mask, grain_label, adjoint_two, gy_lo, gy_hi, gz_lo, gz_hi, a2_lo, a2_hi, a2z_lo, a2z_hi)
    return (final_field, gradient)


def solution(mesh):
    in_specs = (
        P("blk", "gy", "gz"),
        P("blk", "gy", "gz"),
        P("blk", "gy", "gz"),
        P("blk", "gy", "gz"),
    )
    out_specs = (P("blk", "gy", "gz"), P("blk", "gy", "gz"))
    return jax.shard_map(_shards, mesh=mesh, in_specs=in_specs, out_specs=out_specs, check_vma=False)
```

```python
import jax
import jax.numpy as jnp
from jax import lax
from jax.experimental import pallas as pl
from jax.experimental.pallas import tpu as pltpu
from jax.sharding import PartitionSpec as P


cross_rate = 0.0125
boundary_gain = 3.0
F32 = jnp.float32


def face_value(mobility_here, mobility_there, label_here, label_there):
    harmonic = 2.0 * mobility_here * mobility_there / (mobility_here + mobility_there)
    return harmonic * jnp.where(label_here != label_there, boundary_gain, 1.0)


def _vmem():
    return pl.BlockSpec(memory_space=pltpu.VMEM)


def _smem():
    return pl.BlockSpec(memory_space=pltpu.SMEM)


def _shift(x, edge, axis, up):
    n = x.shape[axis]
    idx = lax.broadcasted_iota(jnp.int32, x.shape, axis)
    edge = jnp.broadcast_to(edge, x.shape)
    if up:
        return jnp.where(idx == n - 1, edge, pltpu.roll(x, n - 1, axis))
    return jnp.where(idx == 0, edge, pltpu.roll(x, 1, axis))


def _neighbours(x, ylo, yhi, zlo, zhi):
    return (
        _shift(x, yhi, 0, True),
        _shift(x, ylo, 0, False),
        _shift(x, zhi, 1, True),
        _shift(x, zlo, 1, False),
    )


def _faces(mob, lab, mob_n, lab_n):
    ups = (True, False, True, False)
    out = []
    for up, mn, ln in zip(ups, mob_n, lab_n):
        if up:
            out.append(face_value(mob, mn, lab, ln))
        else:
            out.append(face_value(mn, mob, ln, lab))
    return out


def _flux(u, u_n, faces):
    total = faces[0] * (u_n[0] - u)
    total = total + faces[1] * (u_n[1] - u)
    total = total + faces[2] * (u_n[2] - u)
    total = total + faces[3] * (u_n[3] - u)
    return total


def _yrow(ref, c, i):
    return ref[c, pl.ds(i, 1), :]


def _zcol(ref, c, i):
    return ref[c, :, pl.ds(i, 1)]


def _write_edges(edges, c, r, val):
    y_first, y_last, z_first, z_last = edges
    ny, nz = val.shape
    y_first[c, pl.ds(r, 1), :] = val[0:1, :]
    y_last[c, pl.ds(r, 1), :] = val[ny - 1 : ny, :]
    z_first[c, :, pl.ds(r, 1)] = val[:, 0:1]
    z_last[c, :, pl.ds(r, 1)] = val[:, nz - 1 : nz]


def _geo_row(i, pore_ref, lab_ref, gy_lo, gy_hi, gz_lo, gz_hi):
    mob = 1.0 + 2.0 * pore_ref[i].astype(F32)
    lab = lab_ref[i].astype(F32)
    mob_n = _neighbours(mob, _yrow(gy_lo, 0, i), _yrow(gy_hi, 0, i), _zcol(gz_lo, 0, i), _zcol(gz_hi, 0, i))
    lab_n = _neighbours(lab, _yrow(gy_lo, 1, i), _yrow(gy_hi, 1, i), _zcol(gz_lo, 1, i), _zcol(gz_hi, 1, i))
    return mob, lab, mob_n, _faces(mob, lab, mob_n, lab_n)


def _sweep(m, lower, pivots, ratios, source):
    ys = [None] * m
    prev = None
    for r in range(m - 1):
        num = source[r]
        if num is None:
            if prev is None:
                continue
            num = -(lower[r] * prev)
        elif prev is not None:
            num = num - lower[r] * prev
        ys[r] = num / pivots[r]
        prev = ys[r]
    xs = [None] * m
    prev = None
    for r in range(m - 2, -1, -1):
        if prev is None:
            xs[r] = ys[r]
        elif ys[r] is None:
            xs[r] = -(ratios[r] * prev)
        else:
            xs[r] = ys[r] - ratios[r] * prev
        prev = xs[r]
    return xs


def _factor_kernel(cs, pore_ref, lab_ref, bx_lo, bx_hi, fac_f, fac_a, lr_f, lr_a, rows_ref):
    facs, lrs = (fac_f, fac_a), (lr_f, lr_a)
    m = pore_ref.shape[0]
    zero = jnp.zeros(pore_ref.shape[1:], F32)
    mobs = [1.0 + 2.0 * pore_ref[r].astype(F32) for r in range(m)]
    labs = [lab_ref[r].astype(F32) for r in range(m)]
    m_ext = [bx_lo[0]] + mobs + [bx_hi[0]]
    l_ext = [bx_lo[1]] + labs + [bx_hi[1]]
    w_ext = [0.5 * (1.0 + x) for x in m_ext]
    faces = [face_value(m_ext[k], m_ext[k + 1], l_ext[k], l_ext[k + 1]) for k in range(m + 1)]
    bands = {"f": ([], [], []), "a": ([], [], [])}
    for r in range(m):
        bf, ff = faces[r], faces[r + 1]
        w = w_ext[r + 1]
        main = 1.0 + cs * w * (bf + ff)
        bands["f"][0].append(-cs * bf * w_ext[r])
        bands["f"][1].append(main)
        bands["f"][2].append(-cs * ff * w_ext[r + 2])
        bands["a"][0].append(-cs * bf * w)
        bands["a"][1].append(main)
        bands["a"][2].append(-cs * ff * w)

    for c, key in ((0, "f"), (1, "a")):
        lower, main, upper = bands[key]
        pivots, ratios = [], []
        prev = None
        for r in range(m - 1):
            piv = main[r] if prev is None else main[r] - lower[r] * prev
            rat = upper[r] / piv
            pivots.append(piv)
            ratios.append(rat)
            prev = rat
        left_src = [lower[0]] + [None] * (m - 1)
        right_src = [None] * (m - 2) + [upper[m - 2], None]
        left = _sweep(m, lower, pivots, ratios, left_src)
        right = _sweep(m, lower, pivots, ratios, right_src)
        for r in range(m):
            facs[c][0, r] = lower[r]
            facs[c][1, r] = ratios[r] if r < m - 1 else zero
            facs[c][2, r] = pivots[r] if r < m - 1 else zero + 1.0
            lrs[c][0, r] = left[r] if r < m - 1 else zero
            lrs[c][1, r] = right[r] if r < m - 1 else zero - 1.0
        last_lower = lower[m - 1]
        rows_ref[c, 0] = last_lower * left[m - 2]
        rows_ref[c, 1] = main[m - 1] - last_lower * right[m - 2]
        rows_ref[c, 2] = upper[m - 1]
        rows_ref[c, 3] = left[0]
        rows_ref[c, 4] = right[0]


def _reduced_solve(gs, gv, voff, c, n, pos, cv=None):
    cv = c if cv is None else cv
    slot = [(pos - p + n) % n for p in range(n)]
    g = [[gs[slot[p], c, k] for k in range(5)] for p in range(n)]
    v = [[gv[slot[p], cv, voff + k] for k in range(2)] for p in range(n)]
    lower = [-g[p][0] for p in range(n)]
    main = [g[p][1] - g[p][2] * g[(p + 1) % n][3] for p in range(n)]
    upper = [-g[p][2] * g[(p + 1) % n][4] for p in range(n)]
    src = [v[p][0] - g[p][2] * v[(p + 1) % n][1] for p in range(n)]
    k_in = n - 1
    pivots, ratios = [], []
    prev = None
    for r in range(k_in):
        piv = main[r] if prev is None else main[r] - lower[r] * prev
        rat = upper[r] / piv
        pivots.append(piv)
        ratios.append(rat)
        prev = rat

    def apply(source):
        ys = []
        prev = None
        for r in range(k_in):
            num = source[r] if prev is None else source[r] - lower[r] * prev
            ys.append(num / pivots[r])
            prev = ys[-1]
        xs = [None] * k_in
        prev = None
        for r in range(k_in - 1, -1, -1):
            xs[r] = ys[r] if prev is None else ys[r] - ratios[r] * prev
            prev = xs[r]
        return xs

    coupling = []
    for r in range(k_in):
        term = None
        if r == 0:
            term = lower[0]
        if r == k_in - 1:
            term = upper[k_in - 1] if term is None else term + upper[k_in - 1]
        coupling.append(term if term is not None else jnp.zeros_like(lower[0]))
    linked = apply(coupling)
    closing = main[k_in] - lower[k_in] * linked[k_in - 1] - upper[k_in] * linked[0]
    inner = apply(src[:k_in])
    sep = (src[k_in] - lower[k_in] * inner[k_in - 1] - upper[k_in] * inner[0]) / closing
    return [inner[r] - linked[r] * sep for r in range(k_in)] + [sep]


def _edge_kernel(vac_ref, pore_ref, lab_ref, y_first, y_last, z_first, z_last, bx_first, bx_last):
    m = vac_ref.shape[0]
    edges = (y_first, y_last, z_first, z_last)
    for r in range(m):
        mob = 1.0 + 2.0 * pore_ref[r].astype(F32)
        lab = lab_ref[r].astype(F32)
        for c, val in enumerate((mob, lab, vac_ref[r])):
            _write_edges(edges, c, r, val)
        if r == 0:
            bx_first[0] = mob
            bx_first[1] = lab
        if r == m - 1:
            bx_last[0] = mob
            bx_last[1] = lab


def _solve_one(fac_ref, src, loc_ref, vals_ref):
    m = loc_ref.shape[0]
    zero = jnp.zeros(loc_ref.shape[1:], F32)
    lower = [fac_ref[0, r] for r in range(m)]
    ratios = [fac_ref[1, r] for r in range(m - 1)]
    pivots = [fac_ref[2, r] for r in range(m - 1)]
    local = _sweep(m, lower, pivots, ratios, src[: m - 1] + [None])
    for r in range(m):
        loc_ref[r] = local[r] if r < m - 1 else zero
    vals_ref[0] = src[m - 1] - lower[m - 1] * local[m - 2]
    vals_ref[1] = local[0]


def _first_fwd_kernel(vac_ref, pore_ref, lab_ref, fac_ref, gy_lo, gy_hi, gz_lo, gz_hi, loc_ref, vals_ref):
    m = pore_ref.shape[0]
    src = []
    for i in range(m):
        mob, _, mob_n, fc = _geo_row(i, pore_ref, lab_ref, gy_lo, gy_hi, gz_lo, gz_hi)
        w = 0.5 * (1.0 + mob)
        v = vac_ref[i]
        v_n = _neighbours(v, _yrow(gy_lo, 2, i), _yrow(gy_hi, 2, i), _zcol(gz_lo, 2, i), _zcol(gz_hi, 2, i))
        u_n = [0.5 * (1.0 + mn) * vn for mn, vn in zip(mob_n, v_n)]
        src.append(v + cross_rate * (1.0 * _flux(w * v, u_n, fc)))
    _solve_one(fac_ref, src, loc_ref, vals_ref)


def _first_adj_kernel(cot_ref, fac_ref, loc_ref, vals_ref):
    _solve_one(fac_ref, [cot_ref[r] for r in range(cot_ref.shape[0])], loc_ref, vals_ref)


def _second_one_kernel(ch, pore_ref, lab_ref, x_ref, fac_ref, gy_lo, gy_hi, gz_lo, gz_hi,
                       hy_lo, hy_hi, hz_lo, hz_hi, loc_ref, vals_ref):
    m = pore_ref.shape[0]
    src = []
    for i in range(m):
        mob, _, mob_n, fc = _geo_row(i, pore_ref, lab_ref, gy_lo, gy_hi, gz_lo, gz_hi)
        w = 0.5 * (1.0 + mob)
        x = x_ref[i]
        x_n = _neighbours(x, _yrow(hy_lo, ch, i), _yrow(hy_hi, ch, i), _zcol(hz_lo, ch, i), _zcol(hz_hi, ch, i))
        if ch == 0:
            u_n = [0.5 * (1.0 + mn) * xn for mn, xn in zip(mob_n, x_n)]
            src.append(x + cross_rate * (1.0 * _flux(w * x, u_n, fc)))
        else:
            src.append(x + cross_rate * (w * _flux(x, x_n, fc)))
    _solve_one(fac_ref, src, loc_ref, vals_ref)


def _combine_one_kernel(n, c, extra_edges, pos_ref, *refs):
    gs_parts, gv_parts = refs[:n], refs[n : 2 * n]
    refs = refs[2 * n :]
    lr_ref, loc_ref = refs[0], refs[1]
    refs = refs[2:]
    if extra_edges:
        other, refs = refs[:4], refs[4:]
    out_ref, refs = refs[0], refs[1:]
    edges = refs[:4] if len(refs) > 4 else None
    sep_ref, gs_ref, gv_ref = refs[-3:]
    for k in range(n):
        gs_ref[k] = gs_parts[k][...]
        gv_ref[k, 0] = gv_parts[k][...]
    m = loc_ref.shape[0]
    p = pos_ref[0]
    seps = _reduced_solve(gs_ref, gv_ref, 0, c, n, p, cv=0)
    for q in range(n):
        sep_ref[q] = seps[q]
    own = sep_ref[p]
    prior = sep_ref[(p + n - 1) % n]
    for r in range(m):
        val = loc_ref[r] - lr_ref[0, r] * prior - lr_ref[1, r] * own
        out_ref[r] = val
        if edges is not None:
            _write_edges(edges, 0, r, val)
    if extra_edges:
        for e_out, e_in in zip(edges, other):
            e_out[1] = e_in[0]


def _gradient_kernel(pore_ref, lab_ref, a2_ref, gy_lo, gy_hi, gz_lo, gz_hi,
                     hy_lo, hy_hi, hz_lo, hz_hi, out_ref):
    m = pore_ref.shape[0]
    for i in range(m):
        mob, _, _, fc = _geo_row(i, pore_ref, lab_ref, gy_lo, gy_hi, gz_lo, gz_hi)
        w = 0.5 * (1.0 + mob)
        a2 = a2_ref[i]
        a_n = _neighbours(a2, _yrow(hy_lo, 0, i), _yrow(hy_hi, 0, i), _zcol(hz_lo, 0, i), _zcol(hz_hi, 0, i))
        out_ref[i] = a2 + cross_rate * (w * _flux(a2, a_n, fc))


def _halo_pairs(axis, periodic):
    count = lax.axis_size(axis)
    forward = [(i, i + 1) for i in range(count - 1)]
    if periodic:
        forward.append((count - 1, 0))
    backward = [(t, s) for s, t in forward]
    return forward, backward


def _exchange(first, last, axis, periodic):
    forward, backward = _halo_pairs(axis, periodic)
    lo = lax.ppermute(last, axis, forward)
    hi = lax.ppermute(first, axis, backward)
    return lo, hi


def _gather_blk(x):
    n = lax.axis_size("blk")
    parts = [x]
    for k in range(1, n):
        parts.append(lax.ppermute(x, "blk", [(j, (j + k) % n) for j in range(n)]))
    return parts


def _edge_shapes(chans, m, ny, nz):
    return (
        jax.ShapeDtypeStruct((chans, m, nz), F32),
        jax.ShapeDtypeStruct((chans, m, nz), F32),
        jax.ShapeDtypeStruct((chans, ny, m), F32),
        jax.ShapeDtypeStruct((chans, ny, m), F32),
    )


def _yz_halos(y_first, y_last, z_first, z_last):
    gy_lo, gy_hi = _exchange(y_first, y_last, "gy", False)
    gz_lo, gz_hi = _exchange(z_first, z_last, "gz", False)
    return gy_lo, gy_hi, gz_lo, gz_hi


def _shards(vacancy, grain_label, pore_mask, cotangent):
    m, ny, nz = vacancy.shape
    n_blk = lax.axis_size("blk")
    cycle_step = float((m * n_blk) ** 2 // 64)
    shape = jax.ShapeDtypeStruct((m, ny, nz), F32)

    outs = pl.pallas_call(
        _edge_kernel,
        out_shape=_edge_shapes(3, m, ny, nz) + (jax.ShapeDtypeStruct((2, ny, nz), F32),) * 2,
        in_specs=[_vmem()] * 3,
        out_specs=tuple(_vmem() for _ in range(6)),
    )(vacancy, pore_mask, grain_label)
    bx_lo, bx_hi = _exchange(outs[4], outs[5], "blk", True)
    gy_lo, gy_hi, gz_lo, gz_hi = _yz_halos(*outs[:4])

    fac_f, fac_a, lr_f, lr_a, rows = pl.pallas_call(
        lambda *r: _factor_kernel(cycle_step, *r),
        out_shape=(jax.ShapeDtypeStruct((3, m, ny, nz), F32),) * 2
        + (jax.ShapeDtypeStruct((2, m, ny, nz), F32),) * 2
        + (jax.ShapeDtypeStruct((2, 5, ny, nz), F32),),
        in_specs=[_vmem()] * 4,
        out_specs=tuple(_vmem() for _ in range(5)),
    )(pore_mask, grain_label, bx_lo, bx_hi)
    gathered = _gather_blk(rows)
    pos = jnp.reshape(lax.axis_index("blk"), (1,)).astype(jnp.int32)
    vals_shape = jax.ShapeDtypeStruct((2, ny, nz), F32)

    loc_a, vals_a = pl.pallas_call(
        _first_adj_kernel,
        out_shape=(shape, vals_shape),
        in_specs=[_vmem()] * 2,
        out_specs=(_vmem(), _vmem()),
    )(cotangent, fac_a)
    g_a1 = _gather_blk(vals_a)
    loc_f, vals_f = pl.pallas_call(
        _first_fwd_kernel,
        out_shape=(shape, vals_shape),
        in_specs=[_vmem()] * 8,
        out_specs=(_vmem(), _vmem()),
    )(vacancy, pore_mask, grain_label, fac_f, gy_lo, gy_hi, gz_lo, gz_hi)
    g_f1 = _gather_blk(vals_f)

    def combine(c, g_vals, lr, loc, edge_chans, other=None):
        extra = other is not None
        out_shape = (shape,) + (_edge_shapes(edge_chans, m, ny, nz) if edge_chans else ())
        return pl.pallas_call(
            lambda *r: _combine_one_kernel(n_blk, c, extra, *r),
            out_shape=out_shape,
            in_specs=[_smem()] + [_vmem()] * (2 * n_blk + 2 + (4 if extra else 0)),
            out_specs=tuple(_vmem() for _ in out_shape),
            scratch_shapes=[
                pltpu.VMEM((n_blk, ny, nz), F32),
                pltpu.VMEM((n_blk, 2, 5, ny, nz), F32),
                pltpu.VMEM((n_blk, 1, 2, ny, nz), F32),
            ],
        )(pos, *gathered, *g_vals, lr, loc, *((other or ())))

    a1_out = combine(1, g_a1, lr_a, loc_a, 1)
    f1_out = combine(0, g_f1, lr_f, loc_f, 2, other=a1_out[1:])
    adjoint_one, field_one = a1_out[0], f1_out[0]

    hy_lo, hy_hi, hz_lo, hz_hi = _yz_halos(*f1_out[1:])

    def second(ch, x, fac):
        return pl.pallas_call(
            lambda *r: _second_one_kernel(ch, *r),
            out_shape=(shape, vals_shape),
            in_specs=[_vmem()] * 12,
            out_specs=(_vmem(), _vmem()),
        )(pore_mask, grain_label, x, fac, gy_lo, gy_hi, gz_lo, gz_hi, hy_lo, hy_hi, hz_lo, hz_hi)

    loc2_a, vals2_a = second(1, adjoint_one, fac_a)
    g_a2 = _gather_blk(vals2_a)
    loc2_f, vals2_f = second(0, field_one, fac_f)
    g_f2 = _gather_blk(vals2_f)
    a2_out = combine(1, g_a2, lr_a, loc2_a, 1)
    adjoint_two = a2_out[0]
    a2_lo, a2_hi, a2z_lo, a2z_hi = _yz_halos(*a2_out[1:])
    final_field = combine(0, g_f2, lr_f, loc2_f, 0)[0]
    gradient = pl.pallas_call(
        _gradient_kernel,
        out_shape=shape,
        in_specs=[_vmem()] * 11,
        out_specs=_vmem(),
    )(pore_mask, grain_label, adjoint_two, gy_lo, gy_hi, gz_lo, gz_hi, a2_lo, a2_hi, a2z_lo, a2z_hi)
    return (final_field, gradient)


def solution(mesh):
    in_specs = (
        P("blk", "gy", "gz"),
        P("blk", "gy", "gz"),
        P("blk", "gy", "gz"),
        P("blk", "gy", "gz"),
    )
    out_specs = (P("blk", "gy", "gz"), P("blk", "gy", "gz"))
    return jax.shard_map(_shards, mesh=mesh, in_specs=in_specs, out_specs=out_specs, check_vma=False)
```

```python
import jax
import jax.numpy as jnp
from jax import lax
from jax.experimental import pallas as pl
from jax.experimental.pallas import tpu as pltpu
from jax.sharding import PartitionSpec as P


cross_rate = 0.0125
boundary_gain = 3.0
F32 = jnp.float32


def face_value(mobility_here, mobility_there, label_here, label_there):
    harmonic = 2.0 * mobility_here * mobility_there / (mobility_here + mobility_there)
    return harmonic * jnp.where(label_here != label_there, boundary_gain, 1.0)


def _vmem():
    return pl.BlockSpec(memory_space=pltpu.VMEM)


def _smem():
    return pl.BlockSpec(memory_space=pltpu.SMEM)


def _shift(x, edge, axis, up):
    n = x.shape[axis]
    idx = lax.broadcasted_iota(jnp.int32, x.shape, axis)
    edge = jnp.broadcast_to(edge, x.shape)
    if up:
        return jnp.where(idx == n - 1, edge, pltpu.roll(x, n - 1, axis))
    return jnp.where(idx == 0, edge, pltpu.roll(x, 1, axis))


def _neighbours(x, ylo, yhi, zlo, zhi):
    return (
        _shift(x, yhi, 0, True),
        _shift(x, ylo, 0, False),
        _shift(x, zhi, 1, True),
        _shift(x, zlo, 1, False),
    )


def _faces(mob, lab, mob_n, lab_n):
    ups = (True, False, True, False)
    out = []
    for up, mn, ln in zip(ups, mob_n, lab_n):
        if up:
            out.append(face_value(mob, mn, lab, ln))
        else:
            out.append(face_value(mn, mob, ln, lab))
    return out


def _flux(u, u_n, faces):
    total = faces[0] * (u_n[0] - u)
    total = total + faces[1] * (u_n[1] - u)
    total = total + faces[2] * (u_n[2] - u)
    total = total + faces[3] * (u_n[3] - u)
    return total


def _yrow(ref, c, i):
    return ref[c, pl.ds(i, 1), :]


def _zcol(ref, c, i):
    return ref[c, :, pl.ds(i, 1)]


def _write_edges(edges, c, r, val, par):
    y_a, y_b, z_a, z_b = edges
    even_y, even_z = par
    ny, nz = val.shape
    y_first, y_last = val[0:1, :], val[ny - 1 : ny, :]
    z_first, z_last = val[:, 0:1], val[:, nz - 1 : nz]
    y_a[c, pl.ds(r, 1), :] = jnp.where(even_y, y_last, y_first)
    y_b[c, pl.ds(r, 1), :] = jnp.where(even_y, y_first, y_last)
    z_a[c, :, pl.ds(r, 1)] = jnp.where(even_z, z_last, z_first)
    z_b[c, :, pl.ds(r, 1)] = jnp.where(even_z, z_first, z_last)


class _Pick:
    def __init__(self, a, b, use_b):
        self.a, self.b, self.use_b = a, b, use_b

    def __getitem__(self, idx):
        return jnp.where(self.use_b, self.b[idx], self.a[idx])


def _parity(ctl_ref):
    return ctl_ref[1] == 1, ctl_ref[2] == 1


def _picks(ctl_ref, y_a, y_b, z_a, z_b):
    even_y, even_z = _parity(ctl_ref)
    return (
        _Pick(y_a, y_b, even_y),
        _Pick(y_a, y_b, jnp.logical_not(even_y)),
        _Pick(z_a, z_b, even_z),
        _Pick(z_a, z_b, jnp.logical_not(even_z)),
    )


def _geo_row(i, pore_ref, lab_ref, gy_lo, gy_hi, gz_lo, gz_hi):
    mob = 1.0 + 2.0 * pore_ref[i].astype(F32)
    lab = lab_ref[i].astype(F32)
    mob_n = _neighbours(mob, _yrow(gy_lo, 0, i), _yrow(gy_hi, 0, i), _zcol(gz_lo, 0, i), _zcol(gz_hi, 0, i))
    lab_n = _neighbours(lab, _yrow(gy_lo, 1, i), _yrow(gy_hi, 1, i), _zcol(gz_lo, 1, i), _zcol(gz_hi, 1, i))
    return mob, lab, mob_n, _faces(mob, lab, mob_n, lab_n)


def _sweep(m, lower, pivots, ratios, source):
    ys = [None] * m
    prev = None
    for r in range(m - 1):
        num = source[r]
        if num is None:
            if prev is None:
                continue
            num = -(lower[r] * prev)
        elif prev is not None:
            num = num - lower[r] * prev
        ys[r] = num / pivots[r]
        prev = ys[r]
    xs = [None] * m
    prev = None
    for r in range(m - 2, -1, -1):
        if prev is None:
            xs[r] = ys[r]
        elif ys[r] is None:
            xs[r] = -(ratios[r] * prev)
        else:
            xs[r] = ys[r] - ratios[r] * prev
        prev = xs[r]
    return xs


def _factor_kernel(cs, lo_i, hi_i, pore_ref, lab_ref, bx_ref, fac_ref, lr_ref, rows_ref):
    bx_lo, bx_hi = bx_ref.at[lo_i], bx_ref.at[hi_i]
    m = pore_ref.shape[0]
    zero = jnp.zeros(pore_ref.shape[1:], F32)
    mobs = [1.0 + 2.0 * pore_ref[r].astype(F32) for r in range(m)]
    labs = [lab_ref[r].astype(F32) for r in range(m)]
    m_ext = [bx_lo[0]] + mobs + [bx_hi[0]]
    l_ext = [bx_lo[1]] + labs + [bx_hi[1]]
    w_ext = [0.5 * (1.0 + x) for x in m_ext]
    faces = [face_value(m_ext[k], m_ext[k + 1], l_ext[k], l_ext[k + 1]) for k in range(m + 1)]
    bands = {"f": ([], [], []), "a": ([], [], [])}
    for r in range(m):
        bf, ff = faces[r], faces[r + 1]
        w = w_ext[r + 1]
        main = 1.0 + cs * w * (bf + ff)
        bands["f"][0].append(-cs * bf * w_ext[r])
        bands["f"][1].append(main)
        bands["f"][2].append(-cs * ff * w_ext[r + 2])
        bands["a"][0].append(-cs * bf * w)
        bands["a"][1].append(main)
        bands["a"][2].append(-cs * ff * w)

    for c, key in ((0, "f"), (1, "a")):
        lower, main, upper = bands[key]
        pivots, ratios = [], []
        prev = None
        for r in range(m - 1):
            piv = main[r] if prev is None else main[r] - lower[r] * prev
            rat = upper[r] / piv
            pivots.append(piv)
            ratios.append(rat)
            prev = rat
        left_src = [lower[0]] + [None] * (m - 1)
        right_src = [None] * (m - 2) + [upper[m - 2], None]
        left = _sweep(m, lower, pivots, ratios, left_src)
        right = _sweep(m, lower, pivots, ratios, right_src)
        for r in range(m):
            fac_ref[c, 0, r] = lower[r]
            fac_ref[c, 1, r] = ratios[r] if r < m - 1 else zero
            fac_ref[c, 2, r] = pivots[r] if r < m - 1 else zero + 1.0
            lr_ref[c, 0, r] = left[r] if r < m - 1 else zero
            lr_ref[c, 1, r] = right[r] if r < m - 1 else zero - 1.0
        last_lower = lower[m - 1]
        rows_ref[c, 0] = last_lower * left[m - 2]
        rows_ref[c, 1] = main[m - 1] - last_lower * right[m - 2]
        rows_ref[c, 2] = upper[m - 1]
        rows_ref[c, 3] = left[0]
        rows_ref[c, 4] = right[0]


def _reduced_solve(gs, gv, voff, c, n, pos):
    slot = [(pos - p + n) % n for p in range(n)]
    g = [[gs[slot[p], c, k] for k in range(5)] for p in range(n)]
    v = [[gv[slot[p], c, voff + k] for k in range(2)] for p in range(n)]
    lower = [-g[p][0] for p in range(n)]
    main = [g[p][1] - g[p][2] * g[(p + 1) % n][3] for p in range(n)]
    upper = [-g[p][2] * g[(p + 1) % n][4] for p in range(n)]
    src = [v[p][0] - g[p][2] * v[(p + 1) % n][1] for p in range(n)]
    k_in = n - 1
    pivots, ratios = [], []
    prev = None
    for r in range(k_in):
        piv = main[r] if prev is None else main[r] - lower[r] * prev
        rat = upper[r] / piv
        pivots.append(piv)
        ratios.append(rat)
        prev = rat

    def apply(source):
        ys = []
        prev = None
        for r in range(k_in):
            num = source[r] if prev is None else source[r] - lower[r] * prev
            ys.append(num / pivots[r])
            prev = ys[-1]
        xs = [None] * k_in
        prev = None
        for r in range(k_in - 1, -1, -1):
            xs[r] = ys[r] if prev is None else ys[r] - ratios[r] * prev
            prev = xs[r]
        return xs

    coupling = []
    for r in range(k_in):
        term = None
        if r == 0:
            term = lower[0]
        if r == k_in - 1:
            term = upper[k_in - 1] if term is None else term + upper[k_in - 1]
        coupling.append(term if term is not None else jnp.zeros_like(lower[0]))
    linked = apply(coupling)
    closing = main[k_in] - lower[k_in] * linked[k_in - 1] - upper[k_in] * linked[0]
    inner = apply(src[:k_in])
    sep = (src[k_in] - lower[k_in] * inner[k_in - 1] - upper[k_in] * inner[0]) / closing
    return [inner[r] - linked[r] * sep for r in range(k_in)] + [sep]


def _combine_kernel(n, stacked, edge_of, pos_ref, *refs):
    gs_parts, gv_parts = refs[:n], refs[n : 2 * n]
    lr_ref, loc_ref = refs[2 * n], refs[2 * n + 1]
    refs = refs[2 * n + 2 :]
    if stacked:
        out_ref = refs[0]
        outs = (out_ref.at[0], out_ref.at[1])
        rest = refs[1:]
    else:
        outs = refs[:2]
        rest = refs[2:]
    edges, sep_ref, gs_ref, gv_ref = rest[:4], rest[4], rest[5], rest[6]
    for k in range(n):
        gs_ref[k] = gs_parts[k][...]
        gv_ref[k] = gv_parts[k][...]
    m = loc_ref.shape[1]
    p = pos_ref[0]
    for c in range(2):
        seps = _reduced_solve(gs_ref, gv_ref, 0, c, n, p)
        for q in range(n):
            sep_ref[q] = seps[q]
        own = sep_ref[p]
        prior = sep_ref[(p + n - 1) % n]
        for r in range(m):
            val = loc_ref[c, r] - lr_ref[c, 0, r] * prior - lr_ref[c, 1, r] * own
            outs[c][r] = val
            if c in edge_of:
                _write_edges(edges, edge_of[c], r, val, _parity(pos_ref))


def _edge_kernel(ctl_ref, vac_ref, pore_ref, lab_ref, y_first, y_last, z_first, z_last, bx_ref):
    m = vac_ref.shape[0]
    edges = (y_first, y_last, z_first, z_last)
    for r in range(m):
        mob = 1.0 + 2.0 * pore_ref[r].astype(F32)
        lab = lab_ref[r].astype(F32)
        for c, val in enumerate((mob, lab, vac_ref[r])):
            _write_edges(edges, c, r, val, _parity(ctl_ref))
        if r == 0:
            bx_ref[0, 0] = mob
            bx_ref[0, 1] = lab
        if r == m - 1:
            bx_ref[1, 0] = mob
            bx_ref[1, 1] = lab


def _local_solves(fac_ref, srcs, loc_ref, vals_ref):
    m = loc_ref.shape[1]
    zero = jnp.zeros(loc_ref.shape[2:], F32)
    for c in range(2):
        lower = [fac_ref[c, 0, r] for r in range(m)]
        ratios = [fac_ref[c, 1, r] for r in range(m - 1)]
        pivots = [fac_ref[c, 2, r] for r in range(m - 1)]
        src = srcs[c]
        local = _sweep(m, lower, pivots, ratios, src[: m - 1] + [None])
        for r in range(m):
            loc_ref[c, r] = local[r] if r < m - 1 else zero
        vals_ref[c, 0] = src[m - 1] - lower[m - 1] * local[m - 2]
        vals_ref[c, 1] = local[0]


def _first_kernel(ctl_ref, vac_ref, cot_ref, pore_ref, lab_ref, fac_ref, gy_lo, gy_hi, gz_lo, gz_hi, loc_ref, vals_ref):
    gy_lo, gy_hi, gz_lo, gz_hi = _picks(ctl_ref, gy_lo, gy_hi, gz_lo, gz_hi)
    m = pore_ref.shape[0]
    srcs = ([], [cot_ref[r] for r in range(m)])
    for i in range(m):
        mob, _, mob_n, fc = _geo_row(i, pore_ref, lab_ref, gy_lo, gy_hi, gz_lo, gz_hi)
        w = 0.5 * (1.0 + mob)
        v = vac_ref[i]
        v_n = _neighbours(v, _yrow(gy_lo, 2, i), _yrow(gy_hi, 2, i), _zcol(gz_lo, 2, i), _zcol(gz_hi, 2, i))
        u_n = [0.5 * (1.0 + mn) * vn for mn, vn in zip(mob_n, v_n)]
        srcs[0].append(v + cross_rate * (1.0 * _flux(w * v, u_n, fc)))
    _local_solves(fac_ref, srcs, loc_ref, vals_ref)


def _second_kernel(ctl_ref, pore_ref, lab_ref, fa_ref, fac_ref, gy_lo, gy_hi, gz_lo, gz_hi,
                   hy_lo, hy_hi, hz_lo, hz_hi, loc_ref, vals_ref):
    gy_lo, gy_hi, gz_lo, gz_hi = _picks(ctl_ref, gy_lo, gy_hi, gz_lo, gz_hi)
    hy_lo, hy_hi, hz_lo, hz_hi = _picks(ctl_ref, hy_lo, hy_hi, hz_lo, hz_hi)
    m = pore_ref.shape[0]
    srcs = ([], [])
    for i in range(m):
        mob, _, mob_n, fc = _geo_row(i, pore_ref, lab_ref, gy_lo, gy_hi, gz_lo, gz_hi)
        w = 0.5 * (1.0 + mob)
        f1 = fa_ref[0, i]
        f_n = _neighbours(f1, _yrow(hy_lo, 0, i), _yrow(hy_hi, 0, i), _zcol(hz_lo, 0, i), _zcol(hz_hi, 0, i))
        u_n = [0.5 * (1.0 + mn) * fn for mn, fn in zip(mob_n, f_n)]
        srcs[0].append(f1 + cross_rate * (1.0 * _flux(w * f1, u_n, fc)))
        a1 = fa_ref[1, i]
        a_n = _neighbours(a1, _yrow(hy_lo, 1, i), _yrow(hy_hi, 1, i), _zcol(hz_lo, 1, i), _zcol(hz_hi, 1, i))
        srcs[1].append(a1 + cross_rate * (w * _flux(a1, a_n, fc)))
    _local_solves(fac_ref, srcs, loc_ref, vals_ref)


def _gradient_kernel(ctl_ref, pore_ref, lab_ref, a2_ref, gy_lo, gy_hi, gz_lo, gz_hi,
                     hy_lo, hy_hi, hz_lo, hz_hi, out_ref):
    gy_lo, gy_hi, gz_lo, gz_hi = _picks(ctl_ref, gy_lo, gy_hi, gz_lo, gz_hi)
    hy_lo, hy_hi, hz_lo, hz_hi = _picks(ctl_ref, hy_lo, hy_hi, hz_lo, hz_hi)
    m = pore_ref.shape[0]
    for i in range(m):
        mob, _, _, fc = _geo_row(i, pore_ref, lab_ref, gy_lo, gy_hi, gz_lo, gz_hi)
        w = 0.5 * (1.0 + mob)
        a2 = a2_ref[i]
        a_n = _neighbours(a2, _yrow(hy_lo, 0, i), _yrow(hy_hi, 0, i), _zcol(hz_lo, 0, i), _zcol(hz_hi, 0, i))
        out_ref[i] = a2 + cross_rate * (w * _flux(a2, a_n, fc))


def _halo_pairs(axis, periodic):
    count = lax.axis_size(axis)
    forward = [(i, i + 1) for i in range(count - 1)]
    if periodic:
        forward.append((count - 1, 0))
    backward = [(t, s) for s, t in forward]
    return forward, backward


def _exchange(first, last, axis, periodic):
    forward, backward = _halo_pairs(axis, periodic)
    lo = lax.ppermute(last, axis, forward)
    hi = lax.ppermute(first, axis, backward)
    return lo, hi


def _first_call(m, ny, nz):
    return pl.pallas_call(
        _first_kernel,
        out_shape=(
            jax.ShapeDtypeStruct((2, m, ny, nz), F32),
            jax.ShapeDtypeStruct((2, 2, ny, nz), F32),
        ),
        in_specs=[_smem()] + [_vmem()] * 9,
        out_specs=(_vmem(), _vmem()),
    )


def _combine_scratch(n, ny, nz):
    return [
        pltpu.VMEM((n, ny, nz), F32),
        pltpu.VMEM((n, 2, 5, ny, nz), F32),
        pltpu.VMEM((n, 2, 2, ny, nz), F32),
    ]


def _gather_blk(x):
    n = lax.axis_size("blk")
    parts = [x]
    for k in range(1, n):
        parts.append(lax.ppermute(x, "blk", [(j, (j + k) % n) for j in range(n)]))
    return parts


def _edge_shapes(chans, m, ny, nz):
    return (
        jax.ShapeDtypeStruct((chans, m, nz), F32),
        jax.ShapeDtypeStruct((chans, m, nz), F32),
        jax.ShapeDtypeStruct((chans, ny, m), F32),
        jax.ShapeDtypeStruct((chans, ny, m), F32),
    )


def _swap(x_a, x_b, axis):
    n = lax.axis_size(axis)
    pairs_a = [(i, i ^ 1) for i in range(n) if i ^ 1 < n]
    pairs_b = [(i, i + 1) for i in range(1, n - 1, 2)] + [(i + 1, i) for i in range(1, n - 1, 2)]
    recv_a = lax.ppermute(x_a, axis, pairs_a)
    recv_b = lax.ppermute(x_b, axis, pairs_b) if pairs_b else jnp.zeros_like(x_b)
    return recv_a, recv_b


def _yz_halos(y_a, y_b, z_a, z_b):
    return _swap(y_a, y_b, "gy") + _swap(z_a, z_b, "gz")


def _shards(vacancy, grain_label, pore_mask, cotangent):
    m, ny, nz = vacancy.shape
    n_blk = lax.axis_size("blk")
    cycle_step = float((m * n_blk) ** 2 // 64)
    shape = jax.ShapeDtypeStruct((m, ny, nz), F32)

    ctl = jnp.stack(
        [lax.axis_index("blk"), 1 - lax.axis_index("gy") % 2, 1 - lax.axis_index("gz") % 2]
    ).astype(jnp.int32)
    outs = pl.pallas_call(
        _edge_kernel,
        out_shape=_edge_shapes(3, m, ny, nz) + (jax.ShapeDtypeStruct((2, 2, ny, nz), F32),),
        in_specs=[_smem()] + [_vmem()] * 3,
        out_specs=tuple(_vmem() for _ in range(5)),
    )(ctl, vacancy, pore_mask, grain_label)
    if n_blk == 2:
        bx = lax.ppermute(outs[4], "blk", [(0, 1), (1, 0)])
        lo_i, hi_i = 1, 0
    else:
        bx_lo, bx_hi = _exchange(outs[4][0], outs[4][1], "blk", True)
        bx = jnp.stack([bx_lo, bx_hi])
        lo_i, hi_i = 0, 1
    gy_lo, gy_hi, gz_lo, gz_hi = _yz_halos(*outs[:4])

    fac, lr, rows = pl.pallas_call(
        lambda *r: _factor_kernel(cycle_step, lo_i, hi_i, *r),
        out_shape=(
            jax.ShapeDtypeStruct((2, 3, m, ny, nz), F32),
            jax.ShapeDtypeStruct((2, 2, m, ny, nz), F32),
            jax.ShapeDtypeStruct((2, 5, ny, nz), F32),
        ),
        in_specs=[_vmem()] * 3,
        out_specs=(_vmem(), _vmem(), _vmem()),
    )(pore_mask, grain_label, bx)
    gathered = _gather_blk(rows)

    loc, vals = _first_call(m, ny, nz)(
        ctl, vacancy, cotangent, pore_mask, grain_label, fac, gy_lo, gy_hi, gz_lo, gz_hi
    )
    gathered1 = _gather_blk(vals)
    pos = ctl

    outs = pl.pallas_call(
        lambda *r: _combine_kernel(n_blk, True, {0: 0, 1: 1}, *r),
        out_shape=(jax.ShapeDtypeStruct((2, m, ny, nz), F32),) + _edge_shapes(2, m, ny, nz),
        in_specs=[_smem()] + [_vmem()] * (2 * n_blk + 2),
        out_specs=tuple(_vmem() for _ in range(5)),
        scratch_shapes=_combine_scratch(n_blk, ny, nz),
    )(pos, *gathered, *gathered1, lr, loc)
    fa = outs[0]

    hy_lo, hy_hi, hz_lo, hz_hi = _yz_halos(*outs[1:])
    loc2, vals2 = pl.pallas_call(
        _second_kernel,
        out_shape=(
            jax.ShapeDtypeStruct((2, m, ny, nz), F32),
            jax.ShapeDtypeStruct((2, 2, ny, nz), F32),
        ),
        in_specs=[_smem()] + [_vmem()] * 12,
        out_specs=(_vmem(), _vmem()),
    )(ctl, pore_mask, grain_label, fa, fac, gy_lo, gy_hi, gz_lo, gz_hi, hy_lo, hy_hi, hz_lo, hz_hi)

    gathered2 = _gather_blk(vals2)
    outs = pl.pallas_call(
        lambda *r: _combine_kernel(n_blk, False, {1: 0}, *r),
        out_shape=(shape, shape) + _edge_shapes(1, m, ny, nz),
        in_specs=[_smem()] + [_vmem()] * (2 * n_blk + 2),
        out_specs=tuple(_vmem() for _ in range(6)),
        scratch_shapes=_combine_scratch(n_blk, ny, nz),
    )(pos, *gathered, *gathered2, lr, loc2)
    final_field, adjoint_two = outs[:2]

    a2_lo, a2_hi, a2z_lo, a2z_hi = _yz_halos(*outs[2:])
    gradient = pl.pallas_call(
        _gradient_kernel,
        out_shape=shape,
        in_specs=[_smem()] + [_vmem()] * 11,
        out_specs=_vmem(),
    )(ctl, pore_mask, grain_label, adjoint_two, gy_lo, gy_hi, gz_lo, gz_hi, a2_lo, a2_hi, a2z_lo, a2z_hi)
    return (final_field, gradient)


def solution(mesh):
    in_specs = (
        P("blk", "gy", "gz"),
        P("blk", "gy", "gz"),
        P("blk", "gy", "gz"),
        P("blk", "gy", "gz"),
    )
    out_specs = (P("blk", "gy", "gz"), P("blk", "gy", "gz"))
    fn = jax.shard_map(_shards, mesh=mesh, in_specs=in_specs, out_specs=out_specs, check_vma=False)
    if mesh.shape["blk"] > 4:
        return fn
    return fn
```

```python
import jax
import jax.numpy as jnp
from jax import lax
from jax.experimental import pallas as pl
from jax.experimental.pallas import tpu as pltpu
from jax.sharding import PartitionSpec as P


cross_rate = 0.0125
boundary_gain = 3.0
F32 = jnp.float32


def face_value(mobility_here, mobility_there, label_here, label_there):
    harmonic = 2.0 * mobility_here * mobility_there / (mobility_here + mobility_there)
    return harmonic * jnp.where(label_here != label_there, boundary_gain, 1.0)


def _vmem():
    return pl.BlockSpec(memory_space=pltpu.VMEM)


def _smem():
    return pl.BlockSpec(memory_space=pltpu.SMEM)


def _shift(x, edge, axis, up):
    n = x.shape[axis]
    idx = lax.broadcasted_iota(jnp.int32, x.shape, axis)
    edge = jnp.broadcast_to(edge, x.shape)
    if up:
        return jnp.where(idx == n - 1, edge, pltpu.roll(x, n - 1, axis))
    return jnp.where(idx == 0, edge, pltpu.roll(x, 1, axis))


def _neighbours(x, ylo, yhi, zlo, zhi):
    return (
        _shift(x, yhi, 0, True),
        _shift(x, ylo, 0, False),
        _shift(x, zhi, 1, True),
        _shift(x, zlo, 1, False),
    )


def _faces(mob, lab, mob_n, lab_n):
    ups = (True, False, True, False)
    out = []
    for up, mn, ln in zip(ups, mob_n, lab_n):
        if up:
            out.append(face_value(mob, mn, lab, ln))
        else:
            out.append(face_value(mn, mob, ln, lab))
    return out


def _flux(u, u_n, faces):
    total = faces[0] * (u_n[0] - u)
    total = total + faces[1] * (u_n[1] - u)
    total = total + faces[2] * (u_n[2] - u)
    total = total + faces[3] * (u_n[3] - u)
    return total


def _yrow(ref, c, i):
    return ref[c, pl.ds(i, 1), :]


def _zcol(ref, c, i):
    return ref[c, :, pl.ds(i, 1)]


def _write_edges(edges, c, r, val):
    y_first, y_last, z_first, z_last = edges
    ny, nz = val.shape
    y_first[c, pl.ds(r, 1), :] = val[0:1, :]
    y_last[c, pl.ds(r, 1), :] = val[ny - 1 : ny, :]
    z_first[c, :, pl.ds(r, 1)] = val[:, 0:1]
    z_last[c, :, pl.ds(r, 1)] = val[:, nz - 1 : nz]


def _flush_edges(scratch, outs, par):
    y_first, y_last, z_first, z_last = scratch
    y_a, y_b, z_a, z_b = outs
    even_y, even_z = par
    for even, first, last, out_a, out_b in ((even_y, y_first, y_last, y_a, y_b), (even_z, z_first, z_last, z_a, z_b)):

        @pl.when(even)
        def _():
            out_a[...] = last[...]
            out_b[...] = first[...]

        @pl.when(jnp.logical_not(even))
        def _():
            out_a[...] = first[...]
            out_b[...] = last[...]


def _edge_scratch(chans, m, ny, nz):
    return [
        pltpu.VMEM((chans, m, nz), F32),
        pltpu.VMEM((chans, m, nz), F32),
        pltpu.VMEM((chans, ny, m), F32),
        pltpu.VMEM((chans, ny, m), F32),
    ]


class _Pick:
    def __init__(self, a, b, use_b):
        self.a, self.b, self.use_b = a, b, use_b

    def __getitem__(self, idx):
        return jnp.where(self.use_b, self.b[idx], self.a[idx])


def _parity(ctl_ref):
    return ctl_ref[1] == 1, ctl_ref[2] == 1


def _picks(ctl_ref, y_a, y_b, z_a, z_b):
    even_y, even_z = _parity(ctl_ref)
    return (
        _Pick(y_a, y_b, even_y),
        _Pick(y_a, y_b, jnp.logical_not(even_y)),
        _Pick(z_a, z_b, even_z),
        _Pick(z_a, z_b, jnp.logical_not(even_z)),
    )


def _geo_row(i, pore_ref, lab_ref, gy_lo, gy_hi, gz_lo, gz_hi):
    mob = 1.0 + 2.0 * pore_ref[i].astype(F32)
    lab = lab_ref[i].astype(F32)
    mob_n = _neighbours(mob, _yrow(gy_lo, 0, i), _yrow(gy_hi, 0, i), _zcol(gz_lo, 0, i), _zcol(gz_hi, 0, i))
    lab_n = _neighbours(lab, _yrow(gy_lo, 1, i), _yrow(gy_hi, 1, i), _zcol(gz_lo, 1, i), _zcol(gz_hi, 1, i))
    return mob, lab, mob_n, _faces(mob, lab, mob_n, lab_n)


def _sweep(m, lower, pivots, ratios, source):
    ys = [None] * m
    prev = None
    for r in range(m - 1):
        num = source[r]
        if num is None:
            if prev is None:
                continue
            num = -(lower[r] * prev)
        elif prev is not None:
            num = num - lower[r] * prev
        ys[r] = num / pivots[r]
        prev = ys[r]
    xs = [None] * m
    prev = None
    for r in range(m - 2, -1, -1):
        if prev is None:
            xs[r] = ys[r]
        elif ys[r] is None:
            xs[r] = -(ratios[r] * prev)
        else:
            xs[r] = ys[r] - ratios[r] * prev
        prev = xs[r]
    return xs


def _factor_kernel(cs, lo_i, hi_i, pore_ref, lab_ref, bx_ref, fac_ref, lr_ref, rows_ref):
    bx_lo, bx_hi = bx_ref.at[lo_i], bx_ref.at[hi_i]
    m = pore_ref.shape[0]
    zero = jnp.zeros(pore_ref.shape[1:], F32)
    mobs = [1.0 + 2.0 * pore_ref[r].astype(F32) for r in range(m)]
    labs = [lab_ref[r].astype(F32) for r in range(m)]
    m_ext = [bx_lo[0]] + mobs + [bx_hi[0]]
    l_ext = [bx_lo[1]] + labs + [bx_hi[1]]
    w_ext = [0.5 * (1.0 + x) for x in m_ext]
    faces = [face_value(m_ext[k], m_ext[k + 1], l_ext[k], l_ext[k + 1]) for k in range(m + 1)]
    bands = {"f": ([], [], []), "a": ([], [], [])}
    for r in range(m):
        bf, ff = faces[r], faces[r + 1]
        w = w_ext[r + 1]
        main = 1.0 + cs * w * (bf + ff)
        bands["f"][0].append(-cs * bf * w_ext[r])
        bands["f"][1].append(main)
        bands["f"][2].append(-cs * ff * w_ext[r + 2])
        bands["a"][0].append(-cs * bf * w)
        bands["a"][1].append(main)
        bands["a"][2].append(-cs * ff * w)

    for c, key in ((0, "f"), (1, "a")):
        lower, main, upper = bands[key]
        pivots, ratios = [], []
        prev = None
        for r in range(m - 1):
            piv = main[r] if prev is None else main[r] - lower[r] * prev
            rat = upper[r] / piv
            pivots.append(piv)
            ratios.append(rat)
            prev = rat
        left_src = [lower[0]] + [None] * (m - 1)
        right_src = [None] * (m - 2) + [upper[m - 2], None]
        left = _sweep(m, lower, pivots, ratios, left_src)
        right = _sweep(m, lower, pivots, ratios, right_src)
        for r in range(m):
            fac_ref[c, 0, r] = lower[r]
            fac_ref[c, 1, r] = ratios[r] if r < m - 1 else zero
            fac_ref[c, 2, r] = pivots[r] if r < m - 1 else zero + 1.0
            lr_ref[c, 0, r] = left[r] if r < m - 1 else zero
            lr_ref[c, 1, r] = right[r] if r < m - 1 else zero - 1.0
        last_lower = lower[m - 1]
        rows_ref[c, 0] = last_lower * left[m - 2]
        rows_ref[c, 1] = main[m - 1] - last_lower * right[m - 2]
        rows_ref[c, 2] = upper[m - 1]
        rows_ref[c, 3] = left[0]
        rows_ref[c, 4] = right[0]


def _reduced_solve(gs, gv, voff, c, n, pos):
    slot = [(pos - p + n) % n for p in range(n)]
    g = [[gs[slot[p], c, k] for k in range(5)] for p in range(n)]
    v = [[gv[slot[p], c, voff + k] for k in range(2)] for p in range(n)]
    lower = [-g[p][0] for p in range(n)]
    main = [g[p][1] - g[p][2] * g[(p + 1) % n][3] for p in range(n)]
    upper = [-g[p][2] * g[(p + 1) % n][4] for p in range(n)]
    src = [v[p][0] - g[p][2] * v[(p + 1) % n][1] for p in range(n)]
    k_in = n - 1
    pivots, ratios = [], []
    prev = None
    for r in range(k_in):
        piv = main[r] if prev is None else main[r] - lower[r] * prev
        rat = upper[r] / piv
        pivots.append(piv)
        ratios.append(rat)
        prev = rat

    def apply(source):
        ys = []
        prev = None
        for r in range(k_in):
            num = source[r] if prev is None else source[r] - lower[r] * prev
            ys.append(num / pivots[r])
            prev = ys[-1]
        xs = [None] * k_in
        prev = None
        for r in range(k_in - 1, -1, -1):
            xs[r] = ys[r] if prev is None else ys[r] - ratios[r] * prev
            prev = xs[r]
        return xs

    coupling = []
    for r in range(k_in):
        term = None
        if r == 0:
            term = lower[0]
        if r == k_in - 1:
            term = upper[k_in - 1] if term is None else term + upper[k_in - 1]
        coupling.append(term if term is not None else jnp.zeros_like(lower[0]))
    linked = apply(coupling)
    closing = main[k_in] - lower[k_in] * linked[k_in - 1] - upper[k_in] * linked[0]
    inner = apply(src[:k_in])
    sep = (src[k_in] - lower[k_in] * inner[k_in - 1] - upper[k_in] * inner[0]) / closing
    return [inner[r] - linked[r] * sep for r in range(k_in)] + [sep]


def _combine_kernel(n, stacked, edge_of, pos_ref, *refs):
    gs_parts, gv_parts = refs[:n], refs[n : 2 * n]
    lr_ref, loc_ref = refs[2 * n], refs[2 * n + 1]
    refs = refs[2 * n + 2 :]
    if stacked:
        out_ref = refs[0]
        outs = (out_ref.at[0], out_ref.at[1])
        rest = refs[1:]
    else:
        outs = refs[:2]
        rest = refs[2:]
    edge_outs, sep_ref, gs_ref, gv_ref = rest[:4], rest[4], rest[5], rest[6]
    edges = rest[7:11]
    for k in range(n):
        gs_ref[k] = gs_parts[k][...]
        gv_ref[k] = gv_parts[k][...]
    m = loc_ref.shape[1]
    p = pos_ref[0]
    for c in range(2):
        seps = _reduced_solve(gs_ref, gv_ref, 0, c, n, p)
        for q in range(n):
            sep_ref[q] = seps[q]
        own = sep_ref[p]
        prior = sep_ref[(p + n - 1) % n]
        for r in range(m):
            val = loc_ref[c, r] - lr_ref[c, 0, r] * prior - lr_ref[c, 1, r] * own
            outs[c][r] = val
            if c in edge_of:
                _write_edges(edges, edge_of[c], r, val)
    _flush_edges(edges, edge_outs, _parity(pos_ref))


def _edge_kernel(ctl_ref, vac_ref, pore_ref, lab_ref, y_a, y_b, z_a, z_b, bx_ref, *edges):
    m = vac_ref.shape[0]
    for r in range(m):
        mob = 1.0 + 2.0 * pore_ref[r].astype(F32)
        lab = lab_ref[r].astype(F32)
        for c, val in enumerate((mob, lab, vac_ref[r])):
            _write_edges(edges, c, r, val)
        if r == 0:
            bx_ref[0, 0] = mob
            bx_ref[0, 1] = lab
        if r == m - 1:
            bx_ref[1, 0] = mob
            bx_ref[1, 1] = lab
    _flush_edges(edges, (y_a, y_b, z_a, z_b), _parity(ctl_ref))


def _local_solves(fac_ref, srcs, loc_ref, vals_ref):
    m = loc_ref.shape[1]
    zero = jnp.zeros(loc_ref.shape[2:], F32)
    for c in range(2):
        lower = [fac_ref[c, 0, r] for r in range(m)]
        ratios = [fac_ref[c, 1, r] for r in range(m - 1)]
        pivots = [fac_ref[c, 2, r] for r in range(m - 1)]
        src = srcs[c]
        local = _sweep(m, lower, pivots, ratios, src[: m - 1] + [None])
        for r in range(m):
            loc_ref[c, r] = local[r] if r < m - 1 else zero
        vals_ref[c, 0] = src[m - 1] - lower[m - 1] * local[m - 2]
        vals_ref[c, 1] = local[0]


def _first_kernel(ctl_ref, vac_ref, cot_ref, pore_ref, lab_ref, fac_ref, gy_lo, gy_hi, gz_lo, gz_hi, loc_ref, vals_ref):
    gy_lo, gy_hi, gz_lo, gz_hi = _picks(ctl_ref, gy_lo, gy_hi, gz_lo, gz_hi)
    m = pore_ref.shape[0]
    srcs = ([], [cot_ref[r] for r in range(m)])
    for i in range(m):
        mob, _, mob_n, fc = _geo_row(i, pore_ref, lab_ref, gy_lo, gy_hi, gz_lo, gz_hi)
        w = 0.5 * (1.0 + mob)
        v = vac_ref[i]
        v_n = _neighbours(v, _yrow(gy_lo, 2, i), _yrow(gy_hi, 2, i), _zcol(gz_lo, 2, i), _zcol(gz_hi, 2, i))
        u_n = [0.5 * (1.0 + mn) * vn for mn, vn in zip(mob_n, v_n)]
        srcs[0].append(v + cross_rate * (1.0 * _flux(w * v, u_n, fc)))
    _local_solves(fac_ref, srcs, loc_ref, vals_ref)


def _second_kernel(ctl_ref, pore_ref, lab_ref, fa_ref, fac_ref, gy_lo, gy_hi, gz_lo, gz_hi,
                   hy_lo, hy_hi, hz_lo, hz_hi, loc_ref, vals_ref):
    gy_lo, gy_hi, gz_lo, gz_hi = _picks(ctl_ref, gy_lo, gy_hi, gz_lo, gz_hi)
    hy_lo, hy_hi, hz_lo, hz_hi = _picks(ctl_ref, hy_lo, hy_hi, hz_lo, hz_hi)
    m = pore_ref.shape[0]
    srcs = ([], [])
    for i in range(m):
        mob, _, mob_n, fc = _geo_row(i, pore_ref, lab_ref, gy_lo, gy_hi, gz_lo, gz_hi)
        w = 0.5 * (1.0 + mob)
        f1 = fa_ref[0, i]
        f_n = _neighbours(f1, _yrow(hy_lo, 0, i), _yrow(hy_hi, 0, i), _zcol(hz_lo, 0, i), _zcol(hz_hi, 0, i))
        u_n = [0.5 * (1.0 + mn) * fn for mn, fn in zip(mob_n, f_n)]
        srcs[0].append(f1 + cross_rate * (1.0 * _flux(w * f1, u_n, fc)))
        a1 = fa_ref[1, i]
        a_n = _neighbours(a1, _yrow(hy_lo, 1, i), _yrow(hy_hi, 1, i), _zcol(hz_lo, 1, i), _zcol(hz_hi, 1, i))
        srcs[1].append(a1 + cross_rate * (w * _flux(a1, a_n, fc)))
    _local_solves(fac_ref, srcs, loc_ref, vals_ref)


def _gradient_kernel(ctl_ref, pore_ref, lab_ref, a2_ref, gy_lo, gy_hi, gz_lo, gz_hi,
                     hy_lo, hy_hi, hz_lo, hz_hi, out_ref):
    gy_lo, gy_hi, gz_lo, gz_hi = _picks(ctl_ref, gy_lo, gy_hi, gz_lo, gz_hi)
    hy_lo, hy_hi, hz_lo, hz_hi = _picks(ctl_ref, hy_lo, hy_hi, hz_lo, hz_hi)
    m = pore_ref.shape[0]
    for i in range(m):
        mob, _, _, fc = _geo_row(i, pore_ref, lab_ref, gy_lo, gy_hi, gz_lo, gz_hi)
        w = 0.5 * (1.0 + mob)
        a2 = a2_ref[i]
        a_n = _neighbours(a2, _yrow(hy_lo, 0, i), _yrow(hy_hi, 0, i), _zcol(hz_lo, 0, i), _zcol(hz_hi, 0, i))
        out_ref[i] = a2 + cross_rate * (w * _flux(a2, a_n, fc))


def _halo_pairs(axis, periodic):
    count = lax.axis_size(axis)
    forward = [(i, i + 1) for i in range(count - 1)]
    if periodic:
        forward.append((count - 1, 0))
    backward = [(t, s) for s, t in forward]
    return forward, backward


def _exchange(first, last, axis, periodic):
    forward, backward = _halo_pairs(axis, periodic)
    lo = lax.ppermute(last, axis, forward)
    hi = lax.ppermute(first, axis, backward)
    return lo, hi


def _first_call(m, ny, nz):
    return pl.pallas_call(
        _first_kernel,
        out_shape=(
            jax.ShapeDtypeStruct((2, m, ny, nz), F32),
            jax.ShapeDtypeStruct((2, 2, ny, nz), F32),
        ),
        in_specs=[_smem()] + [_vmem()] * 9,
        out_specs=(_vmem(), _vmem()),
    )


def _combine_scratch(n, ny, nz):
    return [
        pltpu.VMEM((n, ny, nz), F32),
        pltpu.VMEM((n, 2, 5, ny, nz), F32),
        pltpu.VMEM((n, 2, 2, ny, nz), F32),
    ]


def _gather_blk(x):
    n = lax.axis_size("blk")
    parts = [x]
    for k in range(1, n):
        parts.append(lax.ppermute(x, "blk", [(j, (j + k) % n) for j in range(n)]))
    return parts


def _edge_shapes(chans, m, ny, nz):
    return (
        jax.ShapeDtypeStruct((chans, m, nz), F32),
        jax.ShapeDtypeStruct((chans, m, nz), F32),
        jax.ShapeDtypeStruct((chans, ny, m), F32),
        jax.ShapeDtypeStruct((chans, ny, m), F32),
    )


def _swap(x_a, x_b, axis):
    n = lax.axis_size(axis)
    pairs_a = [(i, i ^ 1) for i in range(n) if i ^ 1 < n]
    pairs_b = [(i, i + 1) for i in range(1, n - 1, 2)] + [(i + 1, i) for i in range(1, n - 1, 2)]
    recv_a = lax.ppermute(x_a, axis, pairs_a)
    recv_b = lax.ppermute(x_b, axis, pairs_b) if pairs_b else jnp.zeros_like(x_b)
    return recv_a, recv_b


def _yz_halos(y_a, y_b, z_a, z_b):
    return _swap(y_a, y_b, "gy") + _swap(z_a, z_b, "gz")


def _shards(vacancy, grain_label, pore_mask, cotangent):
    m, ny, nz = vacancy.shape
    n_blk = lax.axis_size("blk")
    cycle_step = float((m * n_blk) ** 2 // 64)
    shape = jax.ShapeDtypeStruct((m, ny, nz), F32)

    ctl = jnp.stack(
        [lax.axis_index("blk"), 1 - lax.axis_index("gy") % 2, 1 - lax.axis_index("gz") % 2]
    ).astype(jnp.int32)
    outs = pl.pallas_call(
        _edge_kernel,
        out_shape=_edge_shapes(3, m, ny, nz) + (jax.ShapeDtypeStruct((2, 2, ny, nz), F32),),
        in_specs=[_smem()] + [_vmem()] * 3,
        out_specs=tuple(_vmem() for _ in range(5)),
        scratch_shapes=_edge_scratch(3, m, ny, nz),
    )(ctl, vacancy, pore_mask, grain_label)
    if n_blk == 2:
        bx = lax.ppermute(outs[4], "blk", [(0, 1), (1, 0)])
        lo_i, hi_i = 1, 0
    else:
        bx_lo, bx_hi = _exchange(outs[4][0], outs[4][1], "blk", True)
        bx = jnp.stack([bx_lo, bx_hi])
        lo_i, hi_i = 0, 1
    gy_lo, gy_hi, gz_lo, gz_hi = _yz_halos(*outs[:4])

    fac, lr, rows = pl.pallas_call(
        lambda *r: _factor_kernel(cycle_step, lo_i, hi_i, *r),
        out_shape=(
            jax.ShapeDtypeStruct((2, 3, m, ny, nz), F32),
            jax.ShapeDtypeStruct((2, 2, m, ny, nz), F32),
            jax.ShapeDtypeStruct((2, 5, ny, nz), F32),
        ),
        in_specs=[_vmem()] * 3,
        out_specs=(_vmem(), _vmem(), _vmem()),
    )(pore_mask, grain_label, bx)
    gathered = _gather_blk(rows)

    loc, vals = _first_call(m, ny, nz)(
        ctl, vacancy, cotangent, pore_mask, grain_label, fac, gy_lo, gy_hi, gz_lo, gz_hi
    )
    gathered1 = _gather_blk(vals)
    pos = ctl

    outs = pl.pallas_call(
        lambda *r: _combine_kernel(n_blk, True, {0: 0, 1: 1}, *r),
        out_shape=(jax.ShapeDtypeStruct((2, m, ny, nz), F32),) + _edge_shapes(2, m, ny, nz),
        in_specs=[_smem()] + [_vmem()] * (2 * n_blk + 2),
        out_specs=tuple(_vmem() for _ in range(5)),
        scratch_shapes=_combine_scratch(n_blk, ny, nz) + _edge_scratch(2, m, ny, nz),
    )(pos, *gathered, *gathered1, lr, loc)
    fa = outs[0]

    hy_lo, hy_hi, hz_lo, hz_hi = _yz_halos(*outs[1:])
    loc2, vals2 = pl.pallas_call(
        _second_kernel,
        out_shape=(
            jax.ShapeDtypeStruct((2, m, ny, nz), F32),
            jax.ShapeDtypeStruct((2, 2, ny, nz), F32),
        ),
        in_specs=[_smem()] + [_vmem()] * 12,
        out_specs=(_vmem(), _vmem()),
    )(ctl, pore_mask, grain_label, fa, fac, gy_lo, gy_hi, gz_lo, gz_hi, hy_lo, hy_hi, hz_lo, hz_hi)

    gathered2 = _gather_blk(vals2)
    outs = pl.pallas_call(
        lambda *r: _combine_kernel(n_blk, False, {1: 0}, *r),
        out_shape=(shape, shape) + _edge_shapes(1, m, ny, nz),
        in_specs=[_smem()] + [_vmem()] * (2 * n_blk + 2),
        out_specs=tuple(_vmem() for _ in range(6)),
        scratch_shapes=_combine_scratch(n_blk, ny, nz) + _edge_scratch(1, m, ny, nz),
    )(pos, *gathered, *gathered2, lr, loc2)
    final_field, adjoint_two = outs[:2]

    a2_lo, a2_hi, a2z_lo, a2z_hi = _yz_halos(*outs[2:])
    gradient = pl.pallas_call(
        _gradient_kernel,
        out_shape=shape,
        in_specs=[_smem()] + [_vmem()] * 11,
        out_specs=_vmem(),
    )(ctl, pore_mask, grain_label, adjoint_two, gy_lo, gy_hi, gz_lo, gz_hi, a2_lo, a2_hi, a2z_lo, a2z_hi)
    return (final_field, gradient)


def solution(mesh):
    in_specs = (
        P("blk", "gy", "gz"),
        P("blk", "gy", "gz"),
        P("blk", "gy", "gz"),
        P("blk", "gy", "gz"),
    )
    out_specs = (P("blk", "gy", "gz"), P("blk", "gy", "gz"))
    fn = jax.shard_map(_shards, mesh=mesh, in_specs=in_specs, out_specs=out_specs, check_vma=False)
    if mesh.shape["blk"] > 4:
        return fn
    return fn
```

```python
import jax
import jax.numpy as jnp
from jax import lax
from jax.experimental import pallas as pl
from jax.experimental.pallas import tpu as pltpu
from jax.sharding import PartitionSpec as P


cross_rate = 0.0125
boundary_gain = 3.0
F32 = jnp.float32


def face_value(mobility_here, mobility_there, label_here, label_there):
    harmonic = 2.0 * mobility_here * mobility_there / (mobility_here + mobility_there)
    return harmonic * jnp.where(label_here != label_there, boundary_gain, 1.0)


def _vmem():
    return pl.BlockSpec(memory_space=pltpu.VMEM)


def _smem():
    return pl.BlockSpec(memory_space=pltpu.SMEM)


def _shift(x, edge, axis, up):
    n = x.shape[axis]
    idx = lax.broadcasted_iota(jnp.int32, x.shape, axis)
    edge = jnp.broadcast_to(edge, x.shape)
    if up:
        return jnp.where(idx == n - 1, edge, pltpu.roll(x, n - 1, axis))
    return jnp.where(idx == 0, edge, pltpu.roll(x, 1, axis))


def _neighbours(x, ylo, yhi, zlo, zhi):
    return (
        _shift(x, yhi, 0, True),
        _shift(x, ylo, 0, False),
        _shift(x, zhi, 1, True),
        _shift(x, zlo, 1, False),
    )


def _flux(u, u_n, faces):
    total = faces[0] * (u_n[0] - u)
    total = total + faces[1] * (u_n[1] - u)
    total = total + faces[2] * (u_n[2] - u)
    total = total + faces[3] * (u_n[3] - u)
    return total


def _yrow(ref, c, i):
    return ref[c, pl.ds(i, 1), :]


def _zcol(ref, c, i):
    return ref[c, :, pl.ds(i, 1)]


def _write_edges(edges, c, r, val):
    y_first, y_last, z_first, z_last = edges
    ny, nz = val.shape
    y_first[c, pl.ds(r, 1), :] = val[0:1, :]
    y_last[c, pl.ds(r, 1), :] = val[ny - 1 : ny, :]
    z_first[c, :, pl.ds(r, 1)] = val[:, 0:1]
    z_last[c, :, pl.ds(r, 1)] = val[:, nz - 1 : nz]


def _flush_edges(scratch, outs, par):
    y_first, y_last, z_first, z_last = scratch
    y_a, y_b, z_a, z_b = outs
    even_y, even_z = par
    for even, first, last, out_a, out_b in ((even_y, y_first, y_last, y_a, y_b), (even_z, z_first, z_last, z_a, z_b)):

        @pl.when(even)
        def _():
            out_a[...] = last[...]
            out_b[...] = first[...]

        @pl.when(jnp.logical_not(even))
        def _():
            out_a[...] = first[...]
            out_b[...] = last[...]


def _edge_scratch(chans, m, ny, nz):
    return [
        pltpu.VMEM((chans, m, nz), F32),
        pltpu.VMEM((chans, m, nz), F32),
        pltpu.VMEM((chans, ny, m), F32),
        pltpu.VMEM((chans, ny, m), F32),
    ]


class _Pick:
    def __init__(self, a, b, use_b):
        self.a, self.b, self.use_b = a, b, use_b

    def __getitem__(self, idx):
        return jnp.where(self.use_b, self.b[idx], self.a[idx])


def _parity(ctl_ref):
    return ctl_ref[1] == 1, ctl_ref[2] == 1


def _picks(ctl_ref, y_a, y_b, z_a, z_b):
    even_y, even_z = _parity(ctl_ref)
    return (
        _Pick(y_a, y_b, even_y),
        _Pick(y_a, y_b, jnp.logical_not(even_y)),
        _Pick(z_a, z_b, even_z),
        _Pick(z_a, z_b, jnp.logical_not(even_z)),
    )


def _geo_row(i, pore_ref, lab_ref, gy_lo, gy_hi, gz_lo, gz_hi):
    mob = 1.0 + 2.0 * pore_ref[i].astype(F32)
    lab = lab_ref[i].astype(F32)
    ny, nz = mob.shape
    m_ylo, m_yhi, m_zlo, m_zhi = _yrow(gy_lo, 0, i), _yrow(gy_hi, 0, i), _zcol(gz_lo, 0, i), _zcol(gz_hi, 0, i)
    l_ylo, l_yhi, l_zlo, l_zhi = _yrow(gy_lo, 1, i), _yrow(gy_hi, 1, i), _zcol(gz_lo, 1, i), _zcol(gz_hi, 1, i)
    mob_n = _neighbours(mob, m_ylo, m_yhi, m_zlo, m_zhi)
    lab_yp = _shift(lab, l_yhi, 0, True)
    lab_zp = _shift(lab, l_zhi, 1, True)
    face_yp = face_value(mob, mob_n[0], lab, lab_yp)
    face_zp = face_value(mob, mob_n[2], lab, lab_zp)
    face_ym = _shift(face_yp, face_value(m_ylo, mob[0:1, :], l_ylo, lab[0:1, :]), 0, False)
    face_zm = _shift(face_zp, face_value(m_zlo, mob[:, 0:1], l_zlo, lab[:, 0:1]), 1, False)
    return mob, lab, mob_n, [face_yp, face_ym, face_zp, face_zm]


def _sweep(m, lower, inv_pivots, ratios, source):
    ys = [None] * m
    prev = None
    for r in range(m - 1):
        num = source[r]
        if num is None:
            if prev is None:
                continue
            num = -(lower[r] * prev)
        elif prev is not None:
            num = num - lower[r] * prev
        ys[r] = num * inv_pivots[r]
        prev = ys[r]
    xs = [None] * m
    prev = None
    for r in range(m - 2, -1, -1):
        if prev is None:
            xs[r] = ys[r]
        elif ys[r] is None:
            xs[r] = -(ratios[r] * prev)
        else:
            xs[r] = ys[r] - ratios[r] * prev
        prev = xs[r]
    return xs


def _factor_kernel(cs, lo_i, hi_i, pore_ref, lab_ref, bx_ref, fac_ref, lr_ref, rows_ref):
    bx_lo, bx_hi = bx_ref.at[lo_i], bx_ref.at[hi_i]
    m = pore_ref.shape[0]
    zero = jnp.zeros(pore_ref.shape[1:], F32)
    mobs = [1.0 + 2.0 * pore_ref[r].astype(F32) for r in range(m)]
    labs = [lab_ref[r].astype(F32) for r in range(m)]
    m_ext = [bx_lo[0]] + mobs + [bx_hi[0]]
    l_ext = [bx_lo[1]] + labs + [bx_hi[1]]
    w_ext = [0.5 * (1.0 + x) for x in m_ext]
    faces = [face_value(m_ext[k], m_ext[k + 1], l_ext[k], l_ext[k + 1]) for k in range(m + 1)]
    bands = {"f": ([], [], []), "a": ([], [], [])}
    for r in range(m):
        bf, ff = faces[r], faces[r + 1]
        w = w_ext[r + 1]
        main = 1.0 + cs * w * (bf + ff)
        bands["f"][0].append(-cs * bf * w_ext[r])
        bands["f"][1].append(main)
        bands["f"][2].append(-cs * ff * w_ext[r + 2])
        bands["a"][0].append(-cs * bf * w)
        bands["a"][1].append(main)
        bands["a"][2].append(-cs * ff * w)

    for c, key in ((0, "f"), (1, "a")):
        lower, main, upper = bands[key]
        pivots, ratios = [], []
        prev = None
        for r in range(m - 1):
            piv = main[r] if prev is None else main[r] - lower[r] * prev
            rat = upper[r] / piv
            pivots.append(piv)
            ratios.append(rat)
            prev = rat
        inv_piv = [1.0 / x for x in pivots]
        left_src = [lower[0]] + [None] * (m - 1)
        right_src = [None] * (m - 2) + [upper[m - 2], None]
        left = _sweep(m, lower, inv_piv, ratios, left_src)
        right = _sweep(m, lower, inv_piv, ratios, right_src)
        for r in range(m):
            fac_ref[c, 0, r] = lower[r]
            fac_ref[c, 1, r] = ratios[r] if r < m - 1 else zero
            fac_ref[c, 2, r] = inv_piv[r] if r < m - 1 else zero + 1.0
            lr_ref[c, 0, r] = left[r] if r < m - 1 else zero
            lr_ref[c, 1, r] = right[r] if r < m - 1 else zero - 1.0
        last_lower = lower[m - 1]
        rows_ref[c, 0] = last_lower * left[m - 2]
        rows_ref[c, 1] = main[m - 1] - last_lower * right[m - 2]
        rows_ref[c, 2] = upper[m - 1]
        rows_ref[c, 3] = left[0]
        rows_ref[c, 4] = right[0]


def _reduced_solve(gs, gv, voff, c, n, pos):
    slot = [(pos - p + n) % n for p in range(n)]
    g = [[gs[slot[p], c, k] for k in range(5)] for p in range(n)]
    v = [[gv[slot[p], c, voff + k] for k in range(2)] for p in range(n)]
    lower = [-g[p][0] for p in range(n)]
    main = [g[p][1] - g[p][2] * g[(p + 1) % n][3] for p in range(n)]
    upper = [-g[p][2] * g[(p + 1) % n][4] for p in range(n)]
    src = [v[p][0] - g[p][2] * v[(p + 1) % n][1] for p in range(n)]
    k_in = n - 1
    pivots, ratios = [], []
    prev = None
    for r in range(k_in):
        piv = main[r] if prev is None else main[r] - lower[r] * prev
        rat = upper[r] / piv
        pivots.append(piv)
        ratios.append(rat)
        prev = rat

    def apply(source):
        ys = []
        prev = None
        for r in range(k_in):
            num = source[r] if prev is None else source[r] - lower[r] * prev
            ys.append(num / pivots[r])
            prev = ys[-1]
        xs = [None] * k_in
        prev = None
        for r in range(k_in - 1, -1, -1):
            xs[r] = ys[r] if prev is None else ys[r] - ratios[r] * prev
            prev = xs[r]
        return xs

    coupling = []
    for r in range(k_in):
        term = None
        if r == 0:
            term = lower[0]
        if r == k_in - 1:
            term = upper[k_in - 1] if term is None else term + upper[k_in - 1]
        coupling.append(term if term is not None else jnp.zeros_like(lower[0]))
    linked = apply(coupling)
    closing = main[k_in] - lower[k_in] * linked[k_in - 1] - upper[k_in] * linked[0]
    inner = apply(src[:k_in])
    sep = (src[k_in] - lower[k_in] * inner[k_in - 1] - upper[k_in] * inner[0]) / closing
    return [inner[r] - linked[r] * sep for r in range(k_in)] + [sep]


def _combine_kernel(n, stacked, edge_of, pos_ref, *refs):
    gs_parts, gv_parts = refs[:n], refs[n : 2 * n]
    lr_ref, loc_ref = refs[2 * n], refs[2 * n + 1]
    refs = refs[2 * n + 2 :]
    if stacked:
        out_ref = refs[0]
        outs = (out_ref.at[0], out_ref.at[1])
        rest = refs[1:]
    else:
        outs = refs[:2]
        rest = refs[2:]
    edge_outs, sep_ref, gs_ref, gv_ref = rest[:4], rest[4], rest[5], rest[6]
    edges = rest[7:11]
    for k in range(n):
        gs_ref[k] = gs_parts[k][...]
        gv_ref[k] = gv_parts[k][...]
    m = loc_ref.shape[1]
    p = pos_ref[0]
    for c in range(2):
        seps = _reduced_solve(gs_ref, gv_ref, 0, c, n, p)
        for q in range(n):
            sep_ref[q] = seps[q]
        own = sep_ref[p]
        prior = sep_ref[(p + n - 1) % n]
        for r in range(m):
            val = loc_ref[c, r] - lr_ref[c, 0, r] * prior - lr_ref[c, 1, r] * own
            outs[c][r] = val
            if c in edge_of:
                _write_edges(edges, edge_of[c], r, val)
    _flush_edges(edges, edge_outs, _parity(pos_ref))


def _edge_kernel(ctl_ref, vac_ref, pore_ref, lab_ref, y_a, y_b, z_a, z_b, bx_ref, *edges):
    m = vac_ref.shape[0]
    for r in range(m):
        mob = 1.0 + 2.0 * pore_ref[r].astype(F32)
        lab = lab_ref[r].astype(F32)
        for c, val in enumerate((mob, lab, vac_ref[r])):
            _write_edges(edges, c, r, val)
        if r == 0:
            bx_ref[0, 0] = mob
            bx_ref[0, 1] = lab
        if r == m - 1:
            bx_ref[1, 0] = mob
            bx_ref[1, 1] = lab
    _flush_edges(edges, (y_a, y_b, z_a, z_b), _parity(ctl_ref))


def _local_solves(fac_ref, srcs, loc_ref, vals_ref):
    m = loc_ref.shape[1]
    zero = jnp.zeros(loc_ref.shape[2:], F32)
    for c in range(2):
        lower = [fac_ref[c, 0, r] for r in range(m)]
        ratios = [fac_ref[c, 1, r] for r in range(m - 1)]
        pivots = [fac_ref[c, 2, r] for r in range(m - 1)]
        src = srcs[c]
        local = _sweep(m, lower, pivots, ratios, src[: m - 1] + [None])
        for r in range(m):
            loc_ref[c, r] = local[r] if r < m - 1 else zero
        vals_ref[c, 0] = src[m - 1] - lower[m - 1] * local[m - 2]
        vals_ref[c, 1] = local[0]


def _first_kernel(ctl_ref, vac_ref, cot_ref, pore_ref, lab_ref, fac_ref, gy_lo, gy_hi, gz_lo, gz_hi, loc_ref, vals_ref):
    gy_lo, gy_hi, gz_lo, gz_hi = _picks(ctl_ref, gy_lo, gy_hi, gz_lo, gz_hi)
    m = pore_ref.shape[0]
    srcs = ([], [cot_ref[r] for r in range(m)])
    for i in range(m):
        mob, _, mob_n, fc = _geo_row(i, pore_ref, lab_ref, gy_lo, gy_hi, gz_lo, gz_hi)
        w = 0.5 * (1.0 + mob)
        v = vac_ref[i]
        v_n = _neighbours(v, _yrow(gy_lo, 2, i), _yrow(gy_hi, 2, i), _zcol(gz_lo, 2, i), _zcol(gz_hi, 2, i))
        u_n = [0.5 * (1.0 + mn) * vn for mn, vn in zip(mob_n, v_n)]
        srcs[0].append(v + cross_rate * (1.0 * _flux(w * v, u_n, fc)))
    _local_solves(fac_ref, srcs, loc_ref, vals_ref)


def _second_kernel(ctl_ref, pore_ref, lab_ref, fa_ref, fac_ref, gy_lo, gy_hi, gz_lo, gz_hi,
                   hy_lo, hy_hi, hz_lo, hz_hi, loc_ref, vals_ref):
    gy_lo, gy_hi, gz_lo, gz_hi = _picks(ctl_ref, gy_lo, gy_hi, gz_lo, gz_hi)
    hy_lo, hy_hi, hz_lo, hz_hi = _picks(ctl_ref, hy_lo, hy_hi, hz_lo, hz_hi)
    m = pore_ref.shape[0]
    srcs = ([], [])
    for i in range(m):
        mob, _, mob_n, fc = _geo_row(i, pore_ref, lab_ref, gy_lo, gy_hi, gz_lo, gz_hi)
        w = 0.5 * (1.0 + mob)
        f1 = fa_ref[0, i]
        f_n = _neighbours(f1, _yrow(hy_lo, 0, i), _yrow(hy_hi, 0, i), _zcol(hz_lo, 0, i), _zcol(hz_hi, 0, i))
        u_n = [0.5 * (1.0 + mn) * fn for mn, fn in zip(mob_n, f_n)]
        srcs[0].append(f1 + cross_rate * (1.0 * _flux(w * f1, u_n, fc)))
        a1 = fa_ref[1, i]
        a_n = _neighbours(a1, _yrow(hy_lo, 1, i), _yrow(hy_hi, 1, i), _zcol(hz_lo, 1, i), _zcol(hz_hi, 1, i))
        srcs[1].append(a1 + cross_rate * (w * _flux(a1, a_n, fc)))
    _local_solves(fac_ref, srcs, loc_ref, vals_ref)


def _gradient_kernel(ctl_ref, pore_ref, lab_ref, a2_ref, gy_lo, gy_hi, gz_lo, gz_hi,
                     hy_lo, hy_hi, hz_lo, hz_hi, out_ref):
    gy_lo, gy_hi, gz_lo, gz_hi = _picks(ctl_ref, gy_lo, gy_hi, gz_lo, gz_hi)
    hy_lo, hy_hi, hz_lo, hz_hi = _picks(ctl_ref, hy_lo, hy_hi, hz_lo, hz_hi)
    m = pore_ref.shape[0]
    for i in range(m):
        mob, _, _, fc = _geo_row(i, pore_ref, lab_ref, gy_lo, gy_hi, gz_lo, gz_hi)
        w = 0.5 * (1.0 + mob)
        a2 = a2_ref[i]
        a_n = _neighbours(a2, _yrow(hy_lo, 0, i), _yrow(hy_hi, 0, i), _zcol(hz_lo, 0, i), _zcol(hz_hi, 0, i))
        out_ref[i] = a2 + cross_rate * (w * _flux(a2, a_n, fc))


def _halo_pairs(axis, periodic):
    count = lax.axis_size(axis)
    forward = [(i, i + 1) for i in range(count - 1)]
    if periodic:
        forward.append((count - 1, 0))
    backward = [(t, s) for s, t in forward]
    return forward, backward


def _exchange(first, last, axis, periodic):
    forward, backward = _halo_pairs(axis, periodic)
    lo = lax.ppermute(last, axis, forward)
    hi = lax.ppermute(first, axis, backward)
    return lo, hi


def _first_call(m, ny, nz):
    return pl.pallas_call(
        _first_kernel,
        out_shape=(
            jax.ShapeDtypeStruct((2, m, ny, nz), F32),
            jax.ShapeDtypeStruct((2, 2, ny, nz), F32),
        ),
        in_specs=[_smem()] + [_vmem()] * 9,
        out_specs=(_vmem(), _vmem()),
    )


def _combine_scratch(n, ny, nz):
    return [
        pltpu.VMEM((n, ny, nz), F32),
        pltpu.VMEM((n, 2, 5, ny, nz), F32),
        pltpu.VMEM((n, 2, 2, ny, nz), F32),
    ]


def _gather_blk(x):
    n = lax.axis_size("blk")
    parts = [x]
    for k in range(1, n):
        parts.append(lax.ppermute(x, "blk", [(j, (j + k) % n) for j in range(n)]))
    return parts


def _edge_shapes(chans, m, ny, nz):
    return (
        jax.ShapeDtypeStruct((chans, m, nz), F32),
        jax.ShapeDtypeStruct((chans, m, nz), F32),
        jax.ShapeDtypeStruct((chans, ny, m), F32),
        jax.ShapeDtypeStruct((chans, ny, m), F32),
    )


def _swap(x_a, x_b, axis):
    n = lax.axis_size(axis)
    pairs_a = [(i, i ^ 1) for i in range(n) if i ^ 1 < n]
    pairs_b = [(i, i + 1) for i in range(1, n - 1, 2)] + [(i + 1, i) for i in range(1, n - 1, 2)]
    recv_a = lax.ppermute(x_a, axis, pairs_a)
    recv_b = lax.ppermute(x_b, axis, pairs_b) if pairs_b else jnp.zeros_like(x_b)
    return recv_a, recv_b


def _yz_halos(y_a, y_b, z_a, z_b):
    return _swap(y_a, y_b, "gy") + _swap(z_a, z_b, "gz")


def _shards(vacancy, grain_label, pore_mask, cotangent):
    m, ny, nz = vacancy.shape
    n_blk = lax.axis_size("blk")
    cycle_step = float((m * n_blk) ** 2 // 64)
    shape = jax.ShapeDtypeStruct((m, ny, nz), F32)

    ctl = jnp.stack(
        [lax.axis_index("blk"), 1 - lax.axis_index("gy") % 2, 1 - lax.axis_index("gz") % 2]
    ).astype(jnp.int32)
    outs = pl.pallas_call(
        _edge_kernel,
        out_shape=_edge_shapes(3, m, ny, nz) + (jax.ShapeDtypeStruct((2, 2, ny, nz), F32),),
        in_specs=[_smem()] + [_vmem()] * 3,
        out_specs=tuple(_vmem() for _ in range(5)),
        scratch_shapes=_edge_scratch(3, m, ny, nz),
    )(ctl, vacancy, pore_mask, grain_label)
    if n_blk == 2:
        bx = lax.ppermute(outs[4], "blk", [(0, 1), (1, 0)])
        lo_i, hi_i = 1, 0
    else:
        bx_lo, bx_hi = _exchange(outs[4][0], outs[4][1], "blk", True)
        bx = jnp.stack([bx_lo, bx_hi])
        lo_i, hi_i = 0, 1
    gy_lo, gy_hi, gz_lo, gz_hi = _yz_halos(*outs[:4])

    fac, lr, rows = pl.pallas_call(
        lambda *r: _factor_kernel(cycle_step, lo_i, hi_i, *r),
        out_shape=(
            jax.ShapeDtypeStruct((2, 3, m, ny, nz), F32),
            jax.ShapeDtypeStruct((2, 2, m, ny, nz), F32),
            jax.ShapeDtypeStruct((2, 5, ny, nz), F32),
        ),
        in_specs=[_vmem()] * 3,
        out_specs=(_vmem(), _vmem(), _vmem()),
    )(pore_mask, grain_label, bx)
    gathered = _gather_blk(rows)

    loc, vals = _first_call(m, ny, nz)(
        ctl, vacancy, cotangent, pore_mask, grain_label, fac, gy_lo, gy_hi, gz_lo, gz_hi
    )
    gathered1 = _gather_blk(vals)
    pos = ctl

    outs = pl.pallas_call(
        lambda *r: _combine_kernel(n_blk, True, {0: 0, 1: 1}, *r),
        out_shape=(jax.ShapeDtypeStruct((2, m, ny, nz), F32),) + _edge_shapes(2, m, ny, nz),
        in_specs=[_smem()] + [_vmem()] * (2 * n_blk + 2),
        out_specs=tuple(_vmem() for _ in range(5)),
        scratch_shapes=_combine_scratch(n_blk, ny, nz) + _edge_scratch(2, m, ny, nz),
    )(pos, *gathered, *gathered1, lr, loc)
    fa = outs[0]

    hy_lo, hy_hi, hz_lo, hz_hi = _yz_halos(*outs[1:])
    loc2, vals2 = pl.pallas_call(
        _second_kernel,
        out_shape=(
            jax.ShapeDtypeStruct((2, m, ny, nz), F32),
            jax.ShapeDtypeStruct((2, 2, ny, nz), F32),
        ),
        in_specs=[_smem()] + [_vmem()] * 12,
        out_specs=(_vmem(), _vmem()),
    )(ctl, pore_mask, grain_label, fa, fac, gy_lo, gy_hi, gz_lo, gz_hi, hy_lo, hy_hi, hz_lo, hz_hi)

    gathered2 = _gather_blk(vals2)
    outs = pl.pallas_call(
        lambda *r: _combine_kernel(n_blk, False, {1: 0}, *r),
        out_shape=(shape, shape) + _edge_shapes(1, m, ny, nz),
        in_specs=[_smem()] + [_vmem()] * (2 * n_blk + 2),
        out_specs=tuple(_vmem() for _ in range(6)),
        scratch_shapes=_combine_scratch(n_blk, ny, nz) + _edge_scratch(1, m, ny, nz),
    )(pos, *gathered, *gathered2, lr, loc2)
    final_field, adjoint_two = outs[:2]

    a2_lo, a2_hi, a2z_lo, a2z_hi = _yz_halos(*outs[2:])
    gradient = pl.pallas_call(
        _gradient_kernel,
        out_shape=shape,
        in_specs=[_smem()] + [_vmem()] * 11,
        out_specs=_vmem(),
    )(ctl, pore_mask, grain_label, adjoint_two, gy_lo, gy_hi, gz_lo, gz_hi, a2_lo, a2_hi, a2z_lo, a2z_hi)
    return (final_field, gradient)


def solution(mesh):
    in_specs = (
        P("blk", "gy", "gz"),
        P("blk", "gy", "gz"),
        P("blk", "gy", "gz"),
        P("blk", "gy", "gz"),
    )
    out_specs = (P("blk", "gy", "gz"), P("blk", "gy", "gz"))
    fn = jax.shard_map(_shards, mesh=mesh, in_specs=in_specs, out_specs=out_specs, check_vma=False)
    if mesh.shape["blk"] > 4:
        return fn
    return fn
```

```python
import jax
import jax.numpy as jnp
from jax import lax
from jax.experimental import pallas as pl
from jax.experimental.pallas import tpu as pltpu
from jax.sharding import PartitionSpec as P


cross_rate = 0.0125
boundary_gain = 3.0
F32 = jnp.float32


def face_value(mobility_here, mobility_there, label_here, label_there):
    harmonic = 2.0 * mobility_here * mobility_there / (mobility_here + mobility_there)
    return harmonic * jnp.where(label_here != label_there, boundary_gain, 1.0)


def _kernel_call(*args, **kwargs):
    return pl.pallas_call(*args, **kwargs)


def _vmem():
    return pl.BlockSpec(memory_space=pltpu.VMEM)


def _smem():
    return pl.BlockSpec(memory_space=pltpu.SMEM)


def _shift(x, edge, axis, up):
    n = x.shape[axis]
    idx = lax.broadcasted_iota(jnp.int32, x.shape, axis)
    edge = jnp.broadcast_to(edge, x.shape)
    if up:
        return jnp.where(idx == n - 1, edge, pltpu.roll(x, n - 1, axis))
    return jnp.where(idx == 0, edge, pltpu.roll(x, 1, axis))


def _neighbours(x, ylo, yhi, zlo, zhi):
    return (
        _shift(x, yhi, 0, True),
        _shift(x, ylo, 0, False),
        _shift(x, zhi, 1, True),
        _shift(x, zlo, 1, False),
    )


def _faces(mob, lab, mob_n, lab_n):
    ups = (True, False, True, False)
    out = []
    for up, mn, ln in zip(ups, mob_n, lab_n):
        if up:
            out.append(face_value(mob, mn, lab, ln))
        else:
            out.append(face_value(mn, mob, ln, lab))
    return out


def _flux(u, u_n, faces):
    total = faces[0] * (u_n[0] - u)
    total = total + faces[1] * (u_n[1] - u)
    total = total + faces[2] * (u_n[2] - u)
    total = total + faces[3] * (u_n[3] - u)
    return total


def _yrow(ref, c, i):
    return ref[c, pl.ds(i, 1), :]


def _zcol(ref, c, i):
    return ref[c, :, pl.ds(i, 1)]


def _write_edges(edges, c, r, val):
    y_first, y_last, z_first, z_last = edges
    ny, nz = val.shape
    y_first[c, pl.ds(r, 1), :] = val[0:1, :]
    y_last[c, pl.ds(r, 1), :] = val[ny - 1 : ny, :]
    z_first[c, :, pl.ds(r, 1)] = val[:, 0:1]
    z_last[c, :, pl.ds(r, 1)] = val[:, nz - 1 : nz]


def _flush_edges(scratch, outs, par):
    y_first, y_last, z_first, z_last = scratch
    y_a, y_b, z_a, z_b = outs
    even_y, even_z = par
    for even, first, last, out_a, out_b in ((even_y, y_first, y_last, y_a, y_b), (even_z, z_first, z_last, z_a, z_b)):

        @pl.when(even)
        def _():
            out_a[...] = last[...]
            out_b[...] = first[...]

        @pl.when(jnp.logical_not(even))
        def _():
            out_a[...] = first[...]
            out_b[...] = last[...]


def _edge_scratch(chans, m, ny, nz):
    return [
        pltpu.VMEM((chans, m, nz), F32),
        pltpu.VMEM((chans, m, nz), F32),
        pltpu.VMEM((chans, ny, m), F32),
        pltpu.VMEM((chans, ny, m), F32),
    ]


class _Pick:
    def __init__(self, a, b, use_b):
        self.a, self.b, self.use_b = a, b, use_b

    def __getitem__(self, idx):
        return jnp.where(self.use_b, self.b[idx], self.a[idx])


def _parity(ctl_ref):
    return ctl_ref[1] == 1, ctl_ref[2] == 1


def _picks(ctl_ref, y_a, y_b, z_a, z_b):
    even_y, even_z = _parity(ctl_ref)
    return (
        _Pick(y_a, y_b, even_y),
        _Pick(y_a, y_b, jnp.logical_not(even_y)),
        _Pick(z_a, z_b, even_z),
        _Pick(z_a, z_b, jnp.logical_not(even_z)),
    )


def _geo_row(i, pore_ref, lab_ref, gy_lo, gy_hi, gz_lo, gz_hi):
    mob = 1.0 + 2.0 * pore_ref[i].astype(F32)
    lab = lab_ref[i].astype(F32)
    mob_n = _neighbours(mob, _yrow(gy_lo, 0, i), _yrow(gy_hi, 0, i), _zcol(gz_lo, 0, i), _zcol(gz_hi, 0, i))
    lab_n = _neighbours(lab, _yrow(gy_lo, 1, i), _yrow(gy_hi, 1, i), _zcol(gz_lo, 1, i), _zcol(gz_hi, 1, i))
    return mob, lab, mob_n, _faces(mob, lab, mob_n, lab_n)


def _sweep(m, lower, inv_pivots, ratios, source):
    ys = [None] * m
    prev = None
    for r in range(m - 1):
        num = source[r]
        if num is None:
            if prev is None:
                continue
            num = -(lower[r] * prev)
        elif prev is not None:
            num = num - lower[r] * prev
        ys[r] = num * inv_pivots[r]
        prev = ys[r]
    xs = [None] * m
    prev = None
    for r in range(m - 2, -1, -1):
        if prev is None:
            xs[r] = ys[r]
        elif ys[r] is None:
            xs[r] = -(ratios[r] * prev)
        else:
            xs[r] = ys[r] - ratios[r] * prev
        prev = xs[r]
    return xs


def _factor_kernel(cs, lo_i, hi_i, pore_ref, lab_ref, bx_ref, fac_ref, lr_ref, rows_ref):
    bx_lo, bx_hi = bx_ref.at[lo_i], bx_ref.at[hi_i]
    m = pore_ref.shape[0]
    zero = jnp.zeros(pore_ref.shape[1:], F32)
    mobs = [1.0 + 2.0 * pore_ref[r].astype(F32) for r in range(m)]
    labs = [lab_ref[r].astype(F32) for r in range(m)]
    m_ext = [bx_lo[0]] + mobs + [bx_hi[0]]
    l_ext = [bx_lo[1]] + labs + [bx_hi[1]]
    w_ext = [0.5 * (1.0 + x) for x in m_ext]
    faces = [face_value(m_ext[k], m_ext[k + 1], l_ext[k], l_ext[k + 1]) for k in range(m + 1)]
    bands = {"f": ([], [], []), "a": ([], [], [])}
    for r in range(m):
        bf, ff = faces[r], faces[r + 1]
        w = w_ext[r + 1]
        main = 1.0 + cs * w * (bf + ff)
        bands["f"][0].append(-cs * bf * w_ext[r])
        bands["f"][1].append(main)
        bands["f"][2].append(-cs * ff * w_ext[r + 2])
        bands["a"][0].append(-cs * bf * w)
        bands["a"][1].append(main)
        bands["a"][2].append(-cs * ff * w)

    for c, key in ((0, "f"), (1, "a")):
        lower, main, upper = bands[key]
        pivots, ratios = [], []
        prev = None
        for r in range(m - 1):
            piv = main[r] if prev is None else main[r] - lower[r] * prev
            rat = upper[r] / piv
            pivots.append(piv)
            ratios.append(rat)
            prev = rat
        inv_piv = [1.0 / x for x in pivots]
        left_src = [lower[0]] + [None] * (m - 1)
        right_src = [None] * (m - 2) + [upper[m - 2], None]
        left = _sweep(m, lower, inv_piv, ratios, left_src)
        right = _sweep(m, lower, inv_piv, ratios, right_src)
        for r in range(m):
            fac_ref[c, 0, r] = lower[r]
            fac_ref[c, 1, r] = ratios[r] if r < m - 1 else zero
            fac_ref[c, 2, r] = inv_piv[r] if r < m - 1 else zero + 1.0
            lr_ref[c, 0, r] = left[r] if r < m - 1 else zero
            lr_ref[c, 1, r] = right[r] if r < m - 1 else zero - 1.0
        last_lower = lower[m - 1]
        rows_ref[c, 0] = last_lower * left[m - 2]
        rows_ref[c, 1] = main[m - 1] - last_lower * right[m - 2]
        rows_ref[c, 2] = upper[m - 1]
        rows_ref[c, 3] = left[0]
        rows_ref[c, 4] = right[0]


def _reduced_solve(gs, gv, voff, c, n, pos):
    slot = [(pos - p + n) % n for p in range(n)]
    g = [[gs[slot[p], c, k] for k in range(5)] for p in range(n)]
    v = [[gv[slot[p], c, voff + k] for k in range(2)] for p in range(n)]
    lower = [-g[p][0] for p in range(n)]
    main = [g[p][1] - g[p][2] * g[(p + 1) % n][3] for p in range(n)]
    upper = [-g[p][2] * g[(p + 1) % n][4] for p in range(n)]
    src = [v[p][0] - g[p][2] * v[(p + 1) % n][1] for p in range(n)]
    k_in = n - 1
    pivots, ratios = [], []
    prev = None
    for r in range(k_in):
        piv = main[r] if prev is None else main[r] - lower[r] * prev
        rat = upper[r] / piv
        pivots.append(piv)
        ratios.append(rat)
        prev = rat

    def apply(source):
        ys = []
        prev = None
        for r in range(k_in):
            num = source[r] if prev is None else source[r] - lower[r] * prev
            ys.append(num / pivots[r])
            prev = ys[-1]
        xs = [None] * k_in
        prev = None
        for r in range(k_in - 1, -1, -1):
            xs[r] = ys[r] if prev is None else ys[r] - ratios[r] * prev
            prev = xs[r]
        return xs

    coupling = []
    for r in range(k_in):
        term = None
        if r == 0:
            term = lower[0]
        if r == k_in - 1:
            term = upper[k_in - 1] if term is None else term + upper[k_in - 1]
        coupling.append(term if term is not None else jnp.zeros_like(lower[0]))
    linked = apply(coupling)
    closing = main[k_in] - lower[k_in] * linked[k_in - 1] - upper[k_in] * linked[0]
    inner = apply(src[:k_in])
    sep = (src[k_in] - lower[k_in] * inner[k_in - 1] - upper[k_in] * inner[0]) / closing
    return [inner[r] - linked[r] * sep for r in range(k_in)] + [sep]


def _combine_kernel(n, stacked, edge_of, pos_ref, *refs):
    gs_parts, gv_parts = refs[:n], refs[n : 2 * n]
    lr_ref, loc_ref = refs[2 * n], refs[2 * n + 1]
    refs = refs[2 * n + 2 :]
    if stacked:
        out_ref = refs[0]
        outs = (out_ref.at[0], out_ref.at[1])
        rest = refs[1:]
    else:
        outs = refs[:2]
        rest = refs[2:]
    edge_outs, sep_ref, gs_ref, gv_ref = rest[:4], rest[4], rest[5], rest[6]
    edges = rest[7:11]
    for k in range(n):
        gs_ref[k] = gs_parts[k][...]
        gv_ref[k] = gv_parts[k][...]
    m = loc_ref.shape[1]
    p = pos_ref[0]
    for c in range(2):
        seps = _reduced_solve(gs_ref, gv_ref, 0, c, n, p)
        for q in range(n):
            sep_ref[q] = seps[q]
        own = sep_ref[p]
        prior = sep_ref[(p + n - 1) % n]
        for r in range(m):
            val = loc_ref[c, r] - lr_ref[c, 0, r] * prior - lr_ref[c, 1, r] * own
            outs[c][r] = val
            if c in edge_of:
                _write_edges(edges, edge_of[c], r, val)
    _flush_edges(edges, edge_outs, _parity(pos_ref))


def _edge_kernel(ctl_ref, vac_ref, pore_ref, lab_ref, y_a, y_b, z_a, z_b, bx_ref, *edges):
    m = vac_ref.shape[0]
    for r in range(m):
        mob = 1.0 + 2.0 * pore_ref[r].astype(F32)
        lab = lab_ref[r].astype(F32)
        for c, val in enumerate((mob, lab, vac_ref[r])):
            _write_edges(edges, c, r, val)
        if r == 0:
            bx_ref[0, 0] = mob
            bx_ref[0, 1] = lab
        if r == m - 1:
            bx_ref[1, 0] = mob
            bx_ref[1, 1] = lab
    _flush_edges(edges, (y_a, y_b, z_a, z_b), _parity(ctl_ref))


def _local_solves(fac_ref, srcs, loc_ref, vals_ref):
    m = loc_ref.shape[1]
    zero = jnp.zeros(loc_ref.shape[2:], F32)
    for c in range(2):
        lower = [fac_ref[c, 0, r] for r in range(m)]
        ratios = [fac_ref[c, 1, r] for r in range(m - 1)]
        pivots = [fac_ref[c, 2, r] for r in range(m - 1)]
        src = srcs[c]
        local = _sweep(m, lower, pivots, ratios, src[: m - 1] + [None])
        for r in range(m):
            loc_ref[c, r] = local[r] if r < m - 1 else zero
        vals_ref[c, 0] = src[m - 1] - lower[m - 1] * local[m - 2]
        vals_ref[c, 1] = local[0]


def _first_kernel(ctl_ref, vac_ref, cot_ref, pore_ref, lab_ref, fac_ref, gy_lo, gy_hi, gz_lo, gz_hi, loc_ref, vals_ref):
    gy_lo, gy_hi, gz_lo, gz_hi = _picks(ctl_ref, gy_lo, gy_hi, gz_lo, gz_hi)
    m = pore_ref.shape[0]
    srcs = ([], [cot_ref[r] for r in range(m)])
    for i in range(m):
        mob, _, mob_n, fc = _geo_row(i, pore_ref, lab_ref, gy_lo, gy_hi, gz_lo, gz_hi)
        w = 0.5 * (1.0 + mob)
        v = vac_ref[i]
        v_n = _neighbours(v, _yrow(gy_lo, 2, i), _yrow(gy_hi, 2, i), _zcol(gz_lo, 2, i), _zcol(gz_hi, 2, i))
        u_n = [0.5 * (1.0 + mn) * vn for mn, vn in zip(mob_n, v_n)]
        srcs[0].append(v + cross_rate * (1.0 * _flux(w * v, u_n, fc)))
    _local_solves(fac_ref, srcs, loc_ref, vals_ref)


def _second_kernel(ctl_ref, pore_ref, lab_ref, fa_ref, fac_ref, gy_lo, gy_hi, gz_lo, gz_hi,
                   hy_lo, hy_hi, hz_lo, hz_hi, loc_ref, vals_ref):
    gy_lo, gy_hi, gz_lo, gz_hi = _picks(ctl_ref, gy_lo, gy_hi, gz_lo, gz_hi)
    hy_lo, hy_hi, hz_lo, hz_hi = _picks(ctl_ref, hy_lo, hy_hi, hz_lo, hz_hi)
    m = pore_ref.shape[0]
    srcs = ([], [])
    for i in range(m):
        mob, _, mob_n, fc = _geo_row(i, pore_ref, lab_ref, gy_lo, gy_hi, gz_lo, gz_hi)
        w = 0.5 * (1.0 + mob)
        f1 = fa_ref[0, i]
        f_n = _neighbours(f1, _yrow(hy_lo, 0, i), _yrow(hy_hi, 0, i), _zcol(hz_lo, 0, i), _zcol(hz_hi, 0, i))
        u_n = [0.5 * (1.0 + mn) * fn for mn, fn in zip(mob_n, f_n)]
        srcs[0].append(f1 + cross_rate * (1.0 * _flux(w * f1, u_n, fc)))
        a1 = fa_ref[1, i]
        a_n = _neighbours(a1, _yrow(hy_lo, 1, i), _yrow(hy_hi, 1, i), _zcol(hz_lo, 1, i), _zcol(hz_hi, 1, i))
        srcs[1].append(a1 + cross_rate * (w * _flux(a1, a_n, fc)))
    _local_solves(fac_ref, srcs, loc_ref, vals_ref)


def _gradient_kernel(ctl_ref, pore_ref, lab_ref, a2_ref, gy_lo, gy_hi, gz_lo, gz_hi,
                     hy_lo, hy_hi, hz_lo, hz_hi, out_ref):
    gy_lo, gy_hi, gz_lo, gz_hi = _picks(ctl_ref, gy_lo, gy_hi, gz_lo, gz_hi)
    hy_lo, hy_hi, hz_lo, hz_hi = _picks(ctl_ref, hy_lo, hy_hi, hz_lo, hz_hi)
    m = pore_ref.shape[0]
    for i in range(m):
        mob, _, _, fc = _geo_row(i, pore_ref, lab_ref, gy_lo, gy_hi, gz_lo, gz_hi)
        w = 0.5 * (1.0 + mob)
        a2 = a2_ref[i]
        a_n = _neighbours(a2, _yrow(hy_lo, 0, i), _yrow(hy_hi, 0, i), _zcol(hz_lo, 0, i), _zcol(hz_hi, 0, i))
        out_ref[i] = a2 + cross_rate * (w * _flux(a2, a_n, fc))


def _halo_pairs(axis, periodic):
    count = lax.axis_size(axis)
    forward = [(i, i + 1) for i in range(count - 1)]
    if periodic:
        forward.append((count - 1, 0))
    backward = [(t, s) for s, t in forward]
    return forward, backward


def _exchange(first, last, axis, periodic):
    forward, backward = _halo_pairs(axis, periodic)
    lo = lax.ppermute(last, axis, forward)
    hi = lax.ppermute(first, axis, backward)
    return lo, hi


def _first_call(m, ny, nz):
    return _kernel_call(
        _first_kernel,
        out_shape=(
            jax.ShapeDtypeStruct((2, m, ny, nz), F32),
            jax.ShapeDtypeStruct((2, 2, ny, nz), F32),
        ),
        in_specs=[_smem()] + [_vmem()] * 9,
        out_specs=(_vmem(), _vmem()),
    )


def _combine_scratch(n, ny, nz):
    return [
        pltpu.VMEM((n, ny, nz), F32),
        pltpu.VMEM((n, 2, 5, ny, nz), F32),
        pltpu.VMEM((n, 2, 2, ny, nz), F32),
    ]


def _gather_blk(x):
    n = lax.axis_size("blk")
    parts = [x]
    for k in range(1, n):
        parts.append(lax.ppermute(x, "blk", [(j, (j + k) % n) for j in range(n)]))
    return parts


def _edge_shapes(chans, m, ny, nz):
    return (
        jax.ShapeDtypeStruct((chans, m, nz), F32),
        jax.ShapeDtypeStruct((chans, m, nz), F32),
        jax.ShapeDtypeStruct((chans, ny, m), F32),
        jax.ShapeDtypeStruct((chans, ny, m), F32),
    )


def _swap(x_a, x_b, axis):
    n = lax.axis_size(axis)
    pairs_a = [(i, i ^ 1) for i in range(n) if i ^ 1 < n]
    pairs_b = [(i, i + 1) for i in range(1, n - 1, 2)] + [(i + 1, i) for i in range(1, n - 1, 2)]
    recv_a = lax.ppermute(x_a, axis, pairs_a)
    recv_b = lax.ppermute(x_b, axis, pairs_b) if pairs_b else jnp.zeros_like(x_b)
    return recv_a, recv_b


def _yz_halos(y_a, y_b, z_a, z_b):
    return _swap(y_a, y_b, "gy") + _swap(z_a, z_b, "gz")


def _shards(vacancy, grain_label, pore_mask, cotangent):
    m, ny, nz = vacancy.shape
    n_blk = lax.axis_size("blk")
    cycle_step = float((m * n_blk) ** 2 // 64)
    shape = jax.ShapeDtypeStruct((m, ny, nz), F32)

    ctl = jnp.stack(
        [lax.axis_index("blk"), 1 - lax.axis_index("gy") % 2, 1 - lax.axis_index("gz") % 2]
    ).astype(jnp.int32)
    outs = _kernel_call(
        _edge_kernel,
        out_shape=_edge_shapes(3, m, ny, nz) + (jax.ShapeDtypeStruct((2, 2, ny, nz), F32),),
        in_specs=[_smem()] + [_vmem()] * 3,
        out_specs=tuple(_vmem() for _ in range(5)),
        scratch_shapes=_edge_scratch(3, m, ny, nz),
    )(ctl, vacancy, pore_mask, grain_label)
    if n_blk == 2:
        bx = lax.ppermute(outs[4], "blk", [(0, 1), (1, 0)])
        lo_i, hi_i = 1, 0
    else:
        bx_lo, bx_hi = _exchange(outs[4][0], outs[4][1], "blk", True)
        bx = jnp.stack([bx_lo, bx_hi])
        lo_i, hi_i = 0, 1
    gy_lo, gy_hi, gz_lo, gz_hi = _yz_halos(*outs[:4])

    fac, lr, rows = _kernel_call(
        lambda *r: _factor_kernel(cycle_step, lo_i, hi_i, *r),
        out_shape=(
            jax.ShapeDtypeStruct((2, 3, m, ny, nz), F32),
            jax.ShapeDtypeStruct((2, 2, m, ny, nz), F32),
            jax.ShapeDtypeStruct((2, 5, ny, nz), F32),
        ),
        in_specs=[_vmem()] * 3,
        out_specs=(_vmem(), _vmem(), _vmem()),
    )(pore_mask, grain_label, bx)
    gathered = _gather_blk(rows)

    loc, vals = _first_call(m, ny, nz)(ctl, vacancy, cotangent, pore_mask, grain_label, fac, gy_lo, gy_hi, gz_lo, gz_hi)
    gathered1 = _gather_blk(vals)
    pos = ctl

    outs = _kernel_call(
        lambda *r: _combine_kernel(n_blk, True, {0: 0, 1: 1}, *r),
        out_shape=(jax.ShapeDtypeStruct((2, m, ny, nz), F32),) + _edge_shapes(2, m, ny, nz),
        in_specs=[_smem()] + [_vmem()] * (2 * n_blk + 2),
        out_specs=tuple(_vmem() for _ in range(5)),
        scratch_shapes=_combine_scratch(n_blk, ny, nz) + _edge_scratch(2, m, ny, nz),
    )(pos, *gathered, *gathered1, lr, loc)
    fa = outs[0]

    hy_lo, hy_hi, hz_lo, hz_hi = _yz_halos(*outs[1:])
    loc2, vals2 = _kernel_call(
        _second_kernel,
        out_shape=(
            jax.ShapeDtypeStruct((2, m, ny, nz), F32),
            jax.ShapeDtypeStruct((2, 2, ny, nz), F32),
        ),
        in_specs=[_smem()] + [_vmem()] * 12,
        out_specs=(_vmem(), _vmem()),
    )(ctl, pore_mask, grain_label, fa, fac, gy_lo, gy_hi, gz_lo, gz_hi, hy_lo, hy_hi, hz_lo, hz_hi)

    gathered2 = _gather_blk(vals2)
    outs = _kernel_call(
        lambda *r: _combine_kernel(n_blk, False, {1: 0}, *r),
        out_shape=(shape, shape) + _edge_shapes(1, m, ny, nz),
        in_specs=[_smem()] + [_vmem()] * (2 * n_blk + 2),
        out_specs=tuple(_vmem() for _ in range(6)),
        scratch_shapes=_combine_scratch(n_blk, ny, nz) + _edge_scratch(1, m, ny, nz),
    )(pos, *gathered, *gathered2, lr, loc2)
    final_field, adjoint_two = outs[:2]

    a2_lo, a2_hi, a2z_lo, a2z_hi = _yz_halos(*outs[2:])
    gradient = _kernel_call(
        _gradient_kernel,
        out_shape=shape,
        in_specs=[_smem()] + [_vmem()] * 11,
        out_specs=_vmem(),
    )(ctl, pore_mask, grain_label, adjoint_two, gy_lo, gy_hi, gz_lo, gz_hi, a2_lo, a2_hi, a2z_lo, a2z_hi)
    return (final_field, gradient)


def solution(mesh):
    in_specs = (
        P("blk", "gy", "gz"),
        P("blk", "gy", "gz"),
        P("blk", "gy", "gz"),
        P("blk", "gy", "gz"),
    )
    out_specs = (P("blk", "gy", "gz"), P("blk", "gy", "gz"))
    fn = jax.shard_map(_shards, mesh=mesh, in_specs=in_specs, out_specs=out_specs, check_vma=False)
    if mesh.shape["blk"] > 4:
        return fn
    return fn
```

```python
import jax
import jax.numpy as jnp
from jax import lax
from jax.experimental import pallas as pl
from jax.experimental.pallas import tpu as pltpu
from jax.sharding import PartitionSpec as P


cross_rate = 0.0125
boundary_gain = 3.0
F32 = jnp.float32


def face_value(mobility_here, mobility_there, label_here, label_there):
    harmonic = 2.0 * mobility_here * mobility_there / (mobility_here + mobility_there)
    return harmonic * jnp.where(label_here != label_there, boundary_gain, 1.0)


def _vmem():
    return pl.BlockSpec(memory_space=pltpu.VMEM)


def _smem():
    return pl.BlockSpec(memory_space=pltpu.SMEM)


def _shift(x, edge, axis, up):
    n = x.shape[axis]
    idx = lax.broadcasted_iota(jnp.int32, x.shape, axis)
    edge = jnp.broadcast_to(edge, x.shape)
    if up:
        return jnp.where(idx == n - 1, edge, pltpu.roll(x, n - 1, axis))
    return jnp.where(idx == 0, edge, pltpu.roll(x, 1, axis))


def _neighbours(x, ylo, yhi, zlo, zhi):
    return (
        _shift(x, yhi, 0, True),
        _shift(x, ylo, 0, False),
        _shift(x, zhi, 1, True),
        _shift(x, zlo, 1, False),
    )


def _faces(mob, lab, mob_n, lab_n):
    ups = (True, False, True, False)
    out = []
    for up, mn, ln in zip(ups, mob_n, lab_n):
        if up:
            out.append(face_value(mob, mn, lab, ln))
        else:
            out.append(face_value(mn, mob, ln, lab))
    return out


def _flux(u, u_n, faces):
    total = faces[0] * (u_n[0] - u)
    total = total + faces[1] * (u_n[1] - u)
    total = total + faces[2] * (u_n[2] - u)
    total = total + faces[3] * (u_n[3] - u)
    return total


def _yrow(ref, c, i):
    return ref[c, pl.ds(i, 1), :]


def _zcol(ref, c, i):
    return ref[c, :, pl.ds(i, 1)]


def _write_edges(edges, c, r, val):
    y_first, y_last, z_first, z_last = edges
    ny, nz = val.shape
    y_first[c, pl.ds(r, 1), :] = val[0:1, :]
    y_last[c, pl.ds(r, 1), :] = val[ny - 1 : ny, :]
    z_first[c, :, pl.ds(r, 1)] = val[:, 0:1]
    z_last[c, :, pl.ds(r, 1)] = val[:, nz - 1 : nz]


def _flush_edges(scratch, outs, par):
    y_first, y_last, z_first, z_last = scratch
    y_a, y_b, z_a, z_b = outs
    even_y, even_z = par
    for even, first, last, out_a, out_b in ((even_y, y_first, y_last, y_a, y_b), (even_z, z_first, z_last, z_a, z_b)):

        @pl.when(even)
        def _():
            out_a[...] = last[...]
            out_b[...] = first[...]

        @pl.when(jnp.logical_not(even))
        def _():
            out_a[...] = first[...]
            out_b[...] = last[...]


def _edge_scratch(chans, m, ny, nz):
    return [
        pltpu.VMEM((chans, m, nz), F32),
        pltpu.VMEM((chans, m, nz), F32),
        pltpu.VMEM((chans, ny, m), F32),
        pltpu.VMEM((chans, ny, m), F32),
    ]


class _Pick:
    def __init__(self, a, b, use_b):
        self.a, self.b, self.use_b = a, b, use_b

    def __getitem__(self, idx):
        return jnp.where(self.use_b, self.b[idx], self.a[idx])


def _parity(ctl_ref):
    return ctl_ref[1] == 1, ctl_ref[2] == 1


def _picks(ctl_ref, y_a, y_b, z_a, z_b):
    even_y, even_z = _parity(ctl_ref)
    return (
        _Pick(y_a, y_b, even_y),
        _Pick(y_a, y_b, jnp.logical_not(even_y)),
        _Pick(z_a, z_b, even_z),
        _Pick(z_a, z_b, jnp.logical_not(even_z)),
    )


def _geo_row(i, pore_ref, lab_ref, gy_lo, gy_hi, gz_lo, gz_hi):
    mob = 1.0 + 2.0 * pore_ref[i].astype(F32)
    lab = lab_ref[i].astype(F32)
    mob_n = _neighbours(mob, _yrow(gy_lo, 0, i), _yrow(gy_hi, 0, i), _zcol(gz_lo, 0, i), _zcol(gz_hi, 0, i))
    lab_n = _neighbours(lab, _yrow(gy_lo, 1, i), _yrow(gy_hi, 1, i), _zcol(gz_lo, 1, i), _zcol(gz_hi, 1, i))
    return mob, lab, mob_n, _faces(mob, lab, mob_n, lab_n)


def _sweep(m, lower, inv_pivots, ratios, source):
    ys = [None] * m
    prev = None
    for r in range(m - 1):
        num = source[r]
        if num is None:
            if prev is None:
                continue
            num = -(lower[r] * prev)
        elif prev is not None:
            num = num - lower[r] * prev
        ys[r] = num * inv_pivots[r]
        prev = ys[r]
    xs = [None] * m
    prev = None
    for r in range(m - 2, -1, -1):
        if prev is None:
            xs[r] = ys[r]
        elif ys[r] is None:
            xs[r] = -(ratios[r] * prev)
        else:
            xs[r] = ys[r] - ratios[r] * prev
        prev = xs[r]
    return xs


def _factor_kernel(cs, lo_i, hi_i, pore_ref, lab_ref, bx_ref, fac_ref, lr_ref, rows_ref):
    bx_lo, bx_hi = bx_ref.at[lo_i], bx_ref.at[hi_i]
    m = pore_ref.shape[0]
    zero = jnp.zeros(pore_ref.shape[1:], F32)
    mobs = [1.0 + 2.0 * pore_ref[r].astype(F32) for r in range(m)]
    labs = [lab_ref[r].astype(F32) for r in range(m)]
    m_ext = [bx_lo[0]] + mobs + [bx_hi[0]]
    l_ext = [bx_lo[1]] + labs + [bx_hi[1]]
    w_ext = [0.5 * (1.0 + x) for x in m_ext]
    faces = [face_value(m_ext[k], m_ext[k + 1], l_ext[k], l_ext[k + 1]) for k in range(m + 1)]
    bands = {"f": ([], [], []), "a": ([], [], [])}
    for r in range(m):
        bf, ff = faces[r], faces[r + 1]
        w = w_ext[r + 1]
        main = 1.0 + cs * w * (bf + ff)
        bands["f"][0].append(-cs * bf * w_ext[r])
        bands["f"][1].append(main)
        bands["f"][2].append(-cs * ff * w_ext[r + 2])
        bands["a"][0].append(-cs * bf * w)
        bands["a"][1].append(main)
        bands["a"][2].append(-cs * ff * w)

    for c, key in ((0, "f"), (1, "a")):
        lower, main, upper = bands[key]
        pivots, ratios = [], []
        prev = None
        for r in range(m - 1):
            piv = main[r] if prev is None else main[r] - lower[r] * prev
            rat = upper[r] / piv
            pivots.append(piv)
            ratios.append(rat)
            prev = rat
        inv_piv = [1.0 / x for x in pivots]
        left_src = [lower[0]] + [None] * (m - 1)
        right_src = [None] * (m - 2) + [upper[m - 2], None]
        left = _sweep(m, lower, inv_piv, ratios, left_src)
        right = _sweep(m, lower, inv_piv, ratios, right_src)
        for r in range(m):
            fac_ref[c, 0, r] = lower[r]
            fac_ref[c, 1, r] = ratios[r] if r < m - 1 else zero
            fac_ref[c, 2, r] = inv_piv[r] if r < m - 1 else zero + 1.0
            lr_ref[c, 0, r] = left[r] if r < m - 1 else zero
            lr_ref[c, 1, r] = right[r] if r < m - 1 else zero - 1.0
        last_lower = lower[m - 1]
        rows_ref[c, 0] = last_lower * left[m - 2]
        rows_ref[c, 1] = main[m - 1] - last_lower * right[m - 2]
        rows_ref[c, 2] = upper[m - 1]
        rows_ref[c, 3] = left[0]
        rows_ref[c, 4] = right[0]


def _reduced_solve(gs, gv, voff, c, n, pos):
    slot = [(pos - p + n) % n for p in range(n)]
    g = [[gs[slot[p], c, k] for k in range(5)] for p in range(n)]
    v = [[gv[slot[p], c, voff + k] for k in range(2)] for p in range(n)]
    lower = [-g[p][0] for p in range(n)]
    main = [g[p][1] - g[p][2] * g[(p + 1) % n][3] for p in range(n)]
    upper = [-g[p][2] * g[(p + 1) % n][4] for p in range(n)]
    src = [v[p][0] - g[p][2] * v[(p + 1) % n][1] for p in range(n)]
    k_in = n - 1
    pivots, ratios = [], []
    prev = None
    for r in range(k_in):
        piv = main[r] if prev is None else main[r] - lower[r] * prev
        rat = upper[r] / piv
        pivots.append(piv)
        ratios.append(rat)
        prev = rat

    def apply(source):
        ys = []
        prev = None
        for r in range(k_in):
            num = source[r] if prev is None else source[r] - lower[r] * prev
            ys.append(num / pivots[r])
            prev = ys[-1]
        xs = [None] * k_in
        prev = None
        for r in range(k_in - 1, -1, -1):
            xs[r] = ys[r] if prev is None else ys[r] - ratios[r] * prev
            prev = xs[r]
        return xs

    coupling = []
    for r in range(k_in):
        term = None
        if r == 0:
            term = lower[0]
        if r == k_in - 1:
            term = upper[k_in - 1] if term is None else term + upper[k_in - 1]
        coupling.append(term if term is not None else jnp.zeros_like(lower[0]))
    linked = apply(coupling)
    closing = main[k_in] - lower[k_in] * linked[k_in - 1] - upper[k_in] * linked[0]
    inner = apply(src[:k_in])
    sep = (src[k_in] - lower[k_in] * inner[k_in - 1] - upper[k_in] * inner[0]) / closing
    return [inner[r] - linked[r] * sep for r in range(k_in)] + [sep]


def _combine_kernel(n, stacked, edge_of, pos_ref, *refs):
    gs_parts, gv_parts = refs[:n], refs[n : 2 * n]
    lr_ref, loc_ref = refs[2 * n], refs[2 * n + 1]
    refs = refs[2 * n + 2 :]
    if stacked:
        out_ref = refs[0]
        outs = (out_ref.at[0], out_ref.at[1])
        rest = refs[1:]
    else:
        outs = refs[:2]
        rest = refs[2:]
    edge_outs, sep_ref, gs_ref, gv_ref = rest[:4], rest[4], rest[5], rest[6]
    edges = rest[7:11]
    for k in range(n):
        gs_ref[k] = gs_parts[k][...]
        gv_ref[k] = gv_parts[k][...]
    m = loc_ref.shape[1]
    p = pos_ref[0]
    for c in range(2):
        seps = _reduced_solve(gs_ref, gv_ref, 0, c, n, p)
        for q in range(n):
            sep_ref[q] = seps[q]
        own = sep_ref[p]
        prior = sep_ref[(p + n - 1) % n]
        for r in range(m):
            val = loc_ref[c, r] - lr_ref[c, 0, r] * prior - lr_ref[c, 1, r] * own
            outs[c][r] = val
            if c in edge_of:
                _write_edges(edges, edge_of[c], r, val)
    _flush_edges(edges, edge_outs, _parity(pos_ref))


def _edge_kernel(ctl_ref, vac_ref, pore_ref, lab_ref, y_a, y_b, z_a, z_b, bx_ref, *edges):
    m = vac_ref.shape[0]
    for r in range(m):
        mob = 1.0 + 2.0 * pore_ref[r].astype(F32)
        lab = lab_ref[r].astype(F32)
        for c, val in enumerate((mob, lab, vac_ref[r])):
            _write_edges(edges, c, r, val)
        if r == 0:
            bx_ref[0, 0] = mob
            bx_ref[0, 1] = lab
        if r == m - 1:
            bx_ref[1, 0] = mob
            bx_ref[1, 1] = lab
    _flush_edges(edges, (y_a, y_b, z_a, z_b), _parity(ctl_ref))


def _local_solves(fac_ref, srcs, loc_ref, vals_ref):
    m = loc_ref.shape[1]
    zero = jnp.zeros(loc_ref.shape[2:], F32)
    for c in range(2):
        lower = [fac_ref[c, 0, r] for r in range(m)]
        ratios = [fac_ref[c, 1, r] for r in range(m - 1)]
        pivots = [fac_ref[c, 2, r] for r in range(m - 1)]
        src = srcs[c]
        local = _sweep(m, lower, pivots, ratios, src[: m - 1] + [None])
        for r in range(m):
            loc_ref[c, r] = local[r] if r < m - 1 else zero
        vals_ref[c, 0] = src[m - 1] - lower[m - 1] * local[m - 2]
        vals_ref[c, 1] = local[0]


def _first_kernel(ctl_ref, vac_ref, cot_ref, pore_ref, lab_ref, fac_ref, gy_lo, gy_hi, gz_lo, gz_hi, loc_ref, vals_ref):
    gy_lo, gy_hi, gz_lo, gz_hi = _picks(ctl_ref, gy_lo, gy_hi, gz_lo, gz_hi)
    m = pore_ref.shape[0]
    srcs = ([], [cot_ref[r] for r in range(m)])
    for i in range(m):
        mob, _, mob_n, fc = _geo_row(i, pore_ref, lab_ref, gy_lo, gy_hi, gz_lo, gz_hi)
        w = 0.5 * (1.0 + mob)
        v = vac_ref[i]
        v_n = _neighbours(v, _yrow(gy_lo, 2, i), _yrow(gy_hi, 2, i), _zcol(gz_lo, 2, i), _zcol(gz_hi, 2, i))
        u_n = [0.5 * (1.0 + mn) * vn for mn, vn in zip(mob_n, v_n)]
        srcs[0].append(v + cross_rate * (1.0 * _flux(w * v, u_n, fc)))
    _local_solves(fac_ref, srcs, loc_ref, vals_ref)


def _second_kernel(ctl_ref, pore_ref, lab_ref, fa_ref, fac_ref, gy_lo, gy_hi, gz_lo, gz_hi,
                   hy_lo, hy_hi, hz_lo, hz_hi, loc_ref, vals_ref):
    gy_lo, gy_hi, gz_lo, gz_hi = _picks(ctl_ref, gy_lo, gy_hi, gz_lo, gz_hi)
    hy_lo, hy_hi, hz_lo, hz_hi = _picks(ctl_ref, hy_lo, hy_hi, hz_lo, hz_hi)
    m = pore_ref.shape[0]
    srcs = ([], [])
    for i in range(m):
        mob, _, mob_n, fc = _geo_row(i, pore_ref, lab_ref, gy_lo, gy_hi, gz_lo, gz_hi)
        w = 0.5 * (1.0 + mob)
        f1 = fa_ref[0, i]
        f_n = _neighbours(f1, _yrow(hy_lo, 0, i), _yrow(hy_hi, 0, i), _zcol(hz_lo, 0, i), _zcol(hz_hi, 0, i))
        u_n = [0.5 * (1.0 + mn) * fn for mn, fn in zip(mob_n, f_n)]
        srcs[0].append(f1 + cross_rate * (1.0 * _flux(w * f1, u_n, fc)))
        a1 = fa_ref[1, i]
        a_n = _neighbours(a1, _yrow(hy_lo, 1, i), _yrow(hy_hi, 1, i), _zcol(hz_lo, 1, i), _zcol(hz_hi, 1, i))
        srcs[1].append(a1 + cross_rate * (w * _flux(a1, a_n, fc)))
    _local_solves(fac_ref, srcs, loc_ref, vals_ref)


def _gradient_kernel(ctl_ref, pore_ref, lab_ref, a2_ref, gy_lo, gy_hi, gz_lo, gz_hi,
                     hy_lo, hy_hi, hz_lo, hz_hi, out_ref):
    gy_lo, gy_hi, gz_lo, gz_hi = _picks(ctl_ref, gy_lo, gy_hi, gz_lo, gz_hi)
    hy_lo, hy_hi, hz_lo, hz_hi = _picks(ctl_ref, hy_lo, hy_hi, hz_lo, hz_hi)
    m = pore_ref.shape[0]
    for i in range(m):
        mob, _, _, fc = _geo_row(i, pore_ref, lab_ref, gy_lo, gy_hi, gz_lo, gz_hi)
        w = 0.5 * (1.0 + mob)
        a2 = a2_ref[i]
        a_n = _neighbours(a2, _yrow(hy_lo, 0, i), _yrow(hy_hi, 0, i), _zcol(hz_lo, 0, i), _zcol(hz_hi, 0, i))
        out_ref[i] = a2 + cross_rate * (w * _flux(a2, a_n, fc))


def _halo_pairs(axis, periodic):
    count = lax.axis_size(axis)
    forward = [(i, i + 1) for i in range(count - 1)]
    if periodic:
        forward.append((count - 1, 0))
    backward = [(t, s) for s, t in forward]
    return forward, backward


def _exchange(first, last, axis, periodic):
    forward, backward = _halo_pairs(axis, periodic)
    lo = lax.ppermute(last, axis, forward)
    hi = lax.ppermute(first, axis, backward)
    return lo, hi


def _first_call(m, ny, nz):
    return pl.pallas_call(
        _first_kernel,
        out_shape=(
            jax.ShapeDtypeStruct((2, m, ny, nz), F32),
            jax.ShapeDtypeStruct((2, 2, ny, nz), F32),
        ),
        in_specs=[_smem()] + [_vmem()] * 9,
        out_specs=(_vmem(), _vmem()),
    )


def _combine_scratch(n, ny, nz):
    return [
        pltpu.VMEM((n, ny, nz), F32),
        pltpu.VMEM((n, 2, 5, ny, nz), F32),
        pltpu.VMEM((n, 2, 2, ny, nz), F32),
    ]


def _gather_blk(x):
    n = lax.axis_size("blk")
    parts = [x]
    for k in range(1, n):
        parts.append(lax.ppermute(x, "blk", [(j, (j + k) % n) for j in range(n)]))
    return parts


def _edge_shapes(chans, m, ny, nz):
    return (
        jax.ShapeDtypeStruct((chans, m, nz), F32),
        jax.ShapeDtypeStruct((chans, m, nz), F32),
        jax.ShapeDtypeStruct((chans, ny, m), F32),
        jax.ShapeDtypeStruct((chans, ny, m), F32),
    )


def _swap(x_a, x_b, axis):
    n = lax.axis_size(axis)
    pairs_a = [(i, i ^ 1) for i in range(n) if i ^ 1 < n]
    pairs_b = [(i, i + 1) for i in range(1, n - 1, 2)] + [(i + 1, i) for i in range(1, n - 1, 2)]
    recv_a = lax.ppermute(x_a, axis, pairs_a)
    recv_b = lax.ppermute(x_b, axis, pairs_b) if pairs_b else jnp.zeros_like(x_b)
    return recv_a, recv_b


def _yz_halos(y_a, y_b, z_a, z_b):
    return _swap(y_a, y_b, "gy") + _swap(z_a, z_b, "gz")


def _shards(vacancy, grain_label, pore_mask, cotangent):
    m, ny, nz = vacancy.shape
    n_blk = lax.axis_size("blk")
    cycle_step = float((m * n_blk) ** 2 // 64)
    shape = jax.ShapeDtypeStruct((m, ny, nz), F32)

    ctl = jnp.stack(
        [lax.axis_index("blk"), 1 - lax.axis_index("gy") % 2, 1 - lax.axis_index("gz") % 2]
    ).astype(jnp.int32)
    mob_ends = 1.0 + 2.0 * jnp.stack([pore_mask[0], pore_mask[m - 1]]).astype(F32)
    lab_ends = jnp.stack([grain_label[0], grain_label[m - 1]]).astype(F32)
    ends = jnp.stack([mob_ends, lab_ends], axis=1)
    if n_blk == 2:
        bx = lax.ppermute(ends, "blk", [(0, 1), (1, 0)])
        lo_i, hi_i = 1, 0
    else:
        bx_lo, bx_hi = _exchange(ends[0], ends[1], "blk", True)
        bx = jnp.stack([bx_lo, bx_hi])
        lo_i, hi_i = 0, 1
    outs = pl.pallas_call(
        _edge_kernel,
        out_shape=_edge_shapes(3, m, ny, nz) + (jax.ShapeDtypeStruct((2, 2, ny, nz), F32),),
        in_specs=[_smem()] + [_vmem()] * 3,
        out_specs=tuple(_vmem() for _ in range(5)),
        scratch_shapes=_edge_scratch(3, m, ny, nz),
    )(ctl, vacancy, pore_mask, grain_label)
    gy_lo, gy_hi, gz_lo, gz_hi = _yz_halos(*outs[:4])

    fac, lr, rows = pl.pallas_call(
        lambda *r: _factor_kernel(cycle_step, lo_i, hi_i, *r),
        out_shape=(
            jax.ShapeDtypeStruct((2, 3, m, ny, nz), F32),
            jax.ShapeDtypeStruct((2, 2, m, ny, nz), F32),
            jax.ShapeDtypeStruct((2, 5, ny, nz), F32),
        ),
        in_specs=[_vmem()] * 3,
        out_specs=(_vmem(), _vmem(), _vmem()),
    )(pore_mask, grain_label, bx)
    gathered = _gather_blk(rows)

    loc, vals = _first_call(m, ny, nz)(
        ctl, vacancy, cotangent, pore_mask, grain_label, fac, gy_lo, gy_hi, gz_lo, gz_hi
    )
    gathered1 = _gather_blk(vals)
    pos = ctl

    outs = pl.pallas_call(
        lambda *r: _combine_kernel(n_blk, True, {0: 0, 1: 1}, *r),
        out_shape=(jax.ShapeDtypeStruct((2, m, ny, nz), F32),) + _edge_shapes(2, m, ny, nz),
        in_specs=[_smem()] + [_vmem()] * (2 * n_blk + 2),
        out_specs=tuple(_vmem() for _ in range(5)),
        scratch_shapes=_combine_scratch(n_blk, ny, nz) + _edge_scratch(2, m, ny, nz),
    )(pos, *gathered, *gathered1, lr, loc)
    fa = outs[0]

    hy_lo, hy_hi, hz_lo, hz_hi = _yz_halos(*outs[1:])
    loc2, vals2 = pl.pallas_call(
        _second_kernel,
        out_shape=(
            jax.ShapeDtypeStruct((2, m, ny, nz), F32),
            jax.ShapeDtypeStruct((2, 2, ny, nz), F32),
        ),
        in_specs=[_smem()] + [_vmem()] * 12,
        out_specs=(_vmem(), _vmem()),
    )(ctl, pore_mask, grain_label, fa, fac, gy_lo, gy_hi, gz_lo, gz_hi, hy_lo, hy_hi, hz_lo, hz_hi)

    gathered2 = _gather_blk(vals2)
    outs = pl.pallas_call(
        lambda *r: _combine_kernel(n_blk, False, {1: 0}, *r),
        out_shape=(shape, shape) + _edge_shapes(1, m, ny, nz),
        in_specs=[_smem()] + [_vmem()] * (2 * n_blk + 2),
        out_specs=tuple(_vmem() for _ in range(6)),
        scratch_shapes=_combine_scratch(n_blk, ny, nz) + _edge_scratch(1, m, ny, nz),
    )(pos, *gathered, *gathered2, lr, loc2)
    final_field, adjoint_two = outs[:2]

    a2_lo, a2_hi, a2z_lo, a2z_hi = _yz_halos(*outs[2:])
    gradient = pl.pallas_call(
        _gradient_kernel,
        out_shape=shape,
        in_specs=[_smem()] + [_vmem()] * 11,
        out_specs=_vmem(),
    )(ctl, pore_mask, grain_label, adjoint_two, gy_lo, gy_hi, gz_lo, gz_hi, a2_lo, a2_hi, a2z_lo, a2z_hi)
    return (final_field, gradient)


def solution(mesh):
    in_specs = (
        P("blk", "gy", "gz"),
        P("blk", "gy", "gz"),
        P("blk", "gy", "gz"),
        P("blk", "gy", "gz"),
    )
    out_specs = (P("blk", "gy", "gz"), P("blk", "gy", "gz"))
    fn = jax.shard_map(_shards, mesh=mesh, in_specs=in_specs, out_specs=out_specs, check_vma=False)
    if mesh.shape["blk"] > 4:
        return fn
    return fn
```

```python
import jax
import jax.numpy as jnp
from jax import lax
from jax.experimental import pallas as pl
from jax.experimental.pallas import tpu as pltpu
from jax.sharding import PartitionSpec as P


cross_rate = 0.0125
boundary_gain = 3.0
F32 = jnp.float32


def face_value(mobility_here, mobility_there, label_here, label_there):
    harmonic = 2.0 * mobility_here * mobility_there / (mobility_here + mobility_there)
    return harmonic * jnp.where(label_here != label_there, boundary_gain, 1.0)


def _vmem():
    return pl.BlockSpec(memory_space=pltpu.VMEM)


def _smem():
    return pl.BlockSpec(memory_space=pltpu.SMEM)


def _shift(x, edge, axis, up):
    n = x.shape[axis]
    idx = lax.broadcasted_iota(jnp.int32, x.shape, axis)
    edge = jnp.broadcast_to(edge, x.shape)
    if up:
        return jnp.where(idx == n - 1, edge, pltpu.roll(x, n - 1, axis))
    return jnp.where(idx == 0, edge, pltpu.roll(x, 1, axis))


def _neighbours(x, ylo, yhi, zlo, zhi):
    return (
        _shift(x, yhi, 0, True),
        _shift(x, ylo, 0, False),
        _shift(x, zhi, 1, True),
        _shift(x, zlo, 1, False),
    )


def _faces(mob, lab, mob_n, lab_n):
    ups = (True, False, True, False)
    out = []
    for up, mn, ln in zip(ups, mob_n, lab_n):
        if up:
            out.append(face_value(mob, mn, lab, ln))
        else:
            out.append(face_value(mn, mob, ln, lab))
    return out


def _flux(u, u_n, faces):
    total = faces[0] * (u_n[0] - u)
    total = total + faces[1] * (u_n[1] - u)
    total = total + faces[2] * (u_n[2] - u)
    total = total + faces[3] * (u_n[3] - u)
    return total


def _yrow(ref, c, i):
    return ref[c, pl.ds(i, 1), :]


def _zcol(ref, c, i):
    return ref[c, :, pl.ds(i, 1)]


def _write_edges(edges, c, r, val):
    y_first, y_last, z_first, z_last = edges
    ny, nz = val.shape
    y_first[c, pl.ds(r, 1), :] = val[0:1, :]
    y_last[c, pl.ds(r, 1), :] = val[ny - 1 : ny, :]
    z_first[c, :, pl.ds(r, 1)] = val[:, 0:1]
    z_last[c, :, pl.ds(r, 1)] = val[:, nz - 1 : nz]


def _flush_edges(scratch, outs, par):
    y_first, y_last, z_first, z_last = scratch
    y_a, y_b, z_a, z_b = outs
    even_y, even_z = par
    for even, first, last, out_a, out_b in ((even_y, y_first, y_last, y_a, y_b), (even_z, z_first, z_last, z_a, z_b)):

        @pl.when(even)
        def _():
            out_a[...] = last[...]
            out_b[...] = first[...]

        @pl.when(jnp.logical_not(even))
        def _():
            out_a[...] = first[...]
            out_b[...] = last[...]


def _edge_scratch(chans, m, ny, nz):
    return [
        pltpu.VMEM((chans, m, nz), F32),
        pltpu.VMEM((chans, m, nz), F32),
        pltpu.VMEM((chans, ny, m), F32),
        pltpu.VMEM((chans, ny, m), F32),
    ]


class _Pick:
    def __init__(self, a, b, use_b):
        self.a, self.b, self.use_b = a, b, use_b

    def __getitem__(self, idx):
        return jnp.where(self.use_b, self.b[idx], self.a[idx])


def _parity(ctl_ref):
    return ctl_ref[1] == 1, ctl_ref[2] == 1


def _picks(ctl_ref, y_a, y_b, z_a, z_b):
    even_y, even_z = _parity(ctl_ref)
    return (
        _Pick(y_a, y_b, even_y),
        _Pick(y_a, y_b, jnp.logical_not(even_y)),
        _Pick(z_a, z_b, even_z),
        _Pick(z_a, z_b, jnp.logical_not(even_z)),
    )


def _geo_row(i, pore_ref, lab_ref, gy_lo, gy_hi, gz_lo, gz_hi):
    mob = 1.0 + 2.0 * pore_ref[i].astype(F32)
    lab = lab_ref[i].astype(F32)
    mob_n = _neighbours(mob, _yrow(gy_lo, 0, i), _yrow(gy_hi, 0, i), _zcol(gz_lo, 0, i), _zcol(gz_hi, 0, i))
    lab_n = _neighbours(lab, _yrow(gy_lo, 1, i), _yrow(gy_hi, 1, i), _zcol(gz_lo, 1, i), _zcol(gz_hi, 1, i))
    return mob, lab, mob_n, _faces(mob, lab, mob_n, lab_n)


def _sweep(m, lower, inv_pivots, ratios, source):
    ys = [None] * m
    prev = None
    for r in range(m - 1):
        num = source[r]
        if num is None:
            if prev is None:
                continue
            num = -(lower[r] * prev)
        elif prev is not None:
            num = num - lower[r] * prev
        ys[r] = num * inv_pivots[r]
        prev = ys[r]
    xs = [None] * m
    prev = None
    for r in range(m - 2, -1, -1):
        if prev is None:
            xs[r] = ys[r]
        elif ys[r] is None:
            xs[r] = -(ratios[r] * prev)
        else:
            xs[r] = ys[r] - ratios[r] * prev
        prev = xs[r]
    return xs


def _factor_kernel(cs, lo_i, hi_i, pore_ref, lab_ref, bx_ref, fac_ref, lr_ref, rows_ref):
    bx_lo, bx_hi = bx_ref.at[lo_i], bx_ref.at[hi_i]
    m = pore_ref.shape[0]
    zero = jnp.zeros(pore_ref.shape[1:], F32)
    mobs = [1.0 + 2.0 * pore_ref[r].astype(F32) for r in range(m)]
    labs = [lab_ref[r].astype(F32) for r in range(m)]
    m_ext = [bx_lo[0]] + mobs + [bx_hi[0]]
    l_ext = [bx_lo[1]] + labs + [bx_hi[1]]
    w_ext = [0.5 * (1.0 + x) for x in m_ext]
    faces = [face_value(m_ext[k], m_ext[k + 1], l_ext[k], l_ext[k + 1]) for k in range(m + 1)]
    bands = {"f": ([], [], []), "a": ([], [], [])}
    for r in range(m):
        bf, ff = faces[r], faces[r + 1]
        w = w_ext[r + 1]
        main = 1.0 + cs * w * (bf + ff)
        bands["f"][0].append(-cs * bf * w_ext[r])
        bands["f"][1].append(main)
        bands["f"][2].append(-cs * ff * w_ext[r + 2])
        bands["a"][0].append(-cs * bf * w)
        bands["a"][1].append(main)
        bands["a"][2].append(-cs * ff * w)

    for c, key in ((0, "f"), (1, "a")):
        lower, main, upper = bands[key]
        pivots, ratios = [], []
        prev = None
        for r in range(m - 1):
            piv = main[r] if prev is None else main[r] - lower[r] * prev
            rat = upper[r] / piv
            pivots.append(piv)
            ratios.append(rat)
            prev = rat
        inv_piv = [1.0 / x for x in pivots]
        left_src = [lower[0]] + [None] * (m - 1)
        right_src = [None] * (m - 2) + [upper[m - 2], None]
        left = _sweep(m, lower, inv_piv, ratios, left_src)
        right = _sweep(m, lower, inv_piv, ratios, right_src)
        for r in range(m):
            fac_ref[c, 0, r] = lower[r]
            fac_ref[c, 1, r] = ratios[r] if r < m - 1 else zero
            fac_ref[c, 2, r] = inv_piv[r] if r < m - 1 else zero + 1.0
            lr_ref[c, 0, r] = left[r] if r < m - 1 else zero
            lr_ref[c, 1, r] = right[r] if r < m - 1 else zero - 1.0
        last_lower = lower[m - 1]
        rows_ref[c, 0] = last_lower * left[m - 2]
        rows_ref[c, 1] = main[m - 1] - last_lower * right[m - 2]
        rows_ref[c, 2] = upper[m - 1]
        rows_ref[c, 3] = left[0]
        rows_ref[c, 4] = right[0]


def _reduced_solve(gs, gv, voff, c, n, pos):
    slot = [(pos - p + n) % n for p in range(n)]
    g = [[gs[slot[p], c, k] for k in range(5)] for p in range(n)]
    v = [[gv[slot[p], c, voff + k] for k in range(2)] for p in range(n)]
    lower = [-g[p][0] for p in range(n)]
    main = [g[p][1] - g[p][2] * g[(p + 1) % n][3] for p in range(n)]
    upper = [-g[p][2] * g[(p + 1) % n][4] for p in range(n)]
    src = [v[p][0] - g[p][2] * v[(p + 1) % n][1] for p in range(n)]
    k_in = n - 1
    pivots, ratios = [], []
    prev = None
    for r in range(k_in):
        piv = main[r] if prev is None else main[r] - lower[r] * prev
        rat = upper[r] / piv
        pivots.append(piv)
        ratios.append(rat)
        prev = rat

    def apply(source):
        ys = []
        prev = None
        for r in range(k_in):
            num = source[r] if prev is None else source[r] - lower[r] * prev
            ys.append(num / pivots[r])
            prev = ys[-1]
        xs = [None] * k_in
        prev = None
        for r in range(k_in - 1, -1, -1):
            xs[r] = ys[r] if prev is None else ys[r] - ratios[r] * prev
            prev = xs[r]
        return xs

    coupling = []
    for r in range(k_in):
        term = None
        if r == 0:
            term = lower[0]
        if r == k_in - 1:
            term = upper[k_in - 1] if term is None else term + upper[k_in - 1]
        coupling.append(term if term is not None else jnp.zeros_like(lower[0]))
    linked = apply(coupling)
    closing = main[k_in] - lower[k_in] * linked[k_in - 1] - upper[k_in] * linked[0]
    inner = apply(src[:k_in])
    sep = (src[k_in] - lower[k_in] * inner[k_in - 1] - upper[k_in] * inner[0]) / closing
    return [inner[r] - linked[r] * sep for r in range(k_in)] + [sep]


def _combine_kernel(n, stacked, edge_of, pos_ref, *refs):
    gs_parts, gv_parts = refs[:n], refs[n : 2 * n]
    lr_ref, loc_ref = refs[2 * n], refs[2 * n + 1]
    refs = refs[2 * n + 2 :]
    if stacked:
        out_ref = refs[0]
        outs = (out_ref.at[0], out_ref.at[1])
        rest = refs[1:]
    else:
        outs = refs[:2]
        rest = refs[2:]
    edge_outs, sep_ref, gs_ref, gv_ref = rest[:4], rest[4], rest[5], rest[6]
    edges = rest[7:11]
    for k in range(n):
        gs_ref[k] = gs_parts[k][...]
        gv_ref[k] = gv_parts[k][...]
    m = loc_ref.shape[1]
    p = pos_ref[0]
    for c in range(2):
        seps = _reduced_solve(gs_ref, gv_ref, 0, c, n, p)
        for q in range(n):
            sep_ref[q] = seps[q]
        own = sep_ref[p]
        prior = sep_ref[(p + n - 1) % n]
        for r in range(m):
            val = loc_ref[c, r] - lr_ref[c, 0, r] * prior - lr_ref[c, 1, r] * own
            outs[c][r] = val
            if c in edge_of:
                _write_edges(edges, edge_of[c], r, val)
    _flush_edges(edges, edge_outs, _parity(pos_ref))


def _edge_kernel(ctl_ref, vac_ref, pore_ref, lab_ref, y_a, y_b, z_a, z_b, bx_ref, *edges):
    m = vac_ref.shape[0]
    for r in range(m):
        mob = 1.0 + 2.0 * pore_ref[r].astype(F32)
        lab = lab_ref[r].astype(F32)
        for c, val in enumerate((mob, lab, vac_ref[r])):
            _write_edges(edges, c, r, val)
        if r == 0:
            bx_ref[0, 0] = mob
            bx_ref[0, 1] = lab
        if r == m - 1:
            bx_ref[1, 0] = mob
            bx_ref[1, 1] = lab
    _flush_edges(edges, (y_a, y_b, z_a, z_b), _parity(ctl_ref))


def _local_solves(fac_ref, srcs, loc_ref, vals_ref):
    m = loc_ref.shape[1]
    zero = jnp.zeros(loc_ref.shape[2:], F32)
    for c in range(2):
        lower = [fac_ref[c, 0, r] for r in range(m)]
        ratios = [fac_ref[c, 1, r] for r in range(m - 1)]
        pivots = [fac_ref[c, 2, r] for r in range(m - 1)]
        src = srcs[c]
        local = _sweep(m, lower, pivots, ratios, src[: m - 1] + [None])
        for r in range(m):
            loc_ref[c, r] = local[r] if r < m - 1 else zero
        vals_ref[c, 0] = src[m - 1] - lower[m - 1] * local[m - 2]
        vals_ref[c, 1] = local[0]


def _first_kernel(ctl_ref, vac_ref, cot_ref, pore_ref, lab_ref, fac_ref, gy_lo, gy_hi, gz_lo, gz_hi, loc_ref, vals_ref):
    gy_lo, gy_hi, gz_lo, gz_hi = _picks(ctl_ref, gy_lo, gy_hi, gz_lo, gz_hi)
    m = pore_ref.shape[0]
    srcs = ([], [cot_ref[r] for r in range(m)])
    for i in range(m):
        mob, _, mob_n, fc = _geo_row(i, pore_ref, lab_ref, gy_lo, gy_hi, gz_lo, gz_hi)
        w = 0.5 * (1.0 + mob)
        v = vac_ref[i]
        v_n = _neighbours(v, _yrow(gy_lo, 2, i), _yrow(gy_hi, 2, i), _zcol(gz_lo, 2, i), _zcol(gz_hi, 2, i))
        u_n = [0.5 * (1.0 + mn) * vn for mn, vn in zip(mob_n, v_n)]
        srcs[0].append(v + cross_rate * (1.0 * _flux(w * v, u_n, fc)))
    _local_solves(fac_ref, srcs, loc_ref, vals_ref)


def _second_kernel(ctl_ref, pore_ref, lab_ref, fa_ref, fac_ref, gy_lo, gy_hi, gz_lo, gz_hi,
                   hy_lo, hy_hi, hz_lo, hz_hi, loc_ref, vals_ref):
    gy_lo, gy_hi, gz_lo, gz_hi = _picks(ctl_ref, gy_lo, gy_hi, gz_lo, gz_hi)
    hy_lo, hy_hi, hz_lo, hz_hi = _picks(ctl_ref, hy_lo, hy_hi, hz_lo, hz_hi)
    m = pore_ref.shape[0]
    srcs = ([], [])
    for i in range(m):
        mob, _, mob_n, fc = _geo_row(i, pore_ref, lab_ref, gy_lo, gy_hi, gz_lo, gz_hi)
        w = 0.5 * (1.0 + mob)
        f1 = fa_ref[0, i]
        f_n = _neighbours(f1, _yrow(hy_lo, 0, i), _yrow(hy_hi, 0, i), _zcol(hz_lo, 0, i), _zcol(hz_hi, 0, i))
        u_n = [0.5 * (1.0 + mn) * fn for mn, fn in zip(mob_n, f_n)]
        srcs[0].append(f1 + cross_rate * (1.0 * _flux(w * f1, u_n, fc)))
        a1 = fa_ref[1, i]
        a_n = _neighbours(a1, _yrow(hy_lo, 1, i), _yrow(hy_hi, 1, i), _zcol(hz_lo, 1, i), _zcol(hz_hi, 1, i))
        srcs[1].append(a1 + cross_rate * (w * _flux(a1, a_n, fc)))
    _local_solves(fac_ref, srcs, loc_ref, vals_ref)


def _gradient_kernel(ctl_ref, pore_ref, lab_ref, a2_ref, gy_lo, gy_hi, gz_lo, gz_hi,
                     hy_lo, hy_hi, hz_lo, hz_hi, out_ref):
    gy_lo, gy_hi, gz_lo, gz_hi = _picks(ctl_ref, gy_lo, gy_hi, gz_lo, gz_hi)
    hy_lo, hy_hi, hz_lo, hz_hi = _picks(ctl_ref, hy_lo, hy_hi, hz_lo, hz_hi)
    m = pore_ref.shape[0]
    for i in range(m):
        mob, _, _, fc = _geo_row(i, pore_ref, lab_ref, gy_lo, gy_hi, gz_lo, gz_hi)
        w = 0.5 * (1.0 + mob)
        a2 = a2_ref[i]
        a_n = _neighbours(a2, _yrow(hy_lo, 0, i), _yrow(hy_hi, 0, i), _zcol(hz_lo, 0, i), _zcol(hz_hi, 0, i))
        out_ref[i] = a2 + cross_rate * (w * _flux(a2, a_n, fc))


def _halo_pairs(axis, periodic):
    count = lax.axis_size(axis)
    forward = [(i, i + 1) for i in range(count - 1)]
    if periodic:
        forward.append((count - 1, 0))
    backward = [(t, s) for s, t in forward]
    return forward, backward


def _exchange(first, last, axis, periodic):
    forward, backward = _halo_pairs(axis, periodic)
    lo = lax.ppermute(last, axis, forward)
    hi = lax.ppermute(first, axis, backward)
    return lo, hi


def _first_call(m, ny, nz):
    return pl.pallas_call(
        _first_kernel,
        out_shape=(
            jax.ShapeDtypeStruct((2, m, ny, nz), F32),
            jax.ShapeDtypeStruct((2, 2, ny, nz), F32),
        ),
        in_specs=[_smem()] + [_vmem()] * 9,
        out_specs=(_vmem(), _vmem()),
    )


def _combine_scratch(n, ny, nz):
    return [
        pltpu.VMEM((n, ny, nz), F32),
        pltpu.VMEM((n, 2, 5, ny, nz), F32),
        pltpu.VMEM((n, 2, 2, ny, nz), F32),
    ]


def _gather_blk(x):
    n = lax.axis_size("blk")
    parts = [x]
    for k in range(1, n):
        parts.append(lax.ppermute(x, "blk", [(j, (j + k) % n) for j in range(n)]))
    return parts


def _edge_shapes(chans, m, ny, nz):
    return (
        jax.ShapeDtypeStruct((chans, m, nz), F32),
        jax.ShapeDtypeStruct((chans, m, nz), F32),
        jax.ShapeDtypeStruct((chans, ny, m), F32),
        jax.ShapeDtypeStruct((chans, ny, m), F32),
    )


def _swap(x_a, x_b, axis):
    n = lax.axis_size(axis)
    pairs_a = [(i, i ^ 1) for i in range(n) if i ^ 1 < n]
    pairs_b = [(i, i + 1) for i in range(1, n - 1, 2)] + [(i + 1, i) for i in range(1, n - 1, 2)]
    recv_a = lax.ppermute(x_a, axis, pairs_a)
    recv_b = lax.ppermute(x_b, axis, pairs_b) if pairs_b else jnp.zeros_like(x_b)
    return recv_a, recv_b


def _yz_halos(y_a, y_b, z_a, z_b):
    z_pair = _swap(z_a, z_b, "gz")
    y_pair = _swap(y_a, y_b, "gy")
    return y_pair + z_pair


def _shards(vacancy, grain_label, pore_mask, cotangent):
    m, ny, nz = vacancy.shape
    n_blk = lax.axis_size("blk")
    cycle_step = float((m * n_blk) ** 2 // 64)
    shape = jax.ShapeDtypeStruct((m, ny, nz), F32)

    ctl = jnp.stack(
        [lax.axis_index("blk"), 1 - lax.axis_index("gy") % 2, 1 - lax.axis_index("gz") % 2]
    ).astype(jnp.int32)
    outs = pl.pallas_call(
        _edge_kernel,
        out_shape=_edge_shapes(3, m, ny, nz) + (jax.ShapeDtypeStruct((2, 2, ny, nz), F32),),
        in_specs=[_smem()] + [_vmem()] * 3,
        out_specs=tuple(_vmem() for _ in range(5)),
        scratch_shapes=_edge_scratch(3, m, ny, nz),
    )(ctl, vacancy, pore_mask, grain_label)
    if n_blk == 2:
        bx = lax.ppermute(outs[4], "blk", [(0, 1), (1, 0)])
        lo_i, hi_i = 1, 0
    else:
        bx_lo, bx_hi = _exchange(outs[4][0], outs[4][1], "blk", True)
        bx = jnp.stack([bx_lo, bx_hi])
        lo_i, hi_i = 0, 1
    gy_lo, gy_hi, gz_lo, gz_hi = _yz_halos(*outs[:4])

    fac, lr, rows = pl.pallas_call(
        lambda *r: _factor_kernel(cycle_step, lo_i, hi_i, *r),
        out_shape=(
            jax.ShapeDtypeStruct((2, 3, m, ny, nz), F32),
            jax.ShapeDtypeStruct((2, 2, m, ny, nz), F32),
            jax.ShapeDtypeStruct((2, 5, ny, nz), F32),
        ),
        in_specs=[_vmem()] * 3,
        out_specs=(_vmem(), _vmem(), _vmem()),
    )(pore_mask, grain_label, bx)
    gathered = _gather_blk(rows)

    loc, vals = _first_call(m, ny, nz)(
        ctl, vacancy, cotangent, pore_mask, grain_label, fac, gy_lo, gy_hi, gz_lo, gz_hi
    )
    gathered1 = _gather_blk(vals)
    pos = ctl

    outs = pl.pallas_call(
        lambda *r: _combine_kernel(n_blk, True, {0: 0, 1: 1}, *r),
        out_shape=(jax.ShapeDtypeStruct((2, m, ny, nz), F32),) + _edge_shapes(2, m, ny, nz),
        in_specs=[_smem()] + [_vmem()] * (2 * n_blk + 2),
        out_specs=tuple(_vmem() for _ in range(5)),
        scratch_shapes=_combine_scratch(n_blk, ny, nz) + _edge_scratch(2, m, ny, nz),
    )(pos, *gathered, *gathered1, lr, loc)
    fa = outs[0]

    hy_lo, hy_hi, hz_lo, hz_hi = _yz_halos(*outs[1:])
    loc2, vals2 = pl.pallas_call(
        _second_kernel,
        out_shape=(
            jax.ShapeDtypeStruct((2, m, ny, nz), F32),
            jax.ShapeDtypeStruct((2, 2, ny, nz), F32),
        ),
        in_specs=[_smem()] + [_vmem()] * 12,
        out_specs=(_vmem(), _vmem()),
    )(ctl, pore_mask, grain_label, fa, fac, gy_lo, gy_hi, gz_lo, gz_hi, hy_lo, hy_hi, hz_lo, hz_hi)

    gathered2 = _gather_blk(vals2)
    outs = pl.pallas_call(
        lambda *r: _combine_kernel(n_blk, False, {1: 0}, *r),
        out_shape=(shape, shape) + _edge_shapes(1, m, ny, nz),
        in_specs=[_smem()] + [_vmem()] * (2 * n_blk + 2),
        out_specs=tuple(_vmem() for _ in range(6)),
        scratch_shapes=_combine_scratch(n_blk, ny, nz) + _edge_scratch(1, m, ny, nz),
    )(pos, *gathered, *gathered2, lr, loc2)
    final_field, adjoint_two = outs[:2]

    a2_lo, a2_hi, a2z_lo, a2z_hi = _yz_halos(*outs[2:])
    gradient = pl.pallas_call(
        _gradient_kernel,
        out_shape=shape,
        in_specs=[_smem()] + [_vmem()] * 11,
        out_specs=_vmem(),
    )(ctl, pore_mask, grain_label, adjoint_two, gy_lo, gy_hi, gz_lo, gz_hi, a2_lo, a2_hi, a2z_lo, a2z_hi)
    return (final_field, gradient)


def solution(mesh):
    in_specs = (
        P("blk", "gy", "gz"),
        P("blk", "gy", "gz"),
        P("blk", "gy", "gz"),
        P("blk", "gy", "gz"),
    )
    out_specs = (P("blk", "gy", "gz"), P("blk", "gy", "gz"))
    fn = jax.shard_map(_shards, mesh=mesh, in_specs=in_specs, out_specs=out_specs, check_vma=False)
    if mesh.shape["blk"] > 4:
        return fn
    return fn
```
